32 devices in a mesh: alt: 8 (over z, y), raan: 4 (over x, core).
Axes of the slice: x: 2, y: 2, z: 4, core: 2. Of those that a mesh axis runs over, the one named last changes fastest.
Arguments:
- source: float32 [32, 64, 1024], P('alt', None, 'raan'), may hold values from -6 to 6
- k_alt: float32 [32, 64, 1024], P('alt', None, 'raan'), may hold values from 20 to 400
- k_inc: float32 [32, 64, 1024], P('alt', None, 'raan'), may hold values from 20 to 400
- k_raan: float32 [32, 64, 1024], P('alt', None, 'raan'), may hold values from 20 to 400
Outputs:
- density: float32 [32, 64, 1024], P('alt', None, 'raan')
- scaled_residual: float32 [32, 64, 1024], P('alt', None, 'raan')
The draws below stay inside these ranges and needn't reach their ends.
All inputs are finite; a program needn't handle non-finite values.
Results may differ from the reference program's by a relative error of at most 0.00018.
Values sent between devices are 32-bit elements; how exact they have to be, the bound alone decides.
No kernel may reach another device: no remote copies, remote signals or barrier semaphores. Data moves between devices by JAX's collectives and lax.ppermute only.
A program may use at most 128 MiB of HBM per device.

```python
import math
import jax
import jax.numpy as jnp

INC = 64
RAAN = 1024
SWEEPS = 2
COARSE_SWEEPS = 4
NA = 32


def draw_source(key, part):
    base = jax.random.normal(key, (NA, INC, RAAN), jnp.float32)
    return jnp.clip(base, -6.0, 6.0)


def shard_levels(key, dims, split, smallest, top_value):
    gain, own = 1.0, jax.random.fold_in(key, 6)
    for dim, parts in split:
        draws = jnp.exp(jax.random.uniform(jax.random.fold_in(own, dim), (parts,), jnp.float32, smallest / len(split), top_value / len(split)))
        gain = gain * jnp.repeat(draws, dims[dim] // parts).reshape([-1 if axis == dim else 1 for axis in range(len(dims))])
    return gain


def setup_inputs(seed: int = 0) -> dict:
    arg_keys = jax.random.split(jax.random.key(seed), 5)
    source = draw_source(jax.random.fold_in(arg_keys[4], 71), 0)
    k_alt = jnp.clip(jnp.exp(math.log(400.0) - 2.9957323 * jax.random.uniform(arg_keys[1], (NA, INC, RAAN), jnp.float32) ** shard_levels(arg_keys[1], (NA, INC, RAAN), ((0, 8), (2, 4)), -0.2, 0.2)), 20.0, 400.0)
    k_inc = jnp.clip(jnp.exp(math.log(400.0) - 2.9957323 * jax.random.uniform(arg_keys[2], (NA, INC, RAAN), jnp.float32) ** shard_levels(arg_keys[2], (NA, INC, RAAN), ((0, 8), (2, 4)), -0.2, 0.2)), 20.0, 400.0)
    k_raan = jnp.clip(jnp.exp(math.log(400.0) - 2.9957323 * jax.random.uniform(arg_keys[3], (NA, INC, RAAN), jnp.float32) ** shard_levels(arg_keys[3], (NA, INC, RAAN), ((0, 8), (2, 4)), -0.2, 0.2)), 20.0, 400.0)
    return dict(source=source, k_alt=k_alt, k_inc=k_inc, k_raan=k_raan)


OMEGA = 0.75


def coarsen(values):
    depth, width, length = values.shape
    return values.reshape(depth // 2, 2, width // 2, 2, length // 2, 2).mean(axis=(1, 3, 5))


def refine(values):
    return jnp.repeat(jnp.repeat(jnp.repeat(values, 2, 0), 2, 1), 2, 2)


def make_weights(coef_alt, coef_inc, coef_raan, factor):
    zero_alt = jnp.zeros_like(coef_alt[:1])
    alt_down = jnp.concatenate([zero_alt, coef_alt[:-1]], 0)
    alt_up = jnp.concatenate([coef_alt[1:], zero_alt], 0)
    w_alt_lo = factor * 0.5 * (coef_alt + alt_down)
    w_alt_hi = factor * 0.5 * (coef_alt + alt_up)
    inner_faces = factor * 0.5 * (coef_inc[:, :-1] + coef_inc[:, 1:])
    zero_inc = jnp.zeros_like(coef_inc[:, :1])
    w_inc_lo = jnp.concatenate([zero_inc, inner_faces], 1)
    w_inc_hi = jnp.concatenate([inner_faces, zero_inc], 1)
    w_raan_lo = factor * 0.5 * (coef_raan + jnp.roll(coef_raan, 1, 2))
    w_raan_hi = factor * 0.5 * (coef_raan + jnp.roll(coef_raan, -1, 2))
    diagonal = 1.0 + (w_alt_lo + w_alt_hi + w_inc_lo + w_inc_hi + w_raan_lo + w_raan_hi)
    return (w_alt_lo, w_alt_hi, w_inc_lo, w_inc_hi, w_raan_lo, w_raan_hi, diagonal)


def apply_op(weights, field):
    w_alt_lo, w_alt_hi, w_inc_lo, w_inc_hi, w_raan_lo, w_raan_hi, diagonal = weights
    zero_alt = jnp.zeros_like(field[:1])
    v_down = jnp.concatenate([zero_alt, field[:-1]], 0)
    v_up = jnp.concatenate([field[1:], zero_alt], 0)
    zero_inc = jnp.zeros_like(field[:, :1])
    v_prev = jnp.concatenate([zero_inc, field[:, :-1]], 1)
    v_next = jnp.concatenate([field[:, 1:], zero_inc], 1)
    v_left = jnp.roll(field, 1, 2)
    v_right = jnp.roll(field, -1, 2)
    beside = (w_alt_lo * v_down + w_alt_hi * v_up + w_inc_lo * v_prev + w_inc_hi * v_next
              + w_raan_lo * v_left + w_raan_hi * v_right)
    return diagonal * field - beside


def smooth(field, target, weights, repeats):
    for _ in range(repeats):
        field = field + OMEGA * (target - apply_op(weights, field)) / weights[6]
    return field


def reference(source, k_alt, k_inc, k_raan):
    weights_one = make_weights(k_alt, k_inc, k_raan, 1.0)
    coef_two = (coarsen(k_alt), coarsen(k_inc), coarsen(k_raan))
    weights_two = make_weights(coef_two[0], coef_two[1], coef_two[2], 0.25)
    coef_three = (coarsen(coef_two[0]), coarsen(coef_two[1]), coarsen(coef_two[2]))
    weights_three = make_weights(coef_three[0], coef_three[1], coef_three[2], 0.0625)
    density = smooth(source, source, weights_one, SWEEPS)
    rhs_two = coarsen(source - apply_op(weights_one, density))
    correction = OMEGA * rhs_two / weights_two[6]
    correction = smooth(correction, rhs_two, weights_two, SWEEPS - 1)
    rhs_three = coarsen(rhs_two - apply_op(weights_two, correction))
    coarse_part = OMEGA * rhs_three / weights_three[6]
    coarse_part = smooth(coarse_part, rhs_three, weights_three, COARSE_SWEEPS - 1)
    correction = correction + refine(coarse_part)
    correction = smooth(correction, rhs_two, weights_two, SWEEPS)
    density = density + refine(correction)
    density = smooth(density, source, weights_one, SWEEPS)
    scaled_residual = (source - apply_op(weights_one, density)) / weights_one[6]
    return density, scaled_residual
```

```python
import jax
import jax.numpy as jnp
from jax import lax
from jax.sharding import PartitionSpec as P

SWEEPS = 2
COARSE_SWEEPS = 4


OMEGA = 0.75


def with_halo(shard, sides, width, wrap):
    for axis, dim in sides:
        count, length = (lax.axis_size(axis), shard.shape[dim])
        up = [(i, (i + 1) % count) for i in range(count if wrap else count - 1)]
        down = [(j, i) for i, j in up]
        last = lax.slice_in_dim(shard, length - width, length, axis=dim)
        leading = lax.slice_in_dim(shard, 0, width, axis=dim)
        before = lax.ppermute(last, axis, up)
        after = lax.ppermute(leading, axis, down)
        shard = jnp.concatenate([before, shard, after], axis=dim)
    return shard


def shifted(block, axis, distance):
    devices = range(lax.axis_size(axis))
    route = [(i - distance, i) for i in devices if i - distance in devices]
    return lax.ppermute(block, axis, route)


def from_partner(block, axis, distance):
    count = lax.axis_size(axis)
    route = []
    for low in range(count):
        high = low | 1 << distance
        if high != low and high < count:
            route += [(low, high), (high, low)]
    return lax.ppermute(block, axis, route)


HIGH = lax.Precision.HIGHEST


def pairing(fine):
    rows = lax.broadcasted_iota(jnp.int32, (fine, fine // 2), 0) // 2
    cols = lax.broadcasted_iota(jnp.int32, (fine, fine // 2), 1)
    return (rows == cols).astype(jnp.float32)


def coarsen(values):
    depth, width, length = values.shape
    summed = values.reshape(depth // 2, 2, width, length).sum(axis=1)
    summed = jnp.matmul(summed, pairing(length), precision=HIGH)
    summed = jnp.matmul(pairing(width).T[None], summed, precision=HIGH)
    return summed * 0.125


def refine(values):
    depth, width, length = values.shape
    grown = jnp.matmul(values, pairing(2 * length).T, precision=HIGH)
    grown = jnp.matmul(pairing(2 * width)[None], grown, precision=HIGH)
    grown = jnp.broadcast_to(grown[:, None], (depth, 2, 2 * width, 2 * length))
    return grown.reshape(2 * depth, 2 * width, 2 * length)


def alt_ext(values):
    return with_halo(values, (("alt", 0),), 1, False)


def raan_ext(values):
    return with_halo(values, (("raan", 2),), 1, True)


def plain_alt(values):
    padded = alt_ext(values)
    return (padded[:-2], padded[2:])


def fold_alt(values):
    below = shifted(values[-1:], "alt", 2)
    above = shifted(values[:1], "alt", -2)
    v_down = jnp.concatenate([below, values[:-1]], 0)
    v_up = jnp.concatenate([values[1:], above], 0)
    return (v_down, v_up)


def field_near(field):
    v_down, v_up = plain_alt(field)
    wrapped = raan_ext(field)
    return (v_down, v_up, wrapped[:, :, :-2], wrapped[:, :, 2:])


def fold_near(field):
    v_down, v_up = fold_alt(field)
    wrapped = raan_ext(field)
    return (v_down, v_up, wrapped[:, :, :-2], wrapped[:, :, 2:])


def make_weights(coef_alt, coef_inc, coef_raan, factor, alt_pair):
    alt_down, alt_up = alt_pair(coef_alt)
    w_alt_lo = factor * 0.5 * (coef_alt + alt_down)
    w_alt_hi = factor * 0.5 * (coef_alt + alt_up)
    inner_faces = factor * 0.5 * (coef_inc[:, :-1] + coef_inc[:, 1:])
    zero_inc = jnp.zeros_like(coef_inc[:, :1])
    w_inc_lo = jnp.concatenate([zero_inc, inner_faces], 1)
    w_inc_hi = jnp.concatenate([inner_faces, zero_inc], 1)
    wrapped = raan_ext(coef_raan)
    w_raan_lo = factor * 0.5 * (coef_raan + wrapped[:, :, :-2])
    w_raan_hi = factor * 0.5 * (coef_raan + wrapped[:, :, 2:])
    diagonal = 1.0 + (w_alt_lo + w_alt_hi + w_inc_lo + w_inc_hi + w_raan_lo + w_raan_hi)
    return (w_alt_lo, w_alt_hi, w_inc_lo, w_inc_hi, w_raan_lo, w_raan_hi, diagonal)


def apply_op(weights, field, near):
    w_alt_lo, w_alt_hi, w_inc_lo, w_inc_hi, w_raan_lo, w_raan_hi, diagonal = weights
    v_down, v_up, v_left, v_right = near(field)
    zero_inc = jnp.zeros_like(field[:, :1])
    v_prev = jnp.concatenate([zero_inc, field[:, :-1]], 1)
    v_next = jnp.concatenate([field[:, 1:], zero_inc], 1)
    beside = (
        w_alt_lo * v_down
        + w_alt_hi * v_up
        + w_inc_lo * v_prev
        + w_inc_hi * v_next
        + w_raan_lo * v_left
        + w_raan_hi * v_right
    )
    return diagonal * field - beside


def smooth(field, target, weights, near, repeats):
    for _ in range(repeats):
        field = field + OMEGA * (target - apply_op(weights, field, near)) / weights[6]
    return field


def coarse_solve(target, weights, near):
    field = OMEGA * target / weights[6]
    return smooth(field, target, weights, near, COARSE_SWEEPS - 1)


def shards(source, k_alt, k_inc, k_raan):
    weights_one = make_weights(k_alt, k_inc, k_raan, 1.0, plain_alt)
    coef_two = (coarsen(k_alt), coarsen(k_inc), coarsen(k_raan))
    weights_two = make_weights(coef_two[0], coef_two[1], coef_two[2], 0.25, plain_alt)
    coef_three = (coarsen(coef_two[0]), coarsen(coef_two[1]), coarsen(coef_two[2]))
    density = smooth(source, source, weights_one, field_near, SWEEPS)
    rhs_two = coarsen(source - apply_op(weights_one, density, field_near))
    correction = OMEGA * rhs_two / weights_two[6]
    correction = smooth(correction, rhs_two, weights_two, field_near, SWEEPS - 1)
    rhs_three = coarsen(rhs_two - apply_op(weights_two, correction, field_near))
    height = rhs_three.shape[0]
    parity = lax.axis_index("alt") % 2
    own_part = jnp.stack((rhs_three, coef_three[0], coef_three[1], coef_three[2]))
    theirs = from_partner(own_part, "alt", 0)
    low_half = jnp.where(parity == 0, own_part, theirs)
    high_half = jnp.where(parity == 0, theirs, own_part)
    pair_block = jnp.concatenate([low_half, high_half], axis=1)
    weights_three = make_weights(pair_block[1], pair_block[2], pair_block[3], 0.0625, fold_alt)
    pair_result = coarse_solve(pair_block[0], weights_three, fold_near)
    coarse_part = lax.dynamic_slice_in_dim(pair_result, parity * height, height, 0)
    correction = correction + refine(coarse_part)
    correction = smooth(correction, rhs_two, weights_two, field_near, SWEEPS)
    density = density + refine(correction)
    density = smooth(density, source, weights_one, field_near, SWEEPS)
    scaled_residual = (source - apply_op(weights_one, density, field_near)) / weights_one[6]
    return (density, scaled_residual)


def solution(mesh):
    in_specs = (
        P("alt", None, "raan"),
        P("alt", None, "raan"),
        P("alt", None, "raan"),
        P("alt", None, "raan"),
    )
    out_specs = (P("alt", None, "raan"), P("alt", None, "raan"))
    return jax.shard_map(shards, mesh=mesh, in_specs=in_specs, out_specs=out_specs, check_vma=False)
```

```python
import jax
import jax.numpy as jnp
from jax import lax
from jax.sharding import PartitionSpec as P

SWEEPS = 2
COARSE_SWEEPS = 4


OMEGA = 0.75


def with_halo(shard, sides, width, wrap):
    for axis, dim in sides:
        count, length = (lax.axis_size(axis), shard.shape[dim])
        up = [(i, (i + 1) % count) for i in range(count if wrap else count - 1)]
        down = [(j, i) for i, j in up]
        last = lax.slice_in_dim(shard, length - width, length, axis=dim)
        leading = lax.slice_in_dim(shard, 0, width, axis=dim)
        before = lax.ppermute(last, axis, up)
        after = lax.ppermute(leading, axis, down)
        shard = jnp.concatenate([before, shard, after], axis=dim)
    return shard


def shifted(block, axis, distance):
    devices = range(lax.axis_size(axis))
    route = [(i - distance, i) for i in devices if i - distance in devices]
    return lax.ppermute(block, axis, route)


def from_partner(block, axis, distance):
    count = lax.axis_size(axis)
    route = []
    for low in range(count):
        high = low | 1 << distance
        if high != low and high < count:
            route += [(low, high), (high, low)]
    return lax.ppermute(block, axis, route)


HIGH = lax.Precision.HIGHEST


def pairing(fine):
    rows = lax.broadcasted_iota(jnp.int32, (fine, fine // 2), 0) // 2
    cols = lax.broadcasted_iota(jnp.int32, (fine, fine // 2), 1)
    return (rows == cols).astype(jnp.float32)


def coarsen(values):
    depth, width, length = values.shape
    summed = values.reshape(depth // 2, 2, width, length).sum(axis=1)
    summed = jnp.matmul(summed, pairing(length), precision=HIGH)
    summed = jnp.matmul(pairing(width).T[None], summed, precision=HIGH)
    return summed * 0.125


def refine(values):
    depth, width, length = values.shape
    grown = jnp.matmul(values, pairing(2 * length).T, precision=HIGH)
    grown = jnp.matmul(pairing(2 * width)[None], grown, precision=HIGH)
    grown = jnp.broadcast_to(grown[:, None], (depth, 2, 2 * width, 2 * length))
    return grown.reshape(2 * depth, 2 * width, 2 * length)


def alt_ext(values):
    return with_halo(values, (("alt", 0),), 1, False)


def raan_ext(values):
    return with_halo(values, (("raan", 2),), 1, True)


def plain_alt(values):
    padded = alt_ext(values)
    return (padded[:-2], padded[2:])


def fold_alt(values):
    below = shifted(values[-1:], "alt", 2)
    above = shifted(values[:1], "alt", -2)
    v_down = jnp.concatenate([below, values[:-1]], 0)
    v_up = jnp.concatenate([values[1:], above], 0)
    return (v_down, v_up)


def field_near(field):
    v_down, v_up = plain_alt(field)
    wrapped = raan_ext(field)
    return (v_down, v_up, wrapped[:, :, :-2], wrapped[:, :, 2:])


def fold_near(field):
    v_down, v_up = fold_alt(field)
    wrapped = raan_ext(field)
    return (v_down, v_up, wrapped[:, :, :-2], wrapped[:, :, 2:])


def make_weights(coef_alt, coef_inc, coef_raan, factor, alt_pair, whole=False):
    alt_down, alt_up = alt_pair(coef_alt)
    w_alt_lo = factor * 0.5 * (coef_alt + alt_down)
    w_alt_hi = factor * 0.5 * (coef_alt + alt_up)
    inner_faces = factor * 0.5 * (coef_inc[:, :-1] + coef_inc[:, 1:])
    zero_inc = jnp.zeros_like(coef_inc[:, :1])
    w_inc_lo = jnp.concatenate([zero_inc, inner_faces], 1)
    w_inc_hi = jnp.concatenate([inner_faces, zero_inc], 1)
    if whole:
        raan_lo, raan_hi = jnp.roll(coef_raan, 1, 2), jnp.roll(coef_raan, -1, 2)
    else:
        wrapped = raan_ext(coef_raan)
        raan_lo, raan_hi = wrapped[:, :, :-2], wrapped[:, :, 2:]
    w_raan_lo = factor * 0.5 * (coef_raan + raan_lo)
    w_raan_hi = factor * 0.5 * (coef_raan + raan_hi)
    diagonal = 1.0 + (w_alt_lo + w_alt_hi + w_inc_lo + w_inc_hi + w_raan_lo + w_raan_hi)
    return (w_alt_lo, w_alt_hi, w_inc_lo, w_inc_hi, w_raan_lo, w_raan_hi, diagonal)


def apply_op(weights, field, near):
    w_alt_lo, w_alt_hi, w_inc_lo, w_inc_hi, w_raan_lo, w_raan_hi, diagonal = weights
    v_down, v_up, v_left, v_right = near(field)
    zero_inc = jnp.zeros_like(field[:, :1])
    v_prev = jnp.concatenate([zero_inc, field[:, :-1]], 1)
    v_next = jnp.concatenate([field[:, 1:], zero_inc], 1)
    beside = (
        w_alt_lo * v_down
        + w_alt_hi * v_up
        + w_inc_lo * v_prev
        + w_inc_hi * v_next
        + w_raan_lo * v_left
        + w_raan_hi * v_right
    )
    return diagonal * field - beside


def smooth(field, target, weights, near, repeats):
    for _ in range(repeats):
        field = field + OMEGA * (target - apply_op(weights, field, near)) / weights[6]
    return field


def coarse_solve(target, weights, near):
    field = OMEGA * target / weights[6]
    return smooth(field, target, weights, near, COARSE_SWEEPS - 1)


def gather_grid(stacked):
    count, height, width, length = stacked.shape
    alt_n, raan_n = lax.axis_size("alt"), lax.axis_size("raan")
    every = lax.all_gather(stacked, ("alt", "raan"), axis=0, tiled=False)
    every = every.reshape(alt_n, raan_n, count, height, width, length)
    every = every.transpose(2, 0, 3, 4, 1, 5)
    return every.reshape(count, alt_n * height, width, raan_n * length)


def whole_weights(coef_alt, coef_inc, coef_raan, factor):
    zero_alt = jnp.zeros_like(coef_alt[:1])
    alt_down = jnp.concatenate([zero_alt, coef_alt[:-1]], 0)
    alt_up = jnp.concatenate([coef_alt[1:], zero_alt], 0)
    return make_weights(coef_alt, coef_inc, coef_raan, factor, lambda _: (alt_down, alt_up), whole=True)


def whole_near(field):
    zero_alt = jnp.zeros_like(field[:1])
    v_down = jnp.concatenate([zero_alt, field[:-1]], 0)
    v_up = jnp.concatenate([field[1:], zero_alt], 0)
    return (v_down, v_up, jnp.roll(field, 1, 2), jnp.roll(field, -1, 2))


def whole_apply(weights, field):
    return apply_op(weights, field, whole_near)


def shards(source, k_alt, k_inc, k_raan):
    weights_one = make_weights(k_alt, k_inc, k_raan, 1.0, plain_alt)
    coef_two = (coarsen(k_alt), coarsen(k_inc), coarsen(k_raan))
    weights_two = make_weights(coef_two[0], coef_two[1], coef_two[2], 0.25, plain_alt)
    coef_three = (coarsen(coef_two[0]), coarsen(coef_two[1]), coarsen(coef_two[2]))
    density = smooth(source, source, weights_one, field_near, SWEEPS)
    rhs_two = coarsen(source - apply_op(weights_one, density, field_near))
    correction = OMEGA * rhs_two / weights_two[6]
    correction = smooth(correction, rhs_two, weights_two, field_near, SWEEPS - 1)
    rhs_three = coarsen(rhs_two - apply_op(weights_two, correction, field_near))
    whole_coef = gather_grid(jnp.stack(coef_three))
    weights_three = whole_weights(whole_coef[0], whole_coef[1], whole_coef[2], 0.0625)
    whole_rhs = gather_grid(rhs_three[None])[0]
    whole_part = OMEGA * whole_rhs / weights_three[6]
    for _ in range(COARSE_SWEEPS - 1):
        whole_part = whole_part + OMEGA * (whole_rhs - whole_apply(weights_three, whole_part)) / weights_three[6]
    height, width, length = rhs_three.shape
    coarse_part = lax.dynamic_slice(
        whole_part,
        (lax.axis_index("alt") * height, 0, lax.axis_index("raan") * length),
        (height, width, length),
    )
    correction = correction + refine(coarse_part)
    correction = smooth(correction, rhs_two, weights_two, field_near, SWEEPS)
    density = density + refine(correction)
    density = smooth(density, source, weights_one, field_near, SWEEPS)
    scaled_residual = (source - apply_op(weights_one, density, field_near)) / weights_one[6]
    return (density, scaled_residual)


def solution(mesh):
    in_specs = (
        P("alt", None, "raan"),
        P("alt", None, "raan"),
        P("alt", None, "raan"),
        P("alt", None, "raan"),
    )
    out_specs = (P("alt", None, "raan"), P("alt", None, "raan"))
    return jax.shard_map(shards, mesh=mesh, in_specs=in_specs, out_specs=out_specs, check_vma=False)
```

```python
import math

import jax
import jax.numpy as jnp
from jax import lax
from jax.sharding import PartitionSpec as P

SWEEPS = 2
COARSE_SWEEPS = 4
OMEGA = 0.75
RAAN_HALO = 32
HIGH = lax.Precision.HIGHEST


def pairing(fine):
    rows = lax.broadcasted_iota(jnp.int32, (fine, fine // 2), 0) // 2
    cols = lax.broadcasted_iota(jnp.int32, (fine, fine // 2), 1)
    return (rows == cols).astype(jnp.float32)


def coarsen(values):
    depth, width, length = values.shape
    summed = values.reshape(depth // 2, 2, width, length).sum(axis=1)
    summed = jnp.matmul(summed, pairing(length), precision=HIGH)
    summed = jnp.matmul(pairing(width).T[None], summed, precision=HIGH)
    return summed * 0.125


def refine(values):
    depth, width, length = values.shape
    grown = jnp.matmul(values, pairing(2 * length).T, precision=HIGH)
    grown = jnp.matmul(pairing(2 * width)[None], grown, precision=HIGH)
    grown = jnp.broadcast_to(grown[:, None], (depth, 2, 2 * width, 2 * length))
    return grown.reshape(2 * depth, 2 * width, 2 * length)


def raan_extend(values, halo):
    count, length = lax.axis_size("raan"), values.shape[-1]
    up = [(i, (i + 1) % count) for i in range(count)]
    down = [(j, i) for i, j in up]
    before = lax.ppermute(values[..., length - halo:], "raan", up)
    after = lax.ppermute(values[..., :halo], "raan", down)
    return jnp.concatenate([before, values, after], axis=-1)


def alt_extend(items):
    count = lax.axis_size("alt")
    pieces = {}
    for index, (values, halo) in enumerate(items):
        depth = values.shape[0]
        for distance in range(1, -(-halo // depth) + 1):
            low = max(0, distance * depth - halo)
            high = min(depth, halo - (distance - 1) * depth)
            pieces.setdefault(("up", distance), []).append((index, values[low:]))
            pieces.setdefault(("down", distance), []).append((index, values[:high]))
    got = {}
    for (way, distance), parts in pieces.items():
        if way == "up":
            route = [(i, i + distance) for i in range(count) if i + distance < count]
        else:
            route = [(i, i - distance) for i in range(count) if i - distance >= 0]
        flat = jnp.concatenate([part.reshape(-1) for _, part in parts])
        moved = lax.ppermute(flat, "alt", route)
        start = 0
        for index, part in parts:
            size = part.size
            got[(index, way, distance)] = moved[start:start + size].reshape(part.shape)
            start += size
    out = []
    for index, (values, halo) in enumerate(items):
        depth = values.shape[0]
        reach = -(-halo // depth)
        below = [got[(index, "up", d)] for d in range(reach, 0, -1)]
        above = [got[(index, "down", d)] for d in range(1, reach + 1)]
        out.append(jnp.concatenate(below + [values] + above, axis=0))
    return out


def trim(values, have, want):
    cut = have - want
    return values[cut:values.shape[0] - cut] if cut else values


def lane_shifts(values):
    zero = jnp.zeros_like(values[..., :1])
    left = jnp.concatenate([zero, values[..., :-1]], axis=-1)
    right = jnp.concatenate([values[..., 1:], zero], axis=-1)
    return left, right


def make_weights(coef_alt, coef_inc, coef_raan, factor, halo):
    centre = coef_alt[1:-1]
    w_alt_lo = factor * 0.5 * (centre + coef_alt[:-2])
    w_alt_hi = factor * 0.5 * (centre + coef_alt[2:])
    inner_faces = factor * 0.5 * (coef_inc[:, :-1] + coef_inc[:, 1:])
    zero_inc = jnp.zeros_like(coef_inc[:, :1])
    w_inc_lo = jnp.concatenate([zero_inc, inner_faces], 1)
    w_inc_hi = jnp.concatenate([inner_faces, zero_inc], 1)
    raan_left, raan_right = lane_shifts(coef_raan)
    w_raan_lo = factor * 0.5 * (coef_raan + raan_left)
    w_raan_hi = factor * 0.5 * (coef_raan + raan_right)
    diagonal = 1.0 + (w_alt_lo + w_alt_hi + w_inc_lo + w_inc_hi + w_raan_lo + w_raan_hi)
    return (w_alt_lo, w_alt_hi, w_inc_lo, w_inc_hi, w_raan_lo, w_raan_hi, diagonal), halo


def apply_op(weights, field, halo):
    parts, have = weights
    w_alt_lo, w_alt_hi, w_inc_lo, w_inc_hi, w_raan_lo, w_raan_hi, diagonal = (
        trim(part, have, halo - 1) for part in parts
    )
    centre = field[1:-1]
    v_down, v_up = field[:-2], field[2:]
    zero_inc = jnp.zeros_like(centre[:, :1])
    v_prev = jnp.concatenate([zero_inc, centre[:, :-1]], 1)
    v_next = jnp.concatenate([centre[:, 1:], zero_inc], 1)
    v_left, v_right = lane_shifts(centre)
    beside = (
        w_alt_lo * v_down
        + w_alt_hi * v_up
        + w_inc_lo * v_prev
        + w_inc_hi * v_next
        + w_raan_lo * v_left
        + w_raan_hi * v_right
    )
    return diagonal * centre - beside, centre


def inside(shape, halo):
    depth = shape[0] - 2 * halo
    rows = lax.broadcasted_iota(jnp.int32, shape, 0) + lax.axis_index("alt") * depth - halo
    return (rows >= 0) & (rows < depth * lax.axis_size("alt"))


def sweep(weights, field, halo, target, target_halo):
    applied, centre = apply_op(weights, field, halo)
    diagonal = trim(weights[0][6], weights[1], halo - 1)
    updated = centre + OMEGA * (trim(target, target_halo, halo - 1) - applied) / diagonal
    return jnp.where(inside(updated.shape, halo - 1), updated, 0.0)


def first_sweep(weights, target, halo):
    diagonal = trim(weights[0][6], weights[1], halo)
    return OMEGA * target / diagonal


def shards(source, k_alt, k_inc, k_raan):
    length = source.shape[-1]
    halo_r = min(RAAN_HALO, length)
    wide = raan_extend(jnp.stack([source, k_alt, k_inc, k_raan], axis=1), halo_r)
    wide_source, wide_alt, wide_inc, wide_raan = (wide[:, i] for i in range(4))
    coef_two = [coarsen(part) for part in (wide_alt, wide_inc, wide_raan)]
    coef_three = [coarsen(part) for part in coef_two]

    first, second, two_x, three_x = alt_extend(
        [(wide[:, 0:2], 3), (wide[:, 2:4], 2), (jnp.stack(coef_two, 1), 3), (jnp.stack(coef_three, 1), 4)]
    )
    source_x, alt_x = first[:, 0], first[:, 1]
    weights_one = make_weights(alt_x, second[:, 0], second[:, 1], 1.0, 2)
    weights_two = make_weights(two_x[:, 0], trim(two_x[:, 1], 3, 2), trim(two_x[:, 2], 3, 2), 0.25, 2)
    weights_three = make_weights(
        three_x[:, 0], trim(three_x[:, 1], 4, 3), trim(three_x[:, 2], 4, 3), 0.0625, 3
    )

    density = sweep(weights_one, source_x, 3, source_x, 3)
    density = sweep(weights_one, density, 2, source_x, 3)
    applied, _ = apply_op(weights_one, density, 1)
    rhs_two = coarsen(trim(source_x, 3, 0) - applied)
    density = trim(density, 1, 0)

    (rhs_two_x,) = alt_extend([(rhs_two, 2)])
    correction = first_sweep(weights_two, rhs_two_x, 2)
    correction = sweep(weights_two, correction, 2, rhs_two_x, 2)
    applied, _ = apply_op(weights_two, correction, 1)
    rhs_three = coarsen(trim(rhs_two_x, 2, 0) - applied)
    correction = trim(correction, 1, 0)

    (rhs_three_x,) = alt_extend([(rhs_three, COARSE_SWEEPS - 1)])
    coarse_part = first_sweep(weights_three, rhs_three_x, COARSE_SWEEPS - 1)
    for halo in range(COARSE_SWEEPS - 1, 0, -1):
        coarse_part = sweep(weights_three, coarse_part, halo, rhs_three_x, COARSE_SWEEPS - 1)

    correction = correction + refine(coarse_part)
    (correction,) = alt_extend([(correction, SWEEPS)])
    for halo in range(SWEEPS, 0, -1):
        correction = sweep(weights_two, correction, halo, rhs_two_x, 2)

    density = density + refine(correction)
    (density,) = alt_extend([(density, SWEEPS + 1)])
    for halo in range(SWEEPS + 1, 1, -1):
        density = sweep(weights_one, density, halo, source_x, 3)
    applied, centre = apply_op(weights_one, density, 1)
    scaled_residual = (trim(source_x, 3, 0) - applied) / trim(weights_one[0][6], 2, 0)
    keep = slice(halo_r, halo_r + length)
    return (centre[..., keep], scaled_residual[..., keep])


def solution(mesh):
    spec = P("alt", None, "raan")
    return jax.shard_map(
        shards, mesh=mesh, in_specs=(spec,) * 4, out_specs=(spec, spec), check_vma=False
    )
```

```python
import jax
import jax.numpy as jnp
from jax import lax
from jax.sharding import PartitionSpec as P

SWEEPS = 2
COARSE_SWEEPS = 4
OMEGA = 0.75
RAAN_HALO = 32
HIGH = lax.Precision.HIGHEST


def pairing(fine):
    rows = lax.broadcasted_iota(jnp.int32, (fine, fine // 2), 0) // 2
    cols = lax.broadcasted_iota(jnp.int32, (fine, fine // 2), 1)
    return (rows == cols).astype(jnp.float32)


def coarsen(values):
    depth, width, length = values.shape
    summed = values.reshape(depth // 2, 2, width, length).sum(axis=1)
    summed = jnp.matmul(summed, pairing(length), precision=HIGH)
    summed = jnp.matmul(pairing(width).T[None], summed, precision=HIGH)
    return summed * 0.125


def refine(values):
    depth, width, length = values.shape
    grown = jnp.matmul(values, pairing(2 * length).T, precision=HIGH)
    grown = jnp.matmul(pairing(2 * width)[None], grown, precision=HIGH)
    grown = jnp.broadcast_to(grown[:, None], (depth, 2, 2 * width, 2 * length))
    return grown.reshape(2 * depth, 2 * width, 2 * length)


def raan_extend(values, halo):
    count, length = lax.axis_size("raan"), values.shape[-1]
    up = [(i, (i + 1) % count) for i in range(count)]
    down = [(j, i) for i, j in up]
    before = lax.ppermute(values[..., length - halo:], "raan", up)
    after = lax.ppermute(values[..., :halo], "raan", down)
    return jnp.concatenate([before, values, after], axis=-1)


def alt_extend(values, halo):
    count, depth = lax.axis_size("alt"), values.shape[0]
    below, above = [], []
    for distance in range(1, -(-halo // depth) + 1):
        low = max(0, distance * depth - halo)
        high = min(depth, halo - (distance - 1) * depth)
        up = [(i, i + distance) for i in range(count) if i + distance < count]
        down = [(i, i - distance) for i in range(count) if i - distance >= 0]
        below.insert(0, lax.ppermute(values[low:], "alt", up))
        above.append(lax.ppermute(values[:high], "alt", down))
    return jnp.concatenate(below + [values] + above, axis=0)


def trim(values, have, want):
    cut = have - want
    return values[cut:values.shape[0] - cut] if cut else values


def lane_shifts(values):
    zero = jnp.zeros_like(values[..., :1])
    left = jnp.concatenate([zero, values[..., :-1]], axis=-1)
    right = jnp.concatenate([values[..., 1:], zero], axis=-1)
    return left, right


def make_weights(coef_alt, coef_inc, coef_raan, factor, halo):
    centre = coef_alt[1:-1]
    w_alt_lo = factor * 0.5 * (centre + coef_alt[:-2])
    w_alt_hi = factor * 0.5 * (centre + coef_alt[2:])
    inner_faces = factor * 0.5 * (coef_inc[:, :-1] + coef_inc[:, 1:])
    zero_inc = jnp.zeros_like(coef_inc[:, :1])
    w_inc_lo = jnp.concatenate([zero_inc, inner_faces], 1)
    w_inc_hi = jnp.concatenate([inner_faces, zero_inc], 1)
    raan_left, raan_right = lane_shifts(coef_raan)
    w_raan_lo = factor * 0.5 * (coef_raan + raan_left)
    w_raan_hi = factor * 0.5 * (coef_raan + raan_right)
    diagonal = 1.0 + (w_alt_lo + w_alt_hi + w_inc_lo + w_inc_hi + w_raan_lo + w_raan_hi)
    return (w_alt_lo, w_alt_hi, w_inc_lo, w_inc_hi, w_raan_lo, w_raan_hi, diagonal), halo


def apply_op(weights, field, halo):
    parts, have = weights
    w_alt_lo, w_alt_hi, w_inc_lo, w_inc_hi, w_raan_lo, w_raan_hi, diagonal = (
        trim(part, have, halo - 1) for part in parts
    )
    centre = field[1:-1]
    v_down, v_up = field[:-2], field[2:]
    zero_inc = jnp.zeros_like(centre[:, :1])
    v_prev = jnp.concatenate([zero_inc, centre[:, :-1]], 1)
    v_next = jnp.concatenate([centre[:, 1:], zero_inc], 1)
    v_left, v_right = lane_shifts(centre)
    beside = (
        w_alt_lo * v_down
        + w_alt_hi * v_up
        + w_inc_lo * v_prev
        + w_inc_hi * v_next
        + w_raan_lo * v_left
        + w_raan_hi * v_right
    )
    return diagonal * centre - beside, centre


def inside(shape, halo):
    depth = shape[0] - 2 * halo
    rows = lax.broadcasted_iota(jnp.int32, shape, 0) + lax.axis_index("alt") * depth - halo
    return (rows >= 0) & (rows < depth * lax.axis_size("alt"))


def sweep(weights, field, halo, target, target_halo):
    applied, centre = apply_op(weights, field, halo)
    diagonal = trim(weights[0][6], weights[1], halo - 1)
    updated = centre + OMEGA * (trim(target, target_halo, halo - 1) - applied) / diagonal
    return jnp.where(inside(updated.shape, halo - 1), updated, 0.0)


def first_sweep(weights, target, halo):
    diagonal = trim(weights[0][6], weights[1], halo)
    return OMEGA * target / diagonal


def shards(source, k_alt, k_inc, k_raan):
    length = source.shape[-1]
    halo_r = min(RAAN_HALO, length)
    wide = raan_extend(jnp.stack([source, k_alt, k_inc, k_raan], axis=1), halo_r)
    wide_source, wide_alt, wide_inc, wide_raan = (wide[:, i] for i in range(4))
    coef_two = [coarsen(part) for part in (wide_alt, wide_inc, wide_raan)]
    coef_three = [coarsen(part) for part in coef_two]

    first = alt_extend(wide[:, 0:2], 1)
    source_x = first[:, 0]
    weights_one = make_weights(first[:, 1], wide_inc, wide_raan, 1.0, 0)

    density = sweep(weights_one, source_x, 1, source_x, 1)
    density = sweep(weights_one, alt_extend(density, 1), 1, source_x, 1)
    applied, density = apply_op(weights_one, alt_extend(density, 1), 1)
    rhs_two = coarsen(wide_source - applied)

    level_two = alt_extend(jnp.stack([rhs_two] + coef_two, 1), 3)
    weights_two = make_weights(
        level_two[:, 1], trim(level_two[:, 2], 3, 2), trim(level_two[:, 3], 3, 2), 0.25, 2
    )
    rhs_two_x = trim(level_two[:, 0], 3, 2)
    correction = first_sweep(weights_two, rhs_two_x, 2)
    correction = sweep(weights_two, correction, 2, rhs_two_x, 2)
    applied, correction = apply_op(weights_two, correction, 1)
    rhs_three = coarsen(trim(rhs_two_x, 2, 0) - applied)

    reach = COARSE_SWEEPS - 1
    level_three = alt_extend(jnp.stack([rhs_three] + coef_three, 1), reach + 1)
    weights_three = make_weights(
        level_three[:, 1],
        trim(level_three[:, 2], reach + 1, reach),
        trim(level_three[:, 3], reach + 1, reach),
        0.0625,
        reach,
    )
    rhs_three_x = trim(level_three[:, 0], reach + 1, reach)
    coarse_part = first_sweep(weights_three, rhs_three_x, reach)
    for halo in range(reach, 0, -1):
        coarse_part = sweep(weights_three, coarse_part, halo, rhs_three_x, reach)

    correction = correction + refine(coarse_part)
    correction = alt_extend(correction, SWEEPS)
    for halo in range(SWEEPS, 0, -1):
        correction = sweep(weights_two, correction, halo, rhs_two_x, 2)

    density = density + refine(correction)
    for _ in range(SWEEPS):
        density = sweep(weights_one, alt_extend(density, 1), 1, source_x, 1)
    applied, centre = apply_op(weights_one, alt_extend(density, 1), 1)
    scaled_residual = (wide_source - applied) / weights_one[0][6]
    keep = slice(halo_r, halo_r + length)
    return (centre[..., keep], scaled_residual[..., keep])


def solution(mesh):
    spec = P("alt", None, "raan")
    return jax.shard_map(
        shards, mesh=mesh, in_specs=(spec,) * 4, out_specs=(spec, spec), check_vma=False
    )
```

```python
import jax
import jax.numpy as jnp
from jax import lax
from jax.sharding import PartitionSpec as P

SWEEPS = 2
COARSE_SWEEPS = 4
OMEGA = 0.75
RAAN_HALO = 32
HIGH = lax.Precision.HIGHEST


def pairing(fine):
    rows = lax.broadcasted_iota(jnp.int32, (fine, fine // 2), 0) // 2
    cols = lax.broadcasted_iota(jnp.int32, (fine, fine // 2), 1)
    return (rows == cols).astype(jnp.float32)


def coarsen(values):
    depth, width, length = values.shape
    summed = values.reshape(depth // 2, 2, width, length).sum(axis=1)
    summed = jnp.matmul(summed, pairing(length), precision=HIGH)
    summed = jnp.matmul(pairing(width).T[None], summed, precision=HIGH)
    return summed * 0.125


def refine(values):
    depth, width, length = values.shape
    grown = jnp.matmul(values, pairing(2 * length).T, precision=HIGH)
    grown = jnp.matmul(pairing(2 * width)[None], grown, precision=HIGH)
    grown = jnp.broadcast_to(grown[:, None], (depth, 2, 2 * width, 2 * length))
    return grown.reshape(2 * depth, 2 * width, 2 * length)


def raan_extend(values, halo):
    count, length = lax.axis_size("raan"), values.shape[-1]
    up = [(i, (i + 1) % count) for i in range(count)]
    down = [(j, i) for i, j in up]
    before = lax.ppermute(values[..., length - halo:], "raan", up)
    after = lax.ppermute(values[..., :halo], "raan", down)
    return jnp.concatenate([before, values, after], axis=-1)


def alt_extend(values, halo):
    count, depth = lax.axis_size("alt"), values.shape[0]
    below, above = [], []
    for distance in range(1, -(-halo // depth) + 1):
        low = max(0, distance * depth - halo)
        high = min(depth, halo - (distance - 1) * depth)
        up = [(i, i + distance) for i in range(count) if i + distance < count]
        down = [(i, i - distance) for i in range(count) if i - distance >= 0]
        below.insert(0, lax.ppermute(values[low:], "alt", up))
        above.append(lax.ppermute(values[:high], "alt", down))
    return jnp.concatenate(below + [values] + above, axis=0)


def trim(values, have, want):
    cut = have - want
    return values[cut:values.shape[0] - cut] if cut else values


def lane_shifts(values):
    zero = jnp.zeros_like(values[..., :1])
    left = jnp.concatenate([zero, values[..., :-1]], axis=-1)
    right = jnp.concatenate([values[..., 1:], zero], axis=-1)
    return left, right


def make_weights(coef_alt, coef_inc, coef_raan, factor, halo):
    centre = coef_alt[1:-1]
    w_alt_lo = factor * 0.5 * (centre + coef_alt[:-2])
    w_alt_hi = factor * 0.5 * (centre + coef_alt[2:])
    inner_faces = factor * 0.5 * (coef_inc[:, :-1] + coef_inc[:, 1:])
    zero_inc = jnp.zeros_like(coef_inc[:, :1])
    w_inc_lo = jnp.concatenate([zero_inc, inner_faces], 1)
    w_inc_hi = jnp.concatenate([inner_faces, zero_inc], 1)
    raan_left, raan_right = lane_shifts(coef_raan)
    w_raan_lo = factor * 0.5 * (coef_raan + raan_left)
    w_raan_hi = factor * 0.5 * (coef_raan + raan_right)
    diagonal = 1.0 + (w_alt_lo + w_alt_hi + w_inc_lo + w_inc_hi + w_raan_lo + w_raan_hi)
    return (w_alt_lo, w_alt_hi, w_inc_lo, w_inc_hi, w_raan_lo, w_raan_hi, diagonal), halo


def apply_op(weights, field, halo):
    parts, have = weights
    w_alt_lo, w_alt_hi, w_inc_lo, w_inc_hi, w_raan_lo, w_raan_hi, diagonal = (
        trim(part, have, halo - 1) for part in parts
    )
    centre = field[1:-1]
    v_down, v_up = field[:-2], field[2:]
    zero_inc = jnp.zeros_like(centre[:, :1])
    v_prev = jnp.concatenate([zero_inc, centre[:, :-1]], 1)
    v_next = jnp.concatenate([centre[:, 1:], zero_inc], 1)
    v_left, v_right = lane_shifts(centre)
    beside = (
        w_alt_lo * v_down
        + w_alt_hi * v_up
        + w_inc_lo * v_prev
        + w_inc_hi * v_next
        + w_raan_lo * v_left
        + w_raan_hi * v_right
    )
    return diagonal * centre - beside, centre


def inside(shape, halo):
    depth = shape[0] - 2 * halo
    rows = lax.broadcasted_iota(jnp.int32, shape, 0) + lax.axis_index("alt") * depth - halo
    return (rows >= 0) & (rows < depth * lax.axis_size("alt"))


def sweep(weights, field, halo, target, target_halo, masked=True):
    applied, centre = apply_op(weights, field, halo)
    diagonal = trim(weights[0][6], weights[1], halo - 1)
    updated = centre + OMEGA * (trim(target, target_halo, halo - 1) - applied) / diagonal
    if not masked:
        return updated
    return jnp.where(inside(updated.shape, halo - 1), updated, 0.0)


def pad_rows(values):
    zero = jnp.zeros_like(values[:1])
    return jnp.concatenate([zero, values, zero], axis=0)


def first_sweep(weights, target, halo):
    diagonal = trim(weights[0][6], weights[1], halo)
    return OMEGA * target / diagonal


def shards(source, k_alt, k_inc, k_raan):
    length = source.shape[-1]
    halo_r = min(RAAN_HALO, length)
    wide = raan_extend(jnp.stack([source, k_alt, k_inc, k_raan], axis=1), halo_r)
    wide_source, wide_alt, wide_inc, wide_raan = (wide[:, i] for i in range(4))
    coef_two = [coarsen(part) for part in (wide_alt, wide_inc, wide_raan)]
    coef_three = [coarsen(part) for part in coef_two]

    first = alt_extend(wide[:, 0:2], 1)
    source_x = first[:, 0]
    weights_one = make_weights(first[:, 1], wide_inc, wide_raan, 1.0, 0)

    density = sweep(weights_one, source_x, 1, source_x, 1)
    density = sweep(weights_one, alt_extend(density, 1), 1, source_x, 1)
    applied, density = apply_op(weights_one, alt_extend(density, 1), 1)
    rhs_two = coarsen(wide_source - applied)

    level_two = alt_extend(jnp.stack([rhs_two] + coef_two, 1), 3)
    weights_two = make_weights(
        level_two[:, 1], trim(level_two[:, 2], 3, 2), trim(level_two[:, 3], 3, 2), 0.25, 2
    )
    rhs_two_x = trim(level_two[:, 0], 3, 2)
    correction = first_sweep(weights_two, rhs_two_x, 2)
    correction = sweep(weights_two, correction, 2, rhs_two_x, 2)
    applied, correction = apply_op(weights_two, correction, 1)
    rhs_three = coarsen(trim(rhs_two_x, 2, 0) - applied)

    height = rhs_three.shape[0]
    column = lax.all_gather(jnp.stack([rhs_three] + coef_three, 1), "alt", axis=0, tiled=True)
    weights_three = make_weights(pad_rows(column[:, 1]), column[:, 2], column[:, 3], 0.0625, 0)
    rhs_three_x = column[:, 0]
    coarse_part = first_sweep(weights_three, rhs_three_x, 0)
    for _ in range(COARSE_SWEEPS - 1):
        coarse_part = sweep(weights_three, pad_rows(coarse_part), 1, rhs_three_x, 0, masked=False)
    coarse_part = lax.dynamic_slice_in_dim(coarse_part, lax.axis_index("alt") * height, height, 0)

    correction = correction + refine(coarse_part)
    correction = alt_extend(correction, SWEEPS)
    for halo in range(SWEEPS, 0, -1):
        correction = sweep(weights_two, correction, halo, rhs_two_x, 2)

    density = density + refine(correction)
    for _ in range(SWEEPS):
        density = sweep(weights_one, alt_extend(density, 1), 1, source_x, 1)
    applied, centre = apply_op(weights_one, alt_extend(density, 1), 1)
    scaled_residual = (wide_source - applied) / weights_one[0][6]
    keep = slice(halo_r, halo_r + length)
    return (centre[..., keep], scaled_residual[..., keep])


def solution(mesh):
    spec = P("alt", None, "raan")
    return jax.shard_map(
        shards, mesh=mesh, in_specs=(spec,) * 4, out_specs=(spec, spec), check_vma=False
    )
```

```python
import jax
import jax.numpy as jnp
from jax import lax
from jax.sharding import PartitionSpec as P

SWEEPS = 2
COARSE_SWEEPS = 4
OMEGA = 0.75
RAAN_HALO = 32
HIGH = lax.Precision.HIGHEST


def pairing(fine):
    rows = lax.broadcasted_iota(jnp.int32, (fine, fine // 2), 0) // 2
    cols = lax.broadcasted_iota(jnp.int32, (fine, fine // 2), 1)
    return (rows == cols).astype(jnp.float32)


def coarsen(values):
    depth, width, length = values.shape
    summed = values.reshape(depth // 2, 2, width, length).sum(axis=1)
    summed = jnp.matmul(summed, pairing(length), precision=HIGH)
    summed = jnp.matmul(pairing(width).T[None], summed, precision=HIGH)
    return summed * 0.125


def refine(values):
    depth, width, length = values.shape
    grown = jnp.matmul(values, pairing(2 * length).T, precision=HIGH)
    grown = jnp.matmul(pairing(2 * width)[None], grown, precision=HIGH)
    grown = jnp.broadcast_to(grown[:, None], (depth, 2, 2 * width, 2 * length))
    return grown.reshape(2 * depth, 2 * width, 2 * length)


def raan_extend(values, halo):
    count, length = lax.axis_size("raan"), values.shape[-1]
    up = [(i, (i + 1) % count) for i in range(count)]
    down = [(j, i) for i, j in up]
    before = lax.ppermute(values[..., length - halo:], "raan", up)
    after = lax.ppermute(values[..., :halo], "raan", down)
    return jnp.concatenate([before, values, after], axis=-1)


def alt_extend(values, halo):
    count, depth = lax.axis_size("alt"), values.shape[0]
    below, above = [], []
    for distance in range(1, -(-halo // depth) + 1):
        low = max(0, distance * depth - halo)
        high = min(depth, halo - (distance - 1) * depth)
        up = [(i, i + distance) for i in range(count) if i + distance < count]
        down = [(i, i - distance) for i in range(count) if i - distance >= 0]
        below.insert(0, lax.ppermute(values[low:], "alt", up))
        above.append(lax.ppermute(values[:high], "alt", down))
    return jnp.concatenate(below + [values] + above, axis=0)


def trim(values, have, want):
    cut = have - want
    return values[cut:values.shape[0] - cut] if cut else values


def lane_shifts(values):
    zero = jnp.zeros_like(values[..., :1])
    left = jnp.concatenate([zero, values[..., :-1]], axis=-1)
    right = jnp.concatenate([values[..., 1:], zero], axis=-1)
    return left, right


def make_weights(coef_alt, coef_inc, coef_raan, factor, halo):
    centre = coef_alt[1:-1]
    w_alt_lo = factor * 0.5 * (centre + coef_alt[:-2])
    w_alt_hi = factor * 0.5 * (centre + coef_alt[2:])
    inner_faces = factor * 0.5 * (coef_inc[:, :-1] + coef_inc[:, 1:])
    zero_inc = jnp.zeros_like(coef_inc[:, :1])
    w_inc_lo = jnp.concatenate([zero_inc, inner_faces], 1)
    w_inc_hi = jnp.concatenate([inner_faces, zero_inc], 1)
    raan_left, raan_right = lane_shifts(coef_raan)
    w_raan_lo = factor * 0.5 * (coef_raan + raan_left)
    w_raan_hi = factor * 0.5 * (coef_raan + raan_right)
    diagonal = 1.0 + (w_alt_lo + w_alt_hi + w_inc_lo + w_inc_hi + w_raan_lo + w_raan_hi)
    return (w_alt_lo, w_alt_hi, w_inc_lo, w_inc_hi, w_raan_lo, w_raan_hi, diagonal), halo


def apply_op(weights, field, halo):
    parts, have = weights
    w_alt_lo, w_alt_hi, w_inc_lo, w_inc_hi, w_raan_lo, w_raan_hi, diagonal = (
        trim(part, have, halo - 1) for part in parts
    )
    centre = field[1:-1]
    v_down, v_up = field[:-2], field[2:]
    zero_inc = jnp.zeros_like(centre[:, :1])
    v_prev = jnp.concatenate([zero_inc, centre[:, :-1]], 1)
    v_next = jnp.concatenate([centre[:, 1:], zero_inc], 1)
    v_left, v_right = lane_shifts(centre)
    beside = (
        w_alt_lo * v_down
        + w_alt_hi * v_up
        + w_inc_lo * v_prev
        + w_inc_hi * v_next
        + w_raan_lo * v_left
        + w_raan_hi * v_right
    )
    return diagonal * centre - beside, centre


def inside(shape, halo):
    depth = shape[0] - 2 * halo
    rows = lax.broadcasted_iota(jnp.int32, shape, 0) + lax.axis_index("alt") * depth - halo
    return (rows >= 0) & (rows < depth * lax.axis_size("alt"))


def sweep(weights, field, halo, target, target_halo, masked=True):
    applied, centre = apply_op(weights, field, halo)
    diagonal = trim(weights[0][6], weights[1], halo - 1)
    updated = centre + OMEGA * (trim(target, target_halo, halo - 1) - applied) / diagonal
    if not masked:
        return updated
    return jnp.where(inside(updated.shape, halo - 1), updated, 0.0)


def pad_rows(values):
    zero = jnp.zeros_like(values[:1])
    return jnp.concatenate([zero, values, zero], axis=0)


def first_sweep(weights, target, halo):
    diagonal = trim(weights[0][6], weights[1], halo)
    return OMEGA * target / diagonal


def shards(source, k_alt, k_inc, k_raan):
    length = source.shape[-1]
    halo_r = min(RAAN_HALO, length)
    wide = raan_extend(jnp.stack([source, k_alt, k_inc, k_raan], axis=1), halo_r)
    wide_source, wide_alt, wide_inc, wide_raan = (wide[:, i] for i in range(4))
    coef_two = [coarsen(part) for part in (wide_alt, wide_inc, wide_raan)]
    coef_three = [coarsen(part) for part in coef_two]

    reach = SWEEPS + 1
    first = alt_extend(wide, reach)
    source_x = first[:, 0]
    weights_one = make_weights(
        first[:, 1], trim(first[:, 2], reach, reach - 1), trim(first[:, 3], reach, reach - 1), 1.0, reach - 1
    )

    density = source_x
    for halo in range(reach, 1, -1):
        density = sweep(weights_one, density, halo, source_x, reach)
    applied, density = apply_op(weights_one, density, 1)
    rhs_two = coarsen(wide_source - applied)

    level_two = alt_extend(jnp.stack([rhs_two] + coef_two, 1), 3)
    weights_two = make_weights(
        level_two[:, 1], trim(level_two[:, 2], 3, 2), trim(level_two[:, 3], 3, 2), 0.25, 2
    )
    rhs_two_x = trim(level_two[:, 0], 3, 2)
    correction = first_sweep(weights_two, rhs_two_x, 2)
    correction = sweep(weights_two, correction, 2, rhs_two_x, 2)
    applied, correction = apply_op(weights_two, correction, 1)
    rhs_three = coarsen(trim(rhs_two_x, 2, 0) - applied)

    height = rhs_three.shape[0]
    column = lax.all_gather(jnp.stack([rhs_three] + coef_three, 1), "alt", axis=0, tiled=True)
    weights_three = make_weights(pad_rows(column[:, 1]), column[:, 2], column[:, 3], 0.0625, 0)
    rhs_three_x = column[:, 0]
    coarse_part = first_sweep(weights_three, rhs_three_x, 0)
    for _ in range(COARSE_SWEEPS - 1):
        coarse_part = sweep(weights_three, pad_rows(coarse_part), 1, rhs_three_x, 0, masked=False)
    coarse_part = lax.dynamic_slice_in_dim(coarse_part, lax.axis_index("alt") * height, height, 0)

    correction = correction + refine(coarse_part)
    correction = alt_extend(correction, SWEEPS)
    for halo in range(SWEEPS, 0, -1):
        correction = sweep(weights_two, correction, halo, rhs_two_x, 2)

    density = alt_extend(density + refine(correction), reach)
    for halo in range(reach, 1, -1):
        density = sweep(weights_one, density, halo, source_x, reach)
    applied, centre = apply_op(weights_one, density, 1)
    scaled_residual = (wide_source - applied) / trim(weights_one[0][6], weights_one[1], 0)
    keep = slice(halo_r, halo_r + length)
    return (centre[..., keep], scaled_residual[..., keep])


def solution(mesh):
    spec = P("alt", None, "raan")
    return jax.shard_map(
        shards, mesh=mesh, in_specs=(spec,) * 4, out_specs=(spec, spec), check_vma=False
    )
```

```python
import jax
import jax.numpy as jnp
from jax import lax
from jax.sharding import PartitionSpec as P

SWEEPS = 2
COARSE_SWEEPS = 4
OMEGA = 0.75
RAAN_HALO = 32
HIGH = lax.Precision.HIGHEST


def pairing(fine):
    rows = lax.broadcasted_iota(jnp.int32, (fine, fine // 2), 0) // 2
    cols = lax.broadcasted_iota(jnp.int32, (fine, fine // 2), 1)
    return (rows == cols).astype(jnp.float32)


def coarsen(values):
    depth, width, length = values.shape
    summed = values.reshape(depth // 2, 2, width, length).sum(axis=1)
    summed = jnp.matmul(summed, pairing(length), precision=HIGH)
    summed = jnp.matmul(pairing(width).T[None], summed, precision=HIGH)
    return summed * 0.125


def refine(values):
    depth, width, length = values.shape
    grown = jnp.matmul(values, pairing(2 * length).T, precision=HIGH)
    grown = jnp.matmul(pairing(2 * width)[None], grown, precision=HIGH)
    grown = jnp.broadcast_to(grown[:, None], (depth, 2, 2 * width, 2 * length))
    return grown.reshape(2 * depth, 2 * width, 2 * length)


def raan_extend(values, halo):
    count, length = lax.axis_size("raan"), values.shape[-1]
    up = [(i, (i + 1) % count) for i in range(count)]
    down = [(j, i) for i, j in up]
    before = lax.ppermute(values[..., length - halo:], "raan", up)
    after = lax.ppermute(values[..., :halo], "raan", down)
    return jnp.concatenate([before, values, after], axis=-1)


def alt_extend(values, halo):
    count, depth = lax.axis_size("alt"), values.shape[0]
    below, above = [], []
    for distance in range(1, -(-halo // depth) + 1):
        low = max(0, distance * depth - halo)
        high = min(depth, halo - (distance - 1) * depth)
        up = [(i, i + distance) for i in range(count) if i + distance < count]
        down = [(i, i - distance) for i in range(count) if i - distance >= 0]
        below.insert(0, lax.ppermute(values[low:], "alt", up))
        above.append(lax.ppermute(values[:high], "alt", down))
    return jnp.concatenate(below + [values] + above, axis=0)


def slot_gather(values):
    count = lax.axis_size("alt")
    slots = jnp.zeros((count,) + values.shape, values.dtype)
    slots = lax.dynamic_update_index_in_dim(slots, values, lax.axis_index("alt"), 0)
    return lax.psum(slots, "alt").reshape((count * values.shape[0],) + values.shape[1:])


def trim(values, have, want):
    cut = have - want
    return values[cut:values.shape[0] - cut] if cut else values


def lane_shifts(values):
    zero = jnp.zeros_like(values[..., :1])
    left = jnp.concatenate([zero, values[..., :-1]], axis=-1)
    right = jnp.concatenate([values[..., 1:], zero], axis=-1)
    return left, right


def make_weights(coef_alt, coef_inc, coef_raan, factor, halo):
    centre = coef_alt[1:-1]
    w_alt_lo = factor * 0.5 * (centre + coef_alt[:-2])
    w_alt_hi = factor * 0.5 * (centre + coef_alt[2:])
    inner_faces = factor * 0.5 * (coef_inc[:, :-1] + coef_inc[:, 1:])
    zero_inc = jnp.zeros_like(coef_inc[:, :1])
    w_inc_lo = jnp.concatenate([zero_inc, inner_faces], 1)
    w_inc_hi = jnp.concatenate([inner_faces, zero_inc], 1)
    raan_left, raan_right = lane_shifts(coef_raan)
    w_raan_lo = factor * 0.5 * (coef_raan + raan_left)
    w_raan_hi = factor * 0.5 * (coef_raan + raan_right)
    diagonal = 1.0 + (w_alt_lo + w_alt_hi + w_inc_lo + w_inc_hi + w_raan_lo + w_raan_hi)
    return (w_alt_lo, w_alt_hi, w_inc_lo, w_inc_hi, w_raan_lo, w_raan_hi, diagonal), halo


def apply_op(weights, field, halo):
    parts, have = weights
    w_alt_lo, w_alt_hi, w_inc_lo, w_inc_hi, w_raan_lo, w_raan_hi, diagonal = (
        trim(part, have, halo - 1) for part in parts
    )
    centre = field[1:-1]
    v_down, v_up = field[:-2], field[2:]
    zero_inc = jnp.zeros_like(centre[:, :1])
    v_prev = jnp.concatenate([zero_inc, centre[:, :-1]], 1)
    v_next = jnp.concatenate([centre[:, 1:], zero_inc], 1)
    v_left, v_right = lane_shifts(centre)
    beside = (
        w_alt_lo * v_down
        + w_alt_hi * v_up
        + w_inc_lo * v_prev
        + w_inc_hi * v_next
        + w_raan_lo * v_left
        + w_raan_hi * v_right
    )
    return diagonal * centre - beside, centre


def inside(shape, halo):
    depth = shape[0] - 2 * halo
    rows = lax.broadcasted_iota(jnp.int32, shape, 0) + lax.axis_index("alt") * depth - halo
    return (rows >= 0) & (rows < depth * lax.axis_size("alt"))


def sweep(weights, field, halo, target, target_halo, masked=True):
    applied, centre = apply_op(weights, field, halo)
    diagonal = trim(weights[0][6], weights[1], halo - 1)
    updated = centre + OMEGA * (trim(target, target_halo, halo - 1) - applied) / diagonal
    if not masked:
        return updated
    return jnp.where(inside(updated.shape, halo - 1), updated, 0.0)


def pad_rows(values):
    zero = jnp.zeros_like(values[:1])
    return jnp.concatenate([zero, values, zero], axis=0)


def first_sweep(weights, target, halo):
    diagonal = trim(weights[0][6], weights[1], halo)
    return OMEGA * target / diagonal


def shards(source, k_alt, k_inc, k_raan):
    length = source.shape[-1]
    halo_r = min(RAAN_HALO, length)
    wide = raan_extend(jnp.stack([source, k_alt, k_inc, k_raan], axis=1), halo_r)
    wide_source, wide_alt, wide_inc, wide_raan = (wide[:, i] for i in range(4))
    coef_two = [coarsen(part) for part in (wide_alt, wide_inc, wide_raan)]
    coef_three = [coarsen(part) for part in coef_two]

    first = alt_extend(wide[:, 0:2], 1)
    source_x = first[:, 0]
    weights_one = make_weights(first[:, 1], wide_inc, wide_raan, 1.0, 0)

    density = sweep(weights_one, source_x, 1, source_x, 1)
    density = sweep(weights_one, alt_extend(density, 1), 1, source_x, 1)
    applied, density = apply_op(weights_one, alt_extend(density, 1), 1)
    rhs_two = coarsen(wide_source - applied)

    level_two = alt_extend(jnp.stack([rhs_two] + coef_two, 1), 3)
    weights_two = make_weights(
        level_two[:, 1], trim(level_two[:, 2], 3, 2), trim(level_two[:, 3], 3, 2), 0.25, 2
    )
    rhs_two_x = trim(level_two[:, 0], 3, 2)
    correction = first_sweep(weights_two, rhs_two_x, 2)
    correction = sweep(weights_two, correction, 2, rhs_two_x, 2)
    applied, correction = apply_op(weights_two, correction, 1)
    rhs_three = coarsen(trim(rhs_two_x, 2, 0) - applied)

    height = rhs_three.shape[0]
    column = slot_gather(jnp.stack([rhs_three] + coef_three, 1))
    weights_three = make_weights(pad_rows(column[:, 1]), column[:, 2], column[:, 3], 0.0625, 0)
    rhs_three_x = column[:, 0]
    coarse_part = first_sweep(weights_three, rhs_three_x, 0)
    for _ in range(COARSE_SWEEPS - 1):
        coarse_part = sweep(weights_three, pad_rows(coarse_part), 1, rhs_three_x, 0, masked=False)
    coarse_part = lax.dynamic_slice_in_dim(coarse_part, lax.axis_index("alt") * height, height, 0)

    correction = correction + refine(coarse_part)
    correction = alt_extend(correction, SWEEPS)
    for halo in range(SWEEPS, 0, -1):
        correction = sweep(weights_two, correction, halo, rhs_two_x, 2)

    density = density + refine(correction)
    for _ in range(SWEEPS):
        density = sweep(weights_one, alt_extend(density, 1), 1, source_x, 1)
    applied, centre = apply_op(weights_one, alt_extend(density, 1), 1)
    scaled_residual = (wide_source - applied) / weights_one[0][6]
    keep = slice(halo_r, halo_r + length)
    return (centre[..., keep], scaled_residual[..., keep])


def solution(mesh):
    spec = P("alt", None, "raan")
    return jax.shard_map(
        shards, mesh=mesh, in_specs=(spec,) * 4, out_specs=(spec, spec), check_vma=False
    )
```

```python
import jax
import jax.numpy as jnp
from jax import lax
from jax.sharding import PartitionSpec as P

SWEEPS = 2
COARSE_SWEEPS = 4
OMEGA = 0.75
RAAN_HALO = 32
HIGH = lax.Precision.HIGHEST


def pairing(fine):
    rows = lax.broadcasted_iota(jnp.int32, (fine, fine // 2), 0) // 2
    cols = lax.broadcasted_iota(jnp.int32, (fine, fine // 2), 1)
    return (rows == cols).astype(jnp.float32)


def coarsen(values):
    depth, width, length = values.shape
    summed = values.reshape(depth // 2, 2, width, length).sum(axis=1)
    summed = jnp.matmul(summed, pairing(length), precision=HIGH)
    summed = jnp.matmul(pairing(width).T[None], summed, precision=HIGH)
    return summed * 0.125


def refine(values):
    depth, width, length = values.shape
    grown = jnp.matmul(values, pairing(2 * length).T, precision=HIGH)
    grown = jnp.matmul(pairing(2 * width)[None], grown, precision=HIGH)
    grown = jnp.broadcast_to(grown[:, None], (depth, 2, 2 * width, 2 * length))
    return grown.reshape(2 * depth, 2 * width, 2 * length)


def raan_extend(values, halo):
    count, length = lax.axis_size("raan"), values.shape[-1]
    up = [(i, (i + 1) % count) for i in range(count)]
    down = [(j, i) for i, j in up]
    before = lax.ppermute(values[..., length - halo:], "raan", up)
    after = lax.ppermute(values[..., :halo], "raan", down)
    return jnp.concatenate([before, values, after], axis=-1)


def alt_extend(values, halo):
    count, depth = lax.axis_size("alt"), values.shape[0]
    below, above = [], []
    for distance in range(1, -(-halo // depth) + 1):
        low = max(0, distance * depth - halo)
        high = min(depth, halo - (distance - 1) * depth)
        up = [(i, i + distance) for i in range(count) if i + distance < count]
        down = [(i, i - distance) for i in range(count) if i - distance >= 0]
        below.insert(0, lax.ppermute(values[low:], "alt", up))
        above.append(lax.ppermute(values[:high], "alt", down))
    return jnp.concatenate(below + [values] + above, axis=0)


def trim(values, have, want):
    cut = have - want
    return values[cut:values.shape[0] - cut] if cut else values


def lane_shifts(values):
    zero = jnp.zeros_like(values[..., :1])
    left = jnp.concatenate([zero, values[..., :-1]], axis=-1)
    right = jnp.concatenate([values[..., 1:], zero], axis=-1)
    return left, right


def make_weights(coef_alt, coef_inc, coef_raan, factor, halo):
    centre = coef_alt[1:-1]
    w_alt_lo = factor * 0.5 * (centre + coef_alt[:-2])
    w_alt_hi = factor * 0.5 * (centre + coef_alt[2:])
    inner_faces = factor * 0.5 * (coef_inc[:, :-1] + coef_inc[:, 1:])
    zero_inc = jnp.zeros_like(coef_inc[:, :1])
    w_inc_lo = jnp.concatenate([zero_inc, inner_faces], 1)
    w_inc_hi = jnp.concatenate([inner_faces, zero_inc], 1)
    raan_left, raan_right = lane_shifts(coef_raan)
    w_raan_lo = factor * 0.5 * (coef_raan + raan_left)
    w_raan_hi = factor * 0.5 * (coef_raan + raan_right)
    diagonal = 1.0 + (w_alt_lo + w_alt_hi + w_inc_lo + w_inc_hi + w_raan_lo + w_raan_hi)
    return (w_alt_lo, w_alt_hi, w_inc_lo, w_inc_hi, w_raan_lo, w_raan_hi, diagonal), halo


def apply_op(weights, field, halo):
    parts, have = weights
    w_alt_lo, w_alt_hi, w_inc_lo, w_inc_hi, w_raan_lo, w_raan_hi, diagonal = (
        trim(part, have, halo - 1) for part in parts
    )
    centre = field[1:-1]
    v_down, v_up = field[:-2], field[2:]
    zero_inc = jnp.zeros_like(centre[:, :1])
    v_prev = jnp.concatenate([zero_inc, centre[:, :-1]], 1)
    v_next = jnp.concatenate([centre[:, 1:], zero_inc], 1)
    v_left, v_right = lane_shifts(centre)
    beside = (
        w_alt_lo * v_down
        + w_alt_hi * v_up
        + w_inc_lo * v_prev
        + w_inc_hi * v_next
        + w_raan_lo * v_left
        + w_raan_hi * v_right
    )
    return diagonal * centre - beside, centre


def inside(shape, halo):
    depth = shape[0] - 2 * halo
    rows = lax.broadcasted_iota(jnp.int32, shape, 0) + lax.axis_index("alt") * depth - halo
    return (rows >= 0) & (rows < depth * lax.axis_size("alt"))


def sweep(weights, field, halo, target, target_halo, masked=True):
    applied, centre = apply_op(weights, field, halo)
    diagonal = trim(weights[0][6], weights[1], halo - 1)
    updated = centre + OMEGA * (trim(target, target_halo, halo - 1) - applied) / diagonal
    if not masked:
        return updated
    return jnp.where(inside(updated.shape, halo - 1), updated, 0.0)


def pad_rows(values):
    zero = jnp.zeros_like(values[:1])
    return jnp.concatenate([zero, values, zero], axis=0)


def first_sweep(weights, target, halo):
    diagonal = trim(weights[0][6], weights[1], halo)
    return OMEGA * target / diagonal


def shards(source, k_alt, k_inc, k_raan):
    length = source.shape[-1]
    halo_r = min(RAAN_HALO, length)
    wide = raan_extend(jnp.stack([k_alt, source, k_inc, k_raan], axis=1), halo_r)
    wide_alt, wide_source, wide_inc, wide_raan = (wide[:, i] for i in range(4))
    coef_two = [coarsen(part) for part in (wide_alt, wide_inc, wide_raan)]
    coef_three = [coarsen(part) for part in coef_two]

    reach = SWEEPS + 1
    alt_x = alt_extend(wide[:, 0], reach)
    rest = alt_extend(wide[:, 1:4], reach - 1)
    source_x = rest[:, 0]
    weights_one = make_weights(alt_x, rest[:, 1], rest[:, 2], 1.0, reach - 1)

    density = source_x
    for halo in range(reach - 1, 0, -1):
        density = sweep(weights_one, density, halo, source_x, reach - 1)
    applied, density = apply_op(weights_one, alt_extend(density, 1), 1)
    rhs_two = coarsen(wide_source - applied)

    level_two = alt_extend(jnp.stack([rhs_two] + coef_two, 1), 3)
    weights_two = make_weights(
        level_two[:, 1], trim(level_two[:, 2], 3, 2), trim(level_two[:, 3], 3, 2), 0.25, 2
    )
    rhs_two_x = trim(level_two[:, 0], 3, 2)
    correction = first_sweep(weights_two, rhs_two_x, 2)
    correction = sweep(weights_two, correction, 2, rhs_two_x, 2)
    applied, correction = apply_op(weights_two, correction, 1)
    rhs_three = coarsen(trim(rhs_two_x, 2, 0) - applied)

    height = rhs_three.shape[0]
    column = lax.all_gather(jnp.stack([rhs_three] + coef_three, 1), "alt", axis=0, tiled=True)
    weights_three = make_weights(pad_rows(column[:, 1]), column[:, 2], column[:, 3], 0.0625, 0)
    rhs_three_x = column[:, 0]
    coarse_part = first_sweep(weights_three, rhs_three_x, 0)
    for _ in range(COARSE_SWEEPS - 1):
        coarse_part = sweep(weights_three, pad_rows(coarse_part), 1, rhs_three_x, 0, masked=False)
    coarse_part = lax.dynamic_slice_in_dim(coarse_part, lax.axis_index("alt") * height, height, 0)

    correction = correction + refine(coarse_part)
    correction = alt_extend(correction, SWEEPS)
    for halo in range(SWEEPS, 0, -1):
        correction = sweep(weights_two, correction, halo, rhs_two_x, 2)

    density = alt_extend(density + refine(correction), reach)
    for halo in range(reach, 1, -1):
        density = sweep(weights_one, density, halo, source_x, reach - 1)
    applied, centre = apply_op(weights_one, density, 1)
    scaled_residual = (wide_source - applied) / trim(weights_one[0][6], weights_one[1], 0)
    keep = slice(halo_r, halo_r + length)
    return (centre[..., keep], scaled_residual[..., keep])


def solution(mesh):
    spec = P("alt", None, "raan")
    return jax.shard_map(
        shards, mesh=mesh, in_specs=(spec,) * 4, out_specs=(spec, spec), check_vma=False
    )
```

```python
import jax
import jax.numpy as jnp
from jax import lax
from jax.sharding import PartitionSpec as P

SWEEPS = 2
COARSE_SWEEPS = 4
OMEGA = 0.75
RAAN_HALO = 32
HIGH = lax.Precision.HIGHEST


def pairing(fine):
    rows = lax.broadcasted_iota(jnp.int32, (fine, fine // 2), 0) // 2
    cols = lax.broadcasted_iota(jnp.int32, (fine, fine // 2), 1)
    return (rows == cols).astype(jnp.float32)


def coarsen(values):
    depth, width, length = values.shape
    summed = values.reshape(depth // 2, 2, width, length).sum(axis=1)
    summed = jnp.matmul(summed, pairing(length), precision=HIGH)
    summed = jnp.matmul(pairing(width).T[None], summed, precision=HIGH)
    return summed * 0.125


def refine(values):
    depth, width, length = values.shape
    grown = jnp.matmul(values, pairing(2 * length).T, precision=HIGH)
    grown = jnp.matmul(pairing(2 * width)[None], grown, precision=HIGH)
    grown = jnp.broadcast_to(grown[:, None], (depth, 2, 2 * width, 2 * length))
    return grown.reshape(2 * depth, 2 * width, 2 * length)


def raan_extend(values, halo):
    count, length = lax.axis_size("raan"), values.shape[-1]
    up = [(i, (i + 1) % count) for i in range(count)]
    down = [(j, i) for i, j in up]
    before = lax.ppermute(values[..., length - halo:], "raan", up)
    after = lax.ppermute(values[..., :halo], "raan", down)
    return jnp.concatenate([before, values, after], axis=-1)


def alt_extend(values, halo):
    count, depth = lax.axis_size("alt"), values.shape[0]
    below, above = [], []
    for distance in range(1, -(-halo // depth) + 1):
        low = max(0, distance * depth - halo)
        high = min(depth, halo - (distance - 1) * depth)
        up = [(i, i + distance) for i in range(count) if i + distance < count]
        down = [(i, i - distance) for i in range(count) if i - distance >= 0]
        below.insert(0, lax.ppermute(values[low:], "alt", up))
        above.append(lax.ppermute(values[:high], "alt", down))
    return jnp.concatenate(below + [values] + above, axis=0)


def spread_gather(values):
    count = lax.axis_size("alt")
    copies = jnp.broadcast_to(values[None], (count,) + values.shape)
    every = lax.all_to_all(copies, "alt", 0, 0)
    return every.reshape((count * values.shape[0],) + values.shape[1:])


def trim(values, have, want):
    cut = have - want
    return values[cut:values.shape[0] - cut] if cut else values


def lane_shifts(values):
    zero = jnp.zeros_like(values[..., :1])
    left = jnp.concatenate([zero, values[..., :-1]], axis=-1)
    right = jnp.concatenate([values[..., 1:], zero], axis=-1)
    return left, right


def make_weights(coef_alt, coef_inc, coef_raan, factor, halo):
    centre = coef_alt[1:-1]
    w_alt_lo = factor * 0.5 * (centre + coef_alt[:-2])
    w_alt_hi = factor * 0.5 * (centre + coef_alt[2:])
    inner_faces = factor * 0.5 * (coef_inc[:, :-1] + coef_inc[:, 1:])
    zero_inc = jnp.zeros_like(coef_inc[:, :1])
    w_inc_lo = jnp.concatenate([zero_inc, inner_faces], 1)
    w_inc_hi = jnp.concatenate([inner_faces, zero_inc], 1)
    raan_left, raan_right = lane_shifts(coef_raan)
    w_raan_lo = factor * 0.5 * (coef_raan + raan_left)
    w_raan_hi = factor * 0.5 * (coef_raan + raan_right)
    diagonal = 1.0 + (w_alt_lo + w_alt_hi + w_inc_lo + w_inc_hi + w_raan_lo + w_raan_hi)
    return (w_alt_lo, w_alt_hi, w_inc_lo, w_inc_hi, w_raan_lo, w_raan_hi, diagonal), halo


def apply_op(weights, field, halo):
    parts, have = weights
    w_alt_lo, w_alt_hi, w_inc_lo, w_inc_hi, w_raan_lo, w_raan_hi, diagonal = (
        trim(part, have, halo - 1) for part in parts
    )
    centre = field[1:-1]
    v_down, v_up = field[:-2], field[2:]
    zero_inc = jnp.zeros_like(centre[:, :1])
    v_prev = jnp.concatenate([zero_inc, centre[:, :-1]], 1)
    v_next = jnp.concatenate([centre[:, 1:], zero_inc], 1)
    v_left, v_right = lane_shifts(centre)
    beside = (
        w_alt_lo * v_down
        + w_alt_hi * v_up
        + w_inc_lo * v_prev
        + w_inc_hi * v_next
        + w_raan_lo * v_left
        + w_raan_hi * v_right
    )
    return diagonal * centre - beside, centre


def inside(shape, halo):
    depth = shape[0] - 2 * halo
    rows = lax.broadcasted_iota(jnp.int32, shape, 0) + lax.axis_index("alt") * depth - halo
    return (rows >= 0) & (rows < depth * lax.axis_size("alt"))


def sweep(weights, field, halo, target, target_halo, masked=True):
    applied, centre = apply_op(weights, field, halo)
    diagonal = trim(weights[0][6], weights[1], halo - 1)
    updated = centre + OMEGA * (trim(target, target_halo, halo - 1) - applied) / diagonal
    if not masked:
        return updated
    return jnp.where(inside(updated.shape, halo - 1), updated, 0.0)


def pad_rows(values):
    zero = jnp.zeros_like(values[:1])
    return jnp.concatenate([zero, values, zero], axis=0)


def first_sweep(weights, target, halo):
    diagonal = trim(weights[0][6], weights[1], halo)
    return OMEGA * target / diagonal


def shards(source, k_alt, k_inc, k_raan):
    length = source.shape[-1]
    halo_r = min(RAAN_HALO, length)
    wide = raan_extend(jnp.stack([source, k_alt, k_inc, k_raan], axis=1), halo_r)
    wide_source, wide_alt, wide_inc, wide_raan = (wide[:, i] for i in range(4))
    coef_two = [coarsen(part) for part in (wide_alt, wide_inc, wide_raan)]
    coef_three = [coarsen(part) for part in coef_two]

    first = alt_extend(wide[:, 0:2], 1)
    source_x = first[:, 0]
    weights_one = make_weights(first[:, 1], wide_inc, wide_raan, 1.0, 0)

    density = sweep(weights_one, source_x, 1, source_x, 1)
    density = sweep(weights_one, alt_extend(density, 1), 1, source_x, 1)
    applied, density = apply_op(weights_one, alt_extend(density, 1), 1)
    rhs_two = coarsen(wide_source - applied)

    level_two = alt_extend(jnp.stack([rhs_two] + coef_two, 1), 3)
    weights_two = make_weights(
        level_two[:, 1], trim(level_two[:, 2], 3, 2), trim(level_two[:, 3], 3, 2), 0.25, 2
    )
    rhs_two_x = trim(level_two[:, 0], 3, 2)
    correction = first_sweep(weights_two, rhs_two_x, 2)
    correction = sweep(weights_two, correction, 2, rhs_two_x, 2)
    applied, correction = apply_op(weights_two, correction, 1)
    rhs_three = coarsen(trim(rhs_two_x, 2, 0) - applied)

    height = rhs_three.shape[0]
    column = spread_gather(jnp.stack([rhs_three] + coef_three, 1))
    weights_three = make_weights(pad_rows(column[:, 1]), column[:, 2], column[:, 3], 0.0625, 0)
    rhs_three_x = column[:, 0]
    coarse_part = first_sweep(weights_three, rhs_three_x, 0)
    for _ in range(COARSE_SWEEPS - 1):
        coarse_part = sweep(weights_three, pad_rows(coarse_part), 1, rhs_three_x, 0, masked=False)
    coarse_part = lax.dynamic_slice_in_dim(coarse_part, lax.axis_index("alt") * height, height, 0)

    correction = correction + refine(coarse_part)
    correction = alt_extend(correction, SWEEPS)
    for halo in range(SWEEPS, 0, -1):
        correction = sweep(weights_two, correction, halo, rhs_two_x, 2)

    density = density + refine(correction)
    for _ in range(SWEEPS):
        density = sweep(weights_one, alt_extend(density, 1), 1, source_x, 1)
    applied, centre = apply_op(weights_one, alt_extend(density, 1), 1)
    scaled_residual = (wide_source - applied) / weights_one[0][6]
    keep = slice(halo_r, halo_r + length)
    return (centre[..., keep], scaled_residual[..., keep])


def solution(mesh):
    spec = P("alt", None, "raan")
    return jax.shard_map(
        shards, mesh=mesh, in_specs=(spec,) * 4, out_specs=(spec, spec), check_vma=False
    )
```

```python
import jax
import jax.numpy as jnp
from jax import lax
from jax.sharding import PartitionSpec as P

SWEEPS = 2
COARSE_SWEEPS = 4
OMEGA = 0.75
RAAN_HALO = 32
HIGH = lax.Precision.HIGHEST


def pairing(fine):
    rows = lax.broadcasted_iota(jnp.int32, (fine, fine // 2), 0) // 2
    cols = lax.broadcasted_iota(jnp.int32, (fine, fine // 2), 1)
    return (rows == cols).astype(jnp.float32)


def coarsen(values):
    depth, width, length = values.shape
    summed = values.reshape(depth // 2, 2, width, length).sum(axis=1)
    summed = jnp.matmul(summed, pairing(length), precision=HIGH)
    summed = jnp.matmul(pairing(width).T[None], summed, precision=HIGH)
    return summed * 0.125


def refine(values):
    depth, width, length = values.shape
    grown = jnp.matmul(values, pairing(2 * length).T, precision=HIGH)
    grown = jnp.matmul(pairing(2 * width)[None], grown, precision=HIGH)
    grown = jnp.broadcast_to(grown[:, None], (depth, 2, 2 * width, 2 * length))
    return grown.reshape(2 * depth, 2 * width, 2 * length)


def raan_extend(values, halo):
    count, length = lax.axis_size("raan"), values.shape[-1]
    up = [(i, (i + 1) % count) for i in range(count)]
    down = [(j, i) for i, j in up]
    before = lax.ppermute(values[..., length - halo:], "raan", up)
    after = lax.ppermute(values[..., :halo], "raan", down)
    return jnp.concatenate([before, values, after], axis=-1)


def alt_extend(values, halo):
    count, depth = lax.axis_size("alt"), values.shape[0]
    below, above = [], []
    for distance in range(1, -(-halo // depth) + 1):
        low = max(0, distance * depth - halo)
        high = min(depth, halo - (distance - 1) * depth)
        up = [(i, i + distance) for i in range(count) if i + distance < count]
        down = [(i, i - distance) for i in range(count) if i - distance >= 0]
        below.insert(0, lax.ppermute(values[low:], "alt", up))
        above.append(lax.ppermute(values[:high], "alt", down))
    return jnp.concatenate(below + [values] + above, axis=0)


def spread_gather(values):
    count = lax.axis_size("alt")
    copies = jnp.broadcast_to(values[None], (count,) + values.shape)
    every = lax.all_to_all(copies, "alt", 0, 0)
    return every.reshape((count * values.shape[0],) + values.shape[1:])


def trim(values, have, want):
    cut = have - want
    return values[cut:values.shape[0] - cut] if cut else values


def lane_shifts(values):
    zero = jnp.zeros_like(values[..., :1])
    left = jnp.concatenate([zero, values[..., :-1]], axis=-1)
    right = jnp.concatenate([values[..., 1:], zero], axis=-1)
    return left, right


def make_weights(coef_alt, coef_inc, coef_raan, factor, halo):
    centre = coef_alt[1:-1]
    w_alt_lo = factor * 0.5 * (centre + coef_alt[:-2])
    w_alt_hi = factor * 0.5 * (centre + coef_alt[2:])
    inner_faces = factor * 0.5 * (coef_inc[:, :-1] + coef_inc[:, 1:])
    zero_inc = jnp.zeros_like(coef_inc[:, :1])
    w_inc_lo = jnp.concatenate([zero_inc, inner_faces], 1)
    w_inc_hi = jnp.concatenate([inner_faces, zero_inc], 1)
    raan_left, raan_right = lane_shifts(coef_raan)
    w_raan_lo = factor * 0.5 * (coef_raan + raan_left)
    w_raan_hi = factor * 0.5 * (coef_raan + raan_right)
    diagonal = 1.0 + (w_alt_lo + w_alt_hi + w_inc_lo + w_inc_hi + w_raan_lo + w_raan_hi)
    return (w_alt_lo, w_alt_hi, w_inc_lo, w_inc_hi, w_raan_lo, w_raan_hi, diagonal), halo


def apply_op(weights, field, halo):
    parts, have = weights
    w_alt_lo, w_alt_hi, w_inc_lo, w_inc_hi, w_raan_lo, w_raan_hi, diagonal = (
        trim(part, have, halo - 1) for part in parts
    )
    centre = field[1:-1]
    v_down, v_up = field[:-2], field[2:]
    zero_inc = jnp.zeros_like(centre[:, :1])
    v_prev = jnp.concatenate([zero_inc, centre[:, :-1]], 1)
    v_next = jnp.concatenate([centre[:, 1:], zero_inc], 1)
    v_left, v_right = lane_shifts(centre)
    beside = (
        w_alt_lo * v_down
        + w_alt_hi * v_up
        + w_inc_lo * v_prev
        + w_inc_hi * v_next
        + w_raan_lo * v_left
        + w_raan_hi * v_right
    )
    return diagonal * centre - beside, centre


def inside(shape, halo):
    depth = shape[0] - 2 * halo
    rows = lax.broadcasted_iota(jnp.int32, shape, 0) + lax.axis_index("alt") * depth - halo
    return (rows >= 0) & (rows < depth * lax.axis_size("alt"))


def sweep(weights, field, halo, target, target_halo, masked=True):
    applied, centre = apply_op(weights, field, halo)
    diagonal = trim(weights[0][6], weights[1], halo - 1)
    updated = centre + OMEGA * (trim(target, target_halo, halo - 1) - applied) / diagonal
    if not masked:
        return updated
    return jnp.where(inside(updated.shape, halo - 1), updated, 0.0)


def pad_rows(values):
    zero = jnp.zeros_like(values[:1])
    return jnp.concatenate([zero, values, zero], axis=0)


def first_sweep(weights, target, halo):
    diagonal = trim(weights[0][6], weights[1], halo)
    return OMEGA * target / diagonal


def shards(source, k_alt, k_inc, k_raan):
    length = source.shape[-1]
    halo_r = min(RAAN_HALO, length)
    wide = raan_extend(jnp.stack([source, k_alt, k_inc, k_raan], axis=1), halo_r)
    wide_source, wide_alt, wide_inc, wide_raan = (wide[:, i] for i in range(4))
    coef_two = [coarsen(part) for part in (wide_alt, wide_inc, wide_raan)]
    coef_three = [coarsen(part) for part in coef_two]

    first = alt_extend(wide[:, 0:2], 1)
    source_x = first[:, 0]
    weights_one = make_weights(first[:, 1], wide_inc, wide_raan, 1.0, 0)

    density = sweep(weights_one, source_x, 1, source_x, 1)
    density = sweep(weights_one, alt_extend(density, 1), 1, source_x, 1)
    applied, density = apply_op(weights_one, alt_extend(density, 1), 1)
    rhs_two = coarsen(wide_source - applied)

    level_two = alt_extend(jnp.stack([rhs_two] + coef_two, 1), SWEEPS + 2)
    weights_two = make_weights(
        level_two[:, 1],
        trim(level_two[:, 2], SWEEPS + 2, SWEEPS + 1),
        trim(level_two[:, 3], SWEEPS + 2, SWEEPS + 1),
        0.25,
        SWEEPS + 1,
    )
    rhs_two_x = trim(level_two[:, 0], SWEEPS + 2, SWEEPS + 1)
    correction = first_sweep(weights_two, rhs_two_x, SWEEPS + 1)
    correction = sweep(weights_two, correction, SWEEPS + 1, rhs_two_x, SWEEPS + 1)
    applied, _ = apply_op(weights_two, trim(correction, SWEEPS, 1), 1)
    rhs_three = coarsen(trim(rhs_two_x, SWEEPS + 1, 0) - applied)

    height = rhs_three.shape[0]
    column = spread_gather(jnp.stack([rhs_three] + coef_three, 1))
    weights_three = make_weights(pad_rows(column[:, 1]), column[:, 2], column[:, 3], 0.0625, 0)
    rhs_three_x = column[:, 0]
    coarse_part = first_sweep(weights_three, rhs_three_x, 0)
    for _ in range(COARSE_SWEEPS - 1):
        coarse_part = sweep(weights_three, pad_rows(coarse_part), 1, rhs_three_x, 0, masked=False)
    reach = SWEEPS // 2
    coarse_part = jnp.pad(coarse_part, ((reach, reach), (0, 0), (0, 0)))
    coarse_part = lax.dynamic_slice_in_dim(coarse_part, lax.axis_index("alt") * height, height + 2 * reach, 0)

    correction = correction + refine(coarse_part)
    for halo in range(SWEEPS, 0, -1):
        correction = sweep(weights_two, correction, halo, rhs_two_x, SWEEPS + 1)

    density = density + refine(correction)
    for _ in range(SWEEPS):
        density = sweep(weights_one, alt_extend(density, 1), 1, source_x, 1)
    applied, centre = apply_op(weights_one, alt_extend(density, 1), 1)
    scaled_residual = (wide_source - applied) / weights_one[0][6]
    keep = slice(halo_r, halo_r + length)
    return (centre[..., keep], scaled_residual[..., keep])


def solution(mesh):
    spec = P("alt", None, "raan")
    return jax.shard_map(
        shards, mesh=mesh, in_specs=(spec,) * 4, out_specs=(spec, spec), check_vma=False
    )
```

```python
import jax
import jax.numpy as jnp
from jax import lax
from jax.sharding import PartitionSpec as P

SWEEPS = 2
COARSE_SWEEPS = 4
OMEGA = 0.75
RAAN_HALO = 32
HIGH = lax.Precision.HIGHEST


def pairing(fine):
    rows = lax.broadcasted_iota(jnp.int32, (fine, fine // 2), 0) // 2
    cols = lax.broadcasted_iota(jnp.int32, (fine, fine // 2), 1)
    return (rows == cols).astype(jnp.float32)


def coarsen(values):
    depth, width, length = values.shape
    summed = values.reshape(depth // 2, 2, width, length).sum(axis=1)
    summed = jnp.matmul(summed, pairing(length), precision=HIGH)
    summed = jnp.matmul(pairing(width).T[None], summed, precision=HIGH)
    return summed * 0.125


def refine(values):
    depth, width, length = values.shape
    grown = jnp.matmul(values, pairing(2 * length).T, precision=HIGH)
    grown = jnp.matmul(pairing(2 * width)[None], grown, precision=HIGH)
    grown = jnp.broadcast_to(grown[:, None], (depth, 2, 2 * width, 2 * length))
    return grown.reshape(2 * depth, 2 * width, 2 * length)


def raan_extend(values, halo):
    count, length = lax.axis_size("raan"), values.shape[-1]
    up = [(i, (i + 1) % count) for i in range(count)]
    down = [(j, i) for i, j in up]
    before = lax.ppermute(values[..., length - halo:], "raan", up)
    after = lax.ppermute(values[..., :halo], "raan", down)
    return jnp.concatenate([before, values, after], axis=-1)


def alt_extend(values, halo):
    count, depth = lax.axis_size("alt"), values.shape[0]
    below, above = [], []
    for distance in range(1, -(-halo // depth) + 1):
        low = max(0, distance * depth - halo)
        high = min(depth, halo - (distance - 1) * depth)
        up = [(i, i + distance) for i in range(count) if i + distance < count]
        down = [(i, i - distance) for i in range(count) if i - distance >= 0]
        below.insert(0, lax.ppermute(values[low:], "alt", up))
        above.append(lax.ppermute(values[:high], "alt", down))
    return jnp.concatenate(below + [values] + above, axis=0)


def spread_gather(values):
    count = lax.axis_size("alt")
    copies = jnp.broadcast_to(values[None], (count,) + values.shape)
    every = lax.all_to_all(copies, "alt", 0, 0)
    return every.reshape((count * values.shape[0],) + values.shape[1:])


def trim(values, have, want):
    cut = have - want
    return values[cut:values.shape[0] - cut] if cut else values


def lane_shifts(values):
    zero = jnp.zeros_like(values[..., :1])
    left = jnp.concatenate([zero, values[..., :-1]], axis=-1)
    right = jnp.concatenate([values[..., 1:], zero], axis=-1)
    return left, right


def make_weights(coef_alt, coef_inc, coef_raan, factor, halo):
    centre = coef_alt[1:-1]
    w_alt_lo = factor * 0.5 * (centre + coef_alt[:-2])
    w_alt_hi = factor * 0.5 * (centre + coef_alt[2:])
    inner_faces = factor * 0.5 * (coef_inc[:, :-1] + coef_inc[:, 1:])
    zero_inc = jnp.zeros_like(coef_inc[:, :1])
    w_inc_lo = jnp.concatenate([zero_inc, inner_faces], 1)
    w_inc_hi = jnp.concatenate([inner_faces, zero_inc], 1)
    raan_left, raan_right = lane_shifts(coef_raan)
    w_raan_lo = factor * 0.5 * (coef_raan + raan_left)
    w_raan_hi = factor * 0.5 * (coef_raan + raan_right)
    diagonal = 1.0 + (w_alt_lo + w_alt_hi + w_inc_lo + w_inc_hi + w_raan_lo + w_raan_hi)
    return (w_alt_lo, w_alt_hi, w_inc_lo, w_inc_hi, w_raan_lo, w_raan_hi, diagonal), halo


def apply_op(weights, field, halo):
    parts, have = weights
    w_alt_lo, w_alt_hi, w_inc_lo, w_inc_hi, w_raan_lo, w_raan_hi, diagonal = (
        trim(part, have, halo - 1) for part in parts
    )
    centre = field[1:-1]
    v_down, v_up = field[:-2], field[2:]
    zero_inc = jnp.zeros_like(centre[:, :1])
    v_prev = jnp.concatenate([zero_inc, centre[:, :-1]], 1)
    v_next = jnp.concatenate([centre[:, 1:], zero_inc], 1)
    v_left, v_right = lane_shifts(centre)
    beside = (
        w_alt_lo * v_down
        + w_alt_hi * v_up
        + w_inc_lo * v_prev
        + w_inc_hi * v_next
        + w_raan_lo * v_left
        + w_raan_hi * v_right
    )
    return diagonal * centre - beside, centre


def inside(shape, halo):
    depth = shape[0] - 2 * halo
    rows = lax.broadcasted_iota(jnp.int32, shape, 0) + lax.axis_index("alt") * depth - halo
    return (rows >= 0) & (rows < depth * lax.axis_size("alt"))


def sweep(weights, field, halo, target, target_halo, masked=True):
    applied, centre = apply_op(weights, field, halo)
    diagonal = trim(weights[0][6], weights[1], halo - 1)
    updated = centre + OMEGA * (trim(target, target_halo, halo - 1) - applied) / diagonal
    if not masked:
        return updated
    return jnp.where(inside(updated.shape, halo - 1), updated, 0.0)


def pad_rows(values):
    zero = jnp.zeros_like(values[:1])
    return jnp.concatenate([zero, values, zero], axis=0)


def split_sweep(weights, field, target, target_halo):
    parts, have = weights
    depth = field.shape[0] - 2
    cuts = [0, 1, depth - 1, depth] if depth >= 3 else [0, depth]
    rows = []
    for low, high in zip(cuts[:-1], cuts[1:]):
        w_alt_lo, w_alt_hi, w_inc_lo, w_inc_hi, w_raan_lo, w_raan_hi, diagonal = (
            trim(part, have, 0)[low:high] for part in parts
        )
        centre = field[low + 1:high + 1]
        v_down, v_up = field[low:high], field[low + 2:high + 2]
        zero_inc = jnp.zeros_like(centre[:, :1])
        v_prev = jnp.concatenate([zero_inc, centre[:, :-1]], 1)
        v_next = jnp.concatenate([centre[:, 1:], zero_inc], 1)
        v_left, v_right = lane_shifts(centre)
        beside = (
            w_alt_lo * v_down
            + w_alt_hi * v_up
            + w_inc_lo * v_prev
            + w_inc_hi * v_next
            + w_raan_lo * v_left
            + w_raan_hi * v_right
        )
        applied = diagonal * centre - beside
        aim = trim(target, target_halo, 0)[low:high]
        rows.append(centre + OMEGA * (aim - applied) / diagonal)
    return jnp.concatenate(rows, axis=0)


def first_sweep(weights, target, halo):
    diagonal = trim(weights[0][6], weights[1], halo)
    return OMEGA * target / diagonal


def shards(source, k_alt, k_inc, k_raan):
    length = source.shape[-1]
    halo_r = min(RAAN_HALO, length)
    wide = raan_extend(jnp.stack([source, k_alt, k_inc, k_raan], axis=1), halo_r)
    wide_source, wide_alt, wide_inc, wide_raan = (wide[:, i] for i in range(4))
    coef_two = [coarsen(part) for part in (wide_alt, wide_inc, wide_raan)]
    coef_three = [coarsen(part) for part in coef_two]

    first = alt_extend(wide[:, 0:2], 1)
    source_x = first[:, 0]
    weights_one = make_weights(first[:, 1], wide_inc, wide_raan, 1.0, 0)

    density = split_sweep(weights_one, source_x, source_x, 1)
    density = split_sweep(weights_one, alt_extend(density, 1), source_x, 1)
    applied, density = apply_op(weights_one, alt_extend(density, 1), 1)
    rhs_two = coarsen(wide_source - applied)

    level_two = alt_extend(jnp.stack([rhs_two] + coef_two, 1), SWEEPS + 2)
    weights_two = make_weights(
        level_two[:, 1],
        trim(level_two[:, 2], SWEEPS + 2, SWEEPS + 1),
        trim(level_two[:, 3], SWEEPS + 2, SWEEPS + 1),
        0.25,
        SWEEPS + 1,
    )
    rhs_two_x = trim(level_two[:, 0], SWEEPS + 2, SWEEPS + 1)
    correction = first_sweep(weights_two, rhs_two_x, SWEEPS + 1)
    correction = sweep(weights_two, correction, SWEEPS + 1, rhs_two_x, SWEEPS + 1)
    applied, _ = apply_op(weights_two, trim(correction, SWEEPS, 1), 1)
    rhs_three = coarsen(trim(rhs_two_x, SWEEPS + 1, 0) - applied)

    height = rhs_three.shape[0]
    column = spread_gather(jnp.stack([rhs_three] + coef_three, 1))
    weights_three = make_weights(pad_rows(column[:, 1]), column[:, 2], column[:, 3], 0.0625, 0)
    rhs_three_x = column[:, 0]
    coarse_part = first_sweep(weights_three, rhs_three_x, 0)
    for _ in range(COARSE_SWEEPS - 1):
        coarse_part = sweep(weights_three, pad_rows(coarse_part), 1, rhs_three_x, 0, masked=False)
    reach = SWEEPS // 2
    coarse_part = jnp.pad(coarse_part, ((reach, reach), (0, 0), (0, 0)))
    coarse_part = lax.dynamic_slice_in_dim(coarse_part, lax.axis_index("alt") * height, height + 2 * reach, 0)

    correction = correction + refine(coarse_part)
    for halo in range(SWEEPS, 0, -1):
        correction = sweep(weights_two, correction, halo, rhs_two_x, SWEEPS + 1)

    density = density + refine(correction)
    for _ in range(SWEEPS):
        density = split_sweep(weights_one, alt_extend(density, 1), source_x, 1)
    applied, centre = apply_op(weights_one, alt_extend(density, 1), 1)
    scaled_residual = (wide_source - applied) / weights_one[0][6]
    keep = slice(halo_r, halo_r + length)
    return (centre[..., keep], scaled_residual[..., keep])


def solution(mesh):
    spec = P("alt", None, "raan")
    return jax.shard_map(
        shards, mesh=mesh, in_specs=(spec,) * 4, out_specs=(spec, spec), check_vma=False
    )
```

```python
import jax
import jax.numpy as jnp
from jax import lax
from jax.sharding import PartitionSpec as P

SWEEPS = 2
COARSE_SWEEPS = 4
OMEGA = 0.75
RAAN_HALO = 32
HIGH = lax.Precision.HIGHEST


def pairing(fine):
    rows = lax.broadcasted_iota(jnp.int32, (fine, fine // 2), 0) // 2
    cols = lax.broadcasted_iota(jnp.int32, (fine, fine // 2), 1)
    return (rows == cols).astype(jnp.float32)


def coarsen(values):
    depth, width, length = values.shape
    summed = values.reshape(depth // 2, 2, width, length).sum(axis=1)
    summed = jnp.matmul(summed, pairing(length), precision=HIGH)
    summed = jnp.matmul(pairing(width).T[None], summed, precision=HIGH)
    return summed * 0.125


def refine(values):
    depth, width, length = values.shape
    grown = jnp.matmul(values, pairing(2 * length).T, precision=HIGH)
    grown = jnp.matmul(pairing(2 * width)[None], grown, precision=HIGH)
    grown = jnp.broadcast_to(grown[:, None], (depth, 2, 2 * width, 2 * length))
    return grown.reshape(2 * depth, 2 * width, 2 * length)


def raan_extend(values, halo):
    count, length = lax.axis_size("raan"), values.shape[-1]
    up = [(i, (i + 1) % count) for i in range(count)]
    down = [(j, i) for i, j in up]
    before = lax.ppermute(values[..., length - halo:], "raan", up)
    after = lax.ppermute(values[..., :halo], "raan", down)
    return jnp.concatenate([before, values, after], axis=-1)


def alt_extend(values, halo):
    count, depth = lax.axis_size("alt"), values.shape[0]
    below, above = [], []
    for distance in range(1, -(-halo // depth) + 1):
        low = max(0, distance * depth - halo)
        high = min(depth, halo - (distance - 1) * depth)
        up = [(i, i + distance) for i in range(count) if i + distance < count]
        down = [(i, i - distance) for i in range(count) if i - distance >= 0]
        below.insert(0, lax.ppermute(values[low:], "alt", up))
        above.append(lax.ppermute(values[:high], "alt", down))
    return jnp.concatenate(below + [values] + above, axis=0)


def spread_gather(values):
    count = lax.axis_size("alt")
    copies = jnp.broadcast_to(values[None], (count,) + values.shape)
    every = lax.all_to_all(copies, "alt", 0, 0)
    return every.reshape((count * values.shape[0],) + values.shape[1:])


def trim(values, have, want):
    cut = have - want
    return values[cut:values.shape[0] - cut] if cut else values


def lane_shifts(values):
    zero = jnp.zeros_like(values[..., :1])
    left = jnp.concatenate([zero, values[..., :-1]], axis=-1)
    right = jnp.concatenate([values[..., 1:], zero], axis=-1)
    return left, right


def make_weights(coef_alt, coef_inc, coef_raan, factor, halo):
    centre = coef_alt[1:-1]
    w_alt_lo = factor * 0.5 * (centre + coef_alt[:-2])
    w_alt_hi = factor * 0.5 * (centre + coef_alt[2:])
    inner_faces = factor * 0.5 * (coef_inc[:, :-1] + coef_inc[:, 1:])
    zero_inc = jnp.zeros_like(coef_inc[:, :1])
    w_inc_lo = jnp.concatenate([zero_inc, inner_faces], 1)
    w_inc_hi = jnp.concatenate([inner_faces, zero_inc], 1)
    raan_left, raan_right = lane_shifts(coef_raan)
    w_raan_lo = factor * 0.5 * (coef_raan + raan_left)
    w_raan_hi = factor * 0.5 * (coef_raan + raan_right)
    diagonal = 1.0 + (w_alt_lo + w_alt_hi + w_inc_lo + w_inc_hi + w_raan_lo + w_raan_hi)
    return (w_alt_lo, w_alt_hi, w_inc_lo, w_inc_hi, w_raan_lo, w_raan_hi, diagonal), halo


def apply_op(weights, field, halo):
    parts, have = weights
    w_alt_lo, w_alt_hi, w_inc_lo, w_inc_hi, w_raan_lo, w_raan_hi, diagonal = (
        trim(part, have, halo - 1) for part in parts
    )
    centre = field[1:-1]
    v_down, v_up = field[:-2], field[2:]
    zero_inc = jnp.zeros_like(centre[:, :1])
    v_prev = jnp.concatenate([zero_inc, centre[:, :-1]], 1)
    v_next = jnp.concatenate([centre[:, 1:], zero_inc], 1)
    v_left, v_right = lane_shifts(centre)
    beside = (
        w_alt_lo * v_down
        + w_alt_hi * v_up
        + w_inc_lo * v_prev
        + w_inc_hi * v_next
        + w_raan_lo * v_left
        + w_raan_hi * v_right
    )
    return diagonal * centre - beside, centre


def inside(shape, halo):
    depth = shape[0] - 2 * halo
    rows = lax.broadcasted_iota(jnp.int32, shape, 0) + lax.axis_index("alt") * depth - halo
    return (rows >= 0) & (rows < depth * lax.axis_size("alt"))


def sweep(weights, field, halo, target, target_halo, masked=True):
    applied, centre = apply_op(weights, field, halo)
    diagonal = trim(weights[0][6], weights[1], halo - 1)
    updated = centre + OMEGA * (trim(target, target_halo, halo - 1) - applied) / diagonal
    if not masked:
        return updated
    return jnp.where(inside(updated.shape, halo - 1), updated, 0.0)


def pad_rows(values):
    zero = jnp.zeros_like(values[:1])
    return jnp.concatenate([zero, values, zero], axis=0)


def split_sweep(weights, field, target, target_halo):
    parts, have = weights
    depth = field.shape[0] - 2
    cuts = [0, 1, depth - 1, depth] if depth >= 3 else [0, depth]
    rows = []
    for low, high in zip(cuts[:-1], cuts[1:]):
        w_alt_lo, w_alt_hi, w_inc_lo, w_inc_hi, w_raan_lo, w_raan_hi, diagonal = (
            trim(part, have, 0)[low:high] for part in parts
        )
        centre = field[low + 1:high + 1]
        v_down, v_up = field[low:high], field[low + 2:high + 2]
        zero_inc = jnp.zeros_like(centre[:, :1])
        v_prev = jnp.concatenate([zero_inc, centre[:, :-1]], 1)
        v_next = jnp.concatenate([centre[:, 1:], zero_inc], 1)
        v_left, v_right = lane_shifts(centre)
        beside = (
            w_alt_lo * v_down
            + w_alt_hi * v_up
            + w_inc_lo * v_prev
            + w_inc_hi * v_next
            + w_raan_lo * v_left
            + w_raan_hi * v_right
        )
        applied = diagonal * centre - beside
        aim = trim(target, target_halo, 0)[low:high]
        rows.append(centre + OMEGA * (aim - applied) / diagonal)
    return jnp.concatenate(rows, axis=0)


def first_sweep(weights, target, halo):
    diagonal = trim(weights[0][6], weights[1], halo)
    return OMEGA * target / diagonal


def shards(source, k_alt, k_inc, k_raan):
    length = source.shape[-1]
    halo_r = min(RAAN_HALO, length)
    wide = raan_extend(jnp.stack([source, k_alt, k_inc, k_raan], axis=1), halo_r)
    wide_source, wide_alt, wide_inc, wide_raan = (wide[:, i] for i in range(4))
    coef_column = spread_gather(jnp.stack([coarsen(part) for part in (wide_alt, wide_inc, wide_raan)], 1))

    first = alt_extend(wide[:, 0:2], 1)
    source_x = first[:, 0]
    weights_one = make_weights(first[:, 1], wide_inc, wide_raan, 1.0, 0)

    density = split_sweep(weights_one, source_x, source_x, 1)
    density = split_sweep(weights_one, alt_extend(density, 1), source_x, 1)
    applied, density = apply_op(weights_one, alt_extend(density, 1), 1)
    rhs_two = coarsen(wide_source - applied)

    height = rhs_two.shape[0]
    rhs_two_x = spread_gather(rhs_two)
    weights_two = make_weights(pad_rows(coef_column[:, 0]), coef_column[:, 1], coef_column[:, 2], 0.25, 0)
    correction = first_sweep(weights_two, rhs_two_x, 0)
    for _ in range(SWEEPS - 1):
        correction = sweep(weights_two, pad_rows(correction), 1, rhs_two_x, 0, masked=False)
    applied, _ = apply_op(weights_two, pad_rows(correction), 1)
    rhs_three_x = coarsen(rhs_two_x - applied)

    coef_three = [coarsen(coef_column[:, i]) for i in range(3)]
    weights_three = make_weights(pad_rows(coef_three[0]), coef_three[1], coef_three[2], 0.0625, 0)
    coarse_part = first_sweep(weights_three, rhs_three_x, 0)
    for _ in range(COARSE_SWEEPS - 1):
        coarse_part = sweep(weights_three, pad_rows(coarse_part), 1, rhs_three_x, 0, masked=False)

    correction = correction + refine(coarse_part)
    for _ in range(SWEEPS):
        correction = sweep(weights_two, pad_rows(correction), 1, rhs_two_x, 0, masked=False)
    correction = lax.dynamic_slice_in_dim(correction, lax.axis_index("alt") * height, height, 0)

    density = density + refine(correction)
    for _ in range(SWEEPS):
        density = split_sweep(weights_one, alt_extend(density, 1), source_x, 1)
    applied, centre = apply_op(weights_one, alt_extend(density, 1), 1)
    scaled_residual = (wide_source - applied) / weights_one[0][6]
    keep = slice(halo_r, halo_r + length)
    return (centre[..., keep], scaled_residual[..., keep])


def solution(mesh):
    spec = P("alt", None, "raan")
    return jax.shard_map(
        shards, mesh=mesh, in_specs=(spec,) * 4, out_specs=(spec, spec), check_vma=False
    )
```

```python
import jax
import jax.numpy as jnp
from jax import lax
from jax.sharding import PartitionSpec as P

SWEEPS = 2
COARSE_SWEEPS = 4
OMEGA = 0.75
RAAN_HALO = 32
HIGH = lax.Precision.HIGHEST


def pairing(fine):
    rows = lax.broadcasted_iota(jnp.int32, (fine, fine // 2), 0) // 2
    cols = lax.broadcasted_iota(jnp.int32, (fine, fine // 2), 1)
    return (rows == cols).astype(jnp.float32)


def coarsen(values):
    depth, width, length = values.shape
    summed = values.reshape(depth // 2, 2, width, length).sum(axis=1)
    summed = jnp.matmul(summed, pairing(length), precision=HIGH)
    summed = jnp.matmul(pairing(width).T[None], summed, precision=HIGH)
    return summed * 0.125


def refine(values):
    depth, width, length = values.shape
    grown = jnp.matmul(values, pairing(2 * length).T, precision=HIGH)
    grown = jnp.matmul(pairing(2 * width)[None], grown, precision=HIGH)
    grown = jnp.broadcast_to(grown[:, None], (depth, 2, 2 * width, 2 * length))
    return grown.reshape(2 * depth, 2 * width, 2 * length)


def raan_extend(values, halo):
    count, length = lax.axis_size("raan"), values.shape[-1]
    up = [(i, (i + 1) % count) for i in range(count)]
    down = [(j, i) for i, j in up]
    edge = values[..., :halo].shape
    dense = edge[:-2] + (edge[-2] * halo // 128, 128) if edge[-2] * halo % 128 == 0 else edge
    before = lax.ppermute(values[..., length - halo:].reshape(dense), "raan", up).reshape(edge)
    after = lax.ppermute(values[..., :halo].reshape(dense), "raan", down).reshape(edge)
    return jnp.concatenate([before, values, after], axis=-1)


def alt_extend(values, halo):
    count, depth = lax.axis_size("alt"), values.shape[0]
    below, above = [], []
    for distance in range(1, -(-halo // depth) + 1):
        low = max(0, distance * depth - halo)
        high = min(depth, halo - (distance - 1) * depth)
        up = [(i, i + distance) for i in range(count) if i + distance < count]
        down = [(i, i - distance) for i in range(count) if i - distance >= 0]
        below.insert(0, lax.ppermute(values[low:], "alt", up))
        above.append(lax.ppermute(values[:high], "alt", down))
    return jnp.concatenate(below + [values] + above, axis=0)


def spread_gather(values):
    count = lax.axis_size("alt")
    copies = jnp.broadcast_to(values[None], (count,) + values.shape)
    every = lax.all_to_all(copies, "alt", 0, 0)
    return every.reshape((count * values.shape[0],) + values.shape[1:])


def trim(values, have, want):
    cut = have - want
    return values[cut:values.shape[0] - cut] if cut else values


def lane_shifts(values):
    zero = jnp.zeros_like(values[..., :1])
    left = jnp.concatenate([zero, values[..., :-1]], axis=-1)
    right = jnp.concatenate([values[..., 1:], zero], axis=-1)
    return left, right


def make_weights(coef_alt, coef_inc, coef_raan, factor, halo):
    centre = coef_alt[1:-1]
    w_alt_lo = factor * 0.5 * (centre + coef_alt[:-2])
    w_alt_hi = factor * 0.5 * (centre + coef_alt[2:])
    inner_faces = factor * 0.5 * (coef_inc[:, :-1] + coef_inc[:, 1:])
    zero_inc = jnp.zeros_like(coef_inc[:, :1])
    w_inc_lo = jnp.concatenate([zero_inc, inner_faces], 1)
    w_inc_hi = jnp.concatenate([inner_faces, zero_inc], 1)
    raan_left, raan_right = lane_shifts(coef_raan)
    w_raan_lo = factor * 0.5 * (coef_raan + raan_left)
    w_raan_hi = factor * 0.5 * (coef_raan + raan_right)
    diagonal = 1.0 + (w_alt_lo + w_alt_hi + w_inc_lo + w_inc_hi + w_raan_lo + w_raan_hi)
    return (w_alt_lo, w_alt_hi, w_inc_lo, w_inc_hi, w_raan_lo, w_raan_hi, diagonal), halo


def apply_op(weights, field, halo):
    parts, have = weights
    w_alt_lo, w_alt_hi, w_inc_lo, w_inc_hi, w_raan_lo, w_raan_hi, diagonal = (
        trim(part, have, halo - 1) for part in parts
    )
    centre = field[1:-1]
    v_down, v_up = field[:-2], field[2:]
    zero_inc = jnp.zeros_like(centre[:, :1])
    v_prev = jnp.concatenate([zero_inc, centre[:, :-1]], 1)
    v_next = jnp.concatenate([centre[:, 1:], zero_inc], 1)
    v_left, v_right = lane_shifts(centre)
    beside = (
        w_alt_lo * v_down
        + w_alt_hi * v_up
        + w_inc_lo * v_prev
        + w_inc_hi * v_next
        + w_raan_lo * v_left
        + w_raan_hi * v_right
    )
    return diagonal * centre - beside, centre


def inside(shape, halo):
    depth = shape[0] - 2 * halo
    rows = lax.broadcasted_iota(jnp.int32, shape, 0) + lax.axis_index("alt") * depth - halo
    return (rows >= 0) & (rows < depth * lax.axis_size("alt"))


def sweep(weights, field, halo, target, target_halo, masked=True):
    applied, centre = apply_op(weights, field, halo)
    diagonal = trim(weights[0][6], weights[1], halo - 1)
    updated = centre + OMEGA * (trim(target, target_halo, halo - 1) - applied) / diagonal
    if not masked:
        return updated
    return jnp.where(inside(updated.shape, halo - 1), updated, 0.0)


def pad_rows(values):
    zero = jnp.zeros_like(values[:1])
    return jnp.concatenate([zero, values, zero], axis=0)


def split_sweep(weights, field, target, target_halo):
    parts, have = weights
    depth = field.shape[0] - 2
    cuts = [0, 1, depth - 1, depth] if depth >= 3 else [0, depth]
    rows = []
    for low, high in zip(cuts[:-1], cuts[1:]):
        w_alt_lo, w_alt_hi, w_inc_lo, w_inc_hi, w_raan_lo, w_raan_hi, diagonal = (
            trim(part, have, 0)[low:high] for part in parts
        )
        centre = field[low + 1:high + 1]
        v_down, v_up = field[low:high], field[low + 2:high + 2]
        zero_inc = jnp.zeros_like(centre[:, :1])
        v_prev = jnp.concatenate([zero_inc, centre[:, :-1]], 1)
        v_next = jnp.concatenate([centre[:, 1:], zero_inc], 1)
        v_left, v_right = lane_shifts(centre)
        beside = (
            w_alt_lo * v_down
            + w_alt_hi * v_up
            + w_inc_lo * v_prev
            + w_inc_hi * v_next
            + w_raan_lo * v_left
            + w_raan_hi * v_right
        )
        applied = diagonal * centre - beside
        aim = trim(target, target_halo, 0)[low:high]
        rows.append(centre + OMEGA * (aim - applied) / diagonal)
    return jnp.concatenate(rows, axis=0)


def first_sweep(weights, target, halo):
    diagonal = trim(weights[0][6], weights[1], halo)
    return OMEGA * target / diagonal


def shards(source, k_alt, k_inc, k_raan):
    length = source.shape[-1]
    halo_r = min(RAAN_HALO, length)
    wide = raan_extend(jnp.stack([source, k_alt, k_inc, k_raan], axis=1), halo_r)
    wide_source, wide_alt, wide_inc, wide_raan = (wide[:, i] for i in range(4))
    coef_two = [coarsen(part) for part in (wide_alt, wide_inc, wide_raan)]
    coef_three = [coarsen(part) for part in coef_two]

    first = alt_extend(wide[:, 0:2], 1)
    source_x = first[:, 0]
    weights_one = make_weights(first[:, 1], wide_inc, wide_raan, 1.0, 0)

    density = split_sweep(weights_one, source_x, source_x, 1)
    density = split_sweep(weights_one, alt_extend(density, 1), source_x, 1)
    applied, density = apply_op(weights_one, alt_extend(density, 1), 1)
    rhs_two = coarsen(wide_source - applied)

    level_two = alt_extend(jnp.stack([rhs_two] + coef_two, 1), SWEEPS + 2)
    weights_two = make_weights(
        level_two[:, 1],
        trim(level_two[:, 2], SWEEPS + 2, SWEEPS + 1),
        trim(level_two[:, 3], SWEEPS + 2, SWEEPS + 1),
        0.25,
        SWEEPS + 1,
    )
    rhs_two_x = trim(level_two[:, 0], SWEEPS + 2, SWEEPS + 1)
    correction = first_sweep(weights_two, rhs_two_x, SWEEPS + 1)
    correction = sweep(weights_two, correction, SWEEPS + 1, rhs_two_x, SWEEPS + 1)
    applied, _ = apply_op(weights_two, trim(correction, SWEEPS, 1), 1)
    rhs_three = coarsen(trim(rhs_two_x, SWEEPS + 1, 0) - applied)

    height = rhs_three.shape[0]
    column = spread_gather(jnp.stack([rhs_three] + coef_three, 1))
    weights_three = make_weights(pad_rows(column[:, 1]), column[:, 2], column[:, 3], 0.0625, 0)
    rhs_three_x = column[:, 0]
    coarse_part = first_sweep(weights_three, rhs_three_x, 0)
    for _ in range(COARSE_SWEEPS - 1):
        coarse_part = sweep(weights_three, pad_rows(coarse_part), 1, rhs_three_x, 0, masked=False)
    reach = SWEEPS // 2
    coarse_part = jnp.pad(coarse_part, ((reach, reach), (0, 0), (0, 0)))
    coarse_part = lax.dynamic_slice_in_dim(coarse_part, lax.axis_index("alt") * height, height + 2 * reach, 0)

    correction = correction + refine(coarse_part)
    for halo in range(SWEEPS, 0, -1):
        correction = sweep(weights_two, correction, halo, rhs_two_x, SWEEPS + 1)

    density = density + refine(correction)
    for _ in range(SWEEPS):
        density = split_sweep(weights_one, alt_extend(density, 1), source_x, 1)
    applied, centre = apply_op(weights_one, alt_extend(density, 1), 1)
    scaled_residual = (wide_source - applied) / weights_one[0][6]
    keep = slice(halo_r, halo_r + length)
    return (centre[..., keep], scaled_residual[..., keep])


def solution(mesh):
    spec = P("alt", None, "raan")
    return jax.shard_map(
        shards, mesh=mesh, in_specs=(spec,) * 4, out_specs=(spec, spec), check_vma=False
    )
```

```python
import jax
import jax.numpy as jnp
from jax import lax
from jax.sharding import PartitionSpec as P

SWEEPS = 2
COARSE_SWEEPS = 4
OMEGA = 0.75
RAAN_HALO = 32
HIGH = lax.Precision.HIGHEST


def pairing(fine):
    rows = lax.broadcasted_iota(jnp.int32, (fine, fine // 2), 0) // 2
    cols = lax.broadcasted_iota(jnp.int32, (fine, fine // 2), 1)
    return (rows == cols).astype(jnp.float32)


def coarsen(values):
    depth, width, length = values.shape
    summed = values.reshape(depth // 2, 2, width, length).sum(axis=1)
    summed = jnp.matmul(summed, pairing(length), precision=HIGH)
    summed = jnp.matmul(pairing(width).T[None], summed, precision=HIGH)
    return summed * 0.125


def refine(values):
    depth, width, length = values.shape
    grown = jnp.matmul(values, pairing(2 * length).T, precision=HIGH)
    grown = jnp.matmul(pairing(2 * width)[None], grown, precision=HIGH)
    grown = jnp.broadcast_to(grown[:, None], (depth, 2, 2 * width, 2 * length))
    return grown.reshape(2 * depth, 2 * width, 2 * length)


def raan_extend(values, halo):
    count, length = lax.axis_size("raan"), values.shape[-1]
    up = [(i, (i + 1) % count) for i in range(count)]
    down = [(j, i) for i, j in up]
    edge = values[..., :halo].shape
    dense = edge[:-2] + (edge[-2] * halo // 128, 128) if edge[-2] * halo % 128 == 0 else edge
    before = lax.ppermute(values[..., length - halo:].reshape(dense), "raan", up).reshape(edge)
    after = lax.ppermute(values[..., :halo].reshape(dense), "raan", down).reshape(edge)
    return jnp.concatenate([before, values, after], axis=-1)


def packed(values):
    lanes, inner = values.shape[-1], values[0].size
    padded = -(-lanes // 128) * 128
    if lanes % 128 and 4 * (padded - lanes) >= padded and inner % 1024 == 0:
        return values.reshape(values.shape[0], inner // 128, 128)
    return values


def send(values, axis, route):
    return lax.ppermute(packed(values), axis, route).reshape(values.shape)


def alt_extend(values, halo):
    count, depth = lax.axis_size("alt"), values.shape[0]
    below, above = [], []
    for distance in range(1, -(-halo // depth) + 1):
        low = max(0, distance * depth - halo)
        high = min(depth, halo - (distance - 1) * depth)
        up = [(i, i + distance) for i in range(count) if i + distance < count]
        down = [(i, i - distance) for i in range(count) if i - distance >= 0]
        below.insert(0, send(values[low:], "alt", up))
        above.append(send(values[:high], "alt", down))
    return jnp.concatenate(below + [values] + above, axis=0)


def spread_gather(values):
    count = lax.axis_size("alt")
    dense = packed(values)
    copies = jnp.broadcast_to(dense[None], (count,) + dense.shape)
    every = lax.all_to_all(copies, "alt", 0, 0)
    return every.reshape((count * values.shape[0],) + values.shape[1:])


def trim(values, have, want):
    cut = have - want
    return values[cut:values.shape[0] - cut] if cut else values


def lane_shifts(values):
    zero = jnp.zeros_like(values[..., :1])
    left = jnp.concatenate([zero, values[..., :-1]], axis=-1)
    right = jnp.concatenate([values[..., 1:], zero], axis=-1)
    return left, right


def make_weights(coef_alt, coef_inc, coef_raan, factor, halo):
    centre = coef_alt[1:-1]
    w_alt_lo = factor * 0.5 * (centre + coef_alt[:-2])
    w_alt_hi = factor * 0.5 * (centre + coef_alt[2:])
    inner_faces = factor * 0.5 * (coef_inc[:, :-1] + coef_inc[:, 1:])
    zero_inc = jnp.zeros_like(coef_inc[:, :1])
    w_inc_lo = jnp.concatenate([zero_inc, inner_faces], 1)
    w_inc_hi = jnp.concatenate([inner_faces, zero_inc], 1)
    raan_left, raan_right = lane_shifts(coef_raan)
    w_raan_lo = factor * 0.5 * (coef_raan + raan_left)
    w_raan_hi = factor * 0.5 * (coef_raan + raan_right)
    diagonal = 1.0 + (w_alt_lo + w_alt_hi + w_inc_lo + w_inc_hi + w_raan_lo + w_raan_hi)
    return (w_alt_lo, w_alt_hi, w_inc_lo, w_inc_hi, w_raan_lo, w_raan_hi, diagonal), halo


def apply_op(weights, field, halo):
    parts, have = weights
    w_alt_lo, w_alt_hi, w_inc_lo, w_inc_hi, w_raan_lo, w_raan_hi, diagonal = (
        trim(part, have, halo - 1) for part in parts
    )
    centre = field[1:-1]
    v_down, v_up = field[:-2], field[2:]
    zero_inc = jnp.zeros_like(centre[:, :1])
    v_prev = jnp.concatenate([zero_inc, centre[:, :-1]], 1)
    v_next = jnp.concatenate([centre[:, 1:], zero_inc], 1)
    v_left, v_right = lane_shifts(centre)
    beside = (
        w_alt_lo * v_down
        + w_alt_hi * v_up
        + w_inc_lo * v_prev
        + w_inc_hi * v_next
        + w_raan_lo * v_left
        + w_raan_hi * v_right
    )
    return diagonal * centre - beside, centre


def inside(shape, halo):
    depth = shape[0] - 2 * halo
    rows = lax.broadcasted_iota(jnp.int32, shape, 0) + lax.axis_index("alt") * depth - halo
    return (rows >= 0) & (rows < depth * lax.axis_size("alt"))


def sweep(weights, field, halo, target, target_halo, masked=True):
    applied, centre = apply_op(weights, field, halo)
    diagonal = trim(weights[0][6], weights[1], halo - 1)
    updated = centre + OMEGA * (trim(target, target_halo, halo - 1) - applied) / diagonal
    if not masked:
        return updated
    return jnp.where(inside(updated.shape, halo - 1), updated, 0.0)


def pad_rows(values):
    zero = jnp.zeros_like(values[:1])
    return jnp.concatenate([zero, values, zero], axis=0)


def split_sweep(weights, field, target, target_halo):
    parts, have = weights
    depth = field.shape[0] - 2
    cuts = [0, 1, depth - 1, depth] if depth >= 3 else [0, depth]
    rows = []
    for low, high in zip(cuts[:-1], cuts[1:]):
        w_alt_lo, w_alt_hi, w_inc_lo, w_inc_hi, w_raan_lo, w_raan_hi, diagonal = (
            trim(part, have, 0)[low:high] for part in parts
        )
        centre = field[low + 1:high + 1]
        v_down, v_up = field[low:high], field[low + 2:high + 2]
        zero_inc = jnp.zeros_like(centre[:, :1])
        v_prev = jnp.concatenate([zero_inc, centre[:, :-1]], 1)
        v_next = jnp.concatenate([centre[:, 1:], zero_inc], 1)
        v_left, v_right = lane_shifts(centre)
        beside = (
            w_alt_lo * v_down
            + w_alt_hi * v_up
            + w_inc_lo * v_prev
            + w_inc_hi * v_next
            + w_raan_lo * v_left
            + w_raan_hi * v_right
        )
        applied = diagonal * centre - beside
        aim = trim(target, target_halo, 0)[low:high]
        rows.append(centre + OMEGA * (aim - applied) / diagonal)
    return jnp.concatenate(rows, axis=0)


def first_sweep(weights, target, halo):
    diagonal = trim(weights[0][6], weights[1], halo)
    return OMEGA * target / diagonal


def shards(source, k_alt, k_inc, k_raan):
    length = source.shape[-1]
    halo_r = min(RAAN_HALO, length)
    wide = raan_extend(jnp.stack([source, k_alt, k_inc, k_raan], axis=1), halo_r)
    wide_source, wide_alt, wide_inc, wide_raan = (wide[:, i] for i in range(4))
    coef_two = [coarsen(part) for part in (wide_alt, wide_inc, wide_raan)]
    coef_three = [coarsen(part) for part in coef_two]

    first = alt_extend(wide[:, 0:2], 1)
    source_x = first[:, 0]
    weights_one = make_weights(first[:, 1], wide_inc, wide_raan, 1.0, 0)

    density = split_sweep(weights_one, source_x, source_x, 1)
    density = split_sweep(weights_one, alt_extend(density, 1), source_x, 1)
    applied, density = apply_op(weights_one, alt_extend(density, 1), 1)
    rhs_two = coarsen(wide_source - applied)

    level_two = alt_extend(jnp.stack([rhs_two] + coef_two, 1), SWEEPS + 2)
    weights_two = make_weights(
        level_two[:, 1],
        trim(level_two[:, 2], SWEEPS + 2, SWEEPS + 1),
        trim(level_two[:, 3], SWEEPS + 2, SWEEPS + 1),
        0.25,
        SWEEPS + 1,
    )
    rhs_two_x = trim(level_two[:, 0], SWEEPS + 2, SWEEPS + 1)
    correction = first_sweep(weights_two, rhs_two_x, SWEEPS + 1)
    correction = sweep(weights_two, correction, SWEEPS + 1, rhs_two_x, SWEEPS + 1)
    applied, _ = apply_op(weights_two, trim(correction, SWEEPS, 1), 1)
    rhs_three = coarsen(trim(rhs_two_x, SWEEPS + 1, 0) - applied)

    height = rhs_three.shape[0]
    column = spread_gather(jnp.stack([rhs_three] + coef_three, 1))
    weights_three = make_weights(pad_rows(column[:, 1]), column[:, 2], column[:, 3], 0.0625, 0)
    rhs_three_x = column[:, 0]
    coarse_part = first_sweep(weights_three, rhs_three_x, 0)
    for _ in range(COARSE_SWEEPS - 1):
        coarse_part = sweep(weights_three, pad_rows(coarse_part), 1, rhs_three_x, 0, masked=False)
    reach = SWEEPS // 2
    coarse_part = jnp.pad(coarse_part, ((reach, reach), (0, 0), (0, 0)))
    coarse_part = lax.dynamic_slice_in_dim(coarse_part, lax.axis_index("alt") * height, height + 2 * reach, 0)

    correction = correction + refine(coarse_part)
    for halo in range(SWEEPS, 0, -1):
        correction = sweep(weights_two, correction, halo, rhs_two_x, SWEEPS + 1)

    density = density + refine(correction)
    for _ in range(SWEEPS):
        density = split_sweep(weights_one, alt_extend(density, 1), source_x, 1)
    applied, centre = apply_op(weights_one, alt_extend(density, 1), 1)
    scaled_residual = (wide_source - applied) / weights_one[0][6]
    keep = slice(halo_r, halo_r + length)
    return (centre[..., keep], scaled_residual[..., keep])


def solution(mesh):
    spec = P("alt", None, "raan")
    return jax.shard_map(
        shards, mesh=mesh, in_specs=(spec,) * 4, out_specs=(spec, spec), check_vma=False
    )
```

```python
import jax
import jax.numpy as jnp
from jax import lax
from jax.sharding import PartitionSpec as P

SWEEPS = 2
COARSE_SWEEPS = 4
OMEGA = 0.75
RAAN_HALO = 32
HIGH = lax.Precision.HIGHEST


def pairing(fine):
    rows = lax.broadcasted_iota(jnp.int32, (fine, fine // 2), 0) // 2
    cols = lax.broadcasted_iota(jnp.int32, (fine, fine // 2), 1)
    return (rows == cols).astype(jnp.float32)


def coarsen(values):
    depth, width, length = values.shape
    summed = values.reshape(depth // 2, 2, width, length).sum(axis=1)
    summed = jnp.matmul(summed, pairing(length), precision=HIGH)
    summed = jnp.matmul(pairing(width).T[None], summed, precision=HIGH)
    return summed * 0.125


def refine(values):
    depth, width, length = values.shape
    grown = jnp.matmul(values, pairing(2 * length).T, precision=HIGH)
    grown = jnp.matmul(pairing(2 * width)[None], grown, precision=HIGH)
    grown = jnp.broadcast_to(grown[:, None], (depth, 2, 2 * width, 2 * length))
    return grown.reshape(2 * depth, 2 * width, 2 * length)


def raan_extend(values, halo):
    count, length = lax.axis_size("raan"), values.shape[-1]
    up = [(i, (i + 1) % count) for i in range(count)]
    down = [(j, i) for i, j in up]
    edge = values[..., :halo].shape
    dense = edge[:-2] + (edge[-2] * halo // 128, 128) if edge[-2] * halo % 128 == 0 else edge
    before = lax.ppermute(values[..., length - halo:].reshape(dense), "raan", up).reshape(edge)
    after = lax.ppermute(values[..., :halo].reshape(dense), "raan", down).reshape(edge)
    return jnp.concatenate([before, values, after], axis=-1)


def alt_extend(values, halo):
    count, depth = lax.axis_size("alt"), values.shape[0]
    below, above = [], []
    for distance in range(1, -(-halo // depth) + 1):
        low = max(0, distance * depth - halo)
        high = min(depth, halo - (distance - 1) * depth)
        up = [(i, i + distance) for i in range(count) if i + distance < count]
        down = [(i, i - distance) for i in range(count) if i - distance >= 0]
        below.insert(0, lax.ppermute(values[low:], "alt", up))
        above.append(lax.ppermute(values[:high], "alt", down))
    return jnp.concatenate(below + [values] + above, axis=0)


def spread_gather(values):
    count = lax.axis_size("alt")
    copies = jnp.broadcast_to(values[None], (count,) + values.shape)
    every = lax.all_to_all(copies, "alt", 0, 0)
    return every.reshape((count * values.shape[0],) + values.shape[1:])


def trim(values, have, want):
    cut = have - want
    return values[cut:values.shape[0] - cut] if cut else values


def lane_shifts(values):
    zero = jnp.zeros_like(values[..., :1])
    left = jnp.concatenate([zero, values[..., :-1]], axis=-1)
    right = jnp.concatenate([values[..., 1:], zero], axis=-1)
    return left, right


def make_weights(coef_alt, coef_inc, coef_raan, factor, halo):
    centre = coef_alt[1:-1]
    w_alt_lo = factor * 0.5 * (centre + coef_alt[:-2])
    w_alt_hi = factor * 0.5 * (centre + coef_alt[2:])
    inner_faces = factor * 0.5 * (coef_inc[:, :-1] + coef_inc[:, 1:])
    zero_inc = jnp.zeros_like(coef_inc[:, :1])
    w_inc_lo = jnp.concatenate([zero_inc, inner_faces], 1)
    w_inc_hi = jnp.concatenate([inner_faces, zero_inc], 1)
    raan_left, raan_right = lane_shifts(coef_raan)
    w_raan_lo = factor * 0.5 * (coef_raan + raan_left)
    w_raan_hi = factor * 0.5 * (coef_raan + raan_right)
    diagonal = 1.0 + (w_alt_lo + w_alt_hi + w_inc_lo + w_inc_hi + w_raan_lo + w_raan_hi)
    return (w_alt_lo, w_alt_hi, w_inc_lo, w_inc_hi, w_raan_lo, w_raan_hi, diagonal), halo


def apply_op(weights, field, halo):
    parts, have = weights
    w_alt_lo, w_alt_hi, w_inc_lo, w_inc_hi, w_raan_lo, w_raan_hi, diagonal = (
        trim(part, have, halo - 1) for part in parts
    )
    centre = field[1:-1]
    v_down, v_up = field[:-2], field[2:]
    zero_inc = jnp.zeros_like(centre[:, :1])
    v_prev = jnp.concatenate([zero_inc, centre[:, :-1]], 1)
    v_next = jnp.concatenate([centre[:, 1:], zero_inc], 1)
    v_left, v_right = lane_shifts(centre)
    beside = (
        w_alt_lo * v_down
        + w_alt_hi * v_up
        + w_inc_lo * v_prev
        + w_inc_hi * v_next
        + w_raan_lo * v_left
        + w_raan_hi * v_right
    )
    return diagonal * centre - beside, centre


def inside(shape, halo):
    depth = shape[0] - 2 * halo
    rows = lax.broadcasted_iota(jnp.int32, shape, 0) + lax.axis_index("alt") * depth - halo
    return (rows >= 0) & (rows < depth * lax.axis_size("alt"))


def sweep(weights, field, halo, target, target_halo, masked=True):
    applied, centre = apply_op(weights, field, halo)
    diagonal = trim(weights[0][6], weights[1], halo - 1)
    updated = centre + OMEGA * (trim(target, target_halo, halo - 1) - applied) / diagonal
    if not masked:
        return updated
    return jnp.where(inside(updated.shape, halo - 1), updated, 0.0)


def pad_rows(values):
    zero = jnp.zeros_like(values[:1])
    return jnp.concatenate([zero, values, zero], axis=0)


def split_sweep(weights, field, target, target_halo):
    parts, have = weights
    depth = field.shape[0] - 2
    cuts = [0, 1, depth - 1, depth] if depth >= 3 else [0, depth]
    rows = []
    for low, high in zip(cuts[:-1], cuts[1:]):
        w_alt_lo, w_alt_hi, w_inc_lo, w_inc_hi, w_raan_lo, w_raan_hi, diagonal = (
            trim(part, have, 0)[low:high] for part in parts
        )
        centre = field[low + 1:high + 1]
        v_down, v_up = field[low:high], field[low + 2:high + 2]
        zero_inc = jnp.zeros_like(centre[:, :1])
        v_prev = jnp.concatenate([zero_inc, centre[:, :-1]], 1)
        v_next = jnp.concatenate([centre[:, 1:], zero_inc], 1)
        v_left, v_right = lane_shifts(centre)
        beside = (
            w_alt_lo * v_down
            + w_alt_hi * v_up
            + w_inc_lo * v_prev
            + w_inc_hi * v_next
            + w_raan_lo * v_left
            + w_raan_hi * v_right
        )
        applied = diagonal * centre - beside
        aim = trim(target, target_halo, 0)[low:high]
        rows.append(centre + OMEGA * (aim - applied) / diagonal)
    return jnp.concatenate(rows, axis=0)


def first_sweep(weights, target, halo):
    diagonal = trim(weights[0][6], weights[1], halo)
    return OMEGA * target / diagonal


def shards(source, k_alt, k_inc, k_raan):
    length = source.shape[-1]
    halo_r = min(RAAN_HALO, length)
    wide = raan_extend(jnp.stack([source, k_alt, k_inc, k_raan], axis=1), halo_r)
    wide_source, wide_alt, wide_inc, wide_raan = (wide[:, i] for i in range(4))
    coef_two = [coarsen(part) for part in (wide_alt, wide_inc, wide_raan)]
    coef_three = [coarsen(part) for part in coef_two]

    coef_two_x = alt_extend(jnp.stack(coef_two, 1), SWEEPS + 2)
    weights_two = make_weights(
        coef_two_x[:, 0],
        trim(coef_two_x[:, 1], SWEEPS + 2, SWEEPS + 1),
        trim(coef_two_x[:, 2], SWEEPS + 2, SWEEPS + 1),
        0.25,
        SWEEPS + 1,
    )

    first = alt_extend(wide[:, 0:2], 1)
    source_x = first[:, 0]
    weights_one = make_weights(first[:, 1], wide_inc, wide_raan, 1.0, 0)

    density = split_sweep(weights_one, source_x, source_x, 1)
    density = split_sweep(weights_one, alt_extend(density, 1), source_x, 1)
    applied, density = apply_op(weights_one, alt_extend(density, 1), 1)
    rhs_two = coarsen(wide_source - applied)

    rhs_two_x = alt_extend(rhs_two, SWEEPS + 1)
    correction = first_sweep(weights_two, rhs_two_x, SWEEPS + 1)
    correction = sweep(weights_two, correction, SWEEPS + 1, rhs_two_x, SWEEPS + 1)
    applied, _ = apply_op(weights_two, trim(correction, SWEEPS, 1), 1)
    rhs_three = coarsen(trim(rhs_two_x, SWEEPS + 1, 0) - applied)

    height = rhs_three.shape[0]
    column = spread_gather(jnp.stack([rhs_three] + coef_three, 1))
    weights_three = make_weights(pad_rows(column[:, 1]), column[:, 2], column[:, 3], 0.0625, 0)
    rhs_three_x = column[:, 0]
    coarse_part = first_sweep(weights_three, rhs_three_x, 0)
    for _ in range(COARSE_SWEEPS - 1):
        coarse_part = sweep(weights_three, pad_rows(coarse_part), 1, rhs_three_x, 0, masked=False)
    reach = SWEEPS // 2
    coarse_part = jnp.pad(coarse_part, ((reach, reach), (0, 0), (0, 0)))
    coarse_part = lax.dynamic_slice_in_dim(coarse_part, lax.axis_index("alt") * height, height + 2 * reach, 0)

    correction = correction + refine(coarse_part)
    for halo in range(SWEEPS, 0, -1):
        correction = sweep(weights_two, correction, halo, rhs_two_x, SWEEPS + 1)

    density = density + refine(correction)
    for _ in range(SWEEPS):
        density = split_sweep(weights_one, alt_extend(density, 1), source_x, 1)
    applied, centre = apply_op(weights_one, alt_extend(density, 1), 1)
    scaled_residual = (wide_source - applied) / weights_one[0][6]
    keep = slice(halo_r, halo_r + length)
    return (centre[..., keep], scaled_residual[..., keep])


def solution(mesh):
    spec = P("alt", None, "raan")
    return jax.shard_map(
        shards, mesh=mesh, in_specs=(spec,) * 4, out_specs=(spec, spec), check_vma=False
    )
```

```python
import jax
import jax.numpy as jnp
from jax import lax
from jax.sharding import PartitionSpec as P

SWEEPS = 2
COARSE_SWEEPS = 4
OMEGA = 0.75
RAAN_HALO = 32
HIGH = lax.Precision.HIGHEST


def pairing(fine):
    rows = lax.broadcasted_iota(jnp.int32, (fine, fine // 2), 0) // 2
    cols = lax.broadcasted_iota(jnp.int32, (fine, fine // 2), 1)
    return (rows == cols).astype(jnp.float32)


def coarsen(values):
    depth, width, length = values.shape
    summed = values.reshape(depth // 2, 2, width, length).sum(axis=1)
    summed = jnp.matmul(summed, pairing(length), precision=HIGH)
    summed = jnp.matmul(pairing(width).T[None], summed, precision=HIGH)
    return summed * 0.125


def refine(values):
    depth, width, length = values.shape
    grown = jnp.matmul(values, pairing(2 * length).T, precision=HIGH)
    grown = jnp.matmul(pairing(2 * width)[None], grown, precision=HIGH)
    grown = jnp.broadcast_to(grown[:, None], (depth, 2, 2 * width, 2 * length))
    return grown.reshape(2 * depth, 2 * width, 2 * length)


def raan_extend(values, halo):
    count, length = lax.axis_size("raan"), values.shape[-1]
    up = [(i, (i + 1) % count) for i in range(count)]
    down = [(j, i) for i, j in up]
    edge = values[..., :halo].shape
    dense = edge[:-2] + (edge[-2] * halo // 128, 128) if edge[-2] * halo % 128 == 0 else edge
    before = lax.ppermute(values[..., length - halo:].reshape(dense), "raan", up).reshape(edge)
    after = lax.ppermute(values[..., :halo].reshape(dense), "raan", down).reshape(edge)
    return jnp.concatenate([before, values, after], axis=-1)


def alt_extend(values, halo):
    count, depth = lax.axis_size("alt"), values.shape[0]
    below, above = [], []
    for distance in range(1, -(-halo // depth) + 1):
        low = max(0, distance * depth - halo)
        high = min(depth, halo - (distance - 1) * depth)
        up = [(i, i + distance) for i in range(count) if i + distance < count]
        down = [(i, i - distance) for i in range(count) if i - distance >= 0]
        below.insert(0, lax.ppermute(values[low:], "alt", up))
        above.append(lax.ppermute(values[:high], "alt", down))
    return jnp.concatenate(below + [values] + above, axis=0)


def spread_gather(values):
    count = lax.axis_size("alt")
    copies = jnp.broadcast_to(values[None], (count,) + values.shape)
    every = lax.all_to_all(copies, "alt", 0, 0)
    return every.reshape((count * values.shape[0],) + values.shape[1:])


def trim(values, have, want):
    cut = have - want
    return values[cut:values.shape[0] - cut] if cut else values


def lane_shifts(values):
    zero = jnp.zeros_like(values[..., :1])
    left = jnp.concatenate([zero, values[..., :-1]], axis=-1)
    right = jnp.concatenate([values[..., 1:], zero], axis=-1)
    return left, right


def make_weights(coef_alt, coef_inc, coef_raan, factor, halo):
    centre = coef_alt[1:-1]
    w_alt_lo = factor * 0.5 * (centre + coef_alt[:-2])
    w_alt_hi = factor * 0.5 * (centre + coef_alt[2:])
    inner_faces = factor * 0.5 * (coef_inc[:, :-1] + coef_inc[:, 1:])
    zero_inc = jnp.zeros_like(coef_inc[:, :1])
    w_inc_lo = jnp.concatenate([zero_inc, inner_faces], 1)
    w_inc_hi = jnp.concatenate([inner_faces, zero_inc], 1)
    raan_left, raan_right = lane_shifts(coef_raan)
    w_raan_lo = factor * 0.5 * (coef_raan + raan_left)
    w_raan_hi = factor * 0.5 * (coef_raan + raan_right)
    diagonal = 1.0 + (w_alt_lo + w_alt_hi + w_inc_lo + w_inc_hi + w_raan_lo + w_raan_hi)
    return (w_alt_lo, w_alt_hi, w_inc_lo, w_inc_hi, w_raan_lo, w_raan_hi, diagonal), halo


def apply_op(weights, field, halo):
    parts, have = weights
    w_alt_lo, w_alt_hi, w_inc_lo, w_inc_hi, w_raan_lo, w_raan_hi, diagonal = (
        trim(part, have, halo - 1) for part in parts
    )
    centre = field[1:-1]
    v_down, v_up = field[:-2], field[2:]
    zero_inc = jnp.zeros_like(centre[:, :1])
    v_prev = jnp.concatenate([zero_inc, centre[:, :-1]], 1)
    v_next = jnp.concatenate([centre[:, 1:], zero_inc], 1)
    v_left, v_right = lane_shifts(centre)
    beside = (
        w_alt_lo * v_down
        + w_alt_hi * v_up
        + w_inc_lo * v_prev
        + w_inc_hi * v_next
        + w_raan_lo * v_left
        + w_raan_hi * v_right
    )
    return diagonal * centre - beside, centre


def inside(shape, halo):
    depth = shape[0] - 2 * halo
    rows = lax.broadcasted_iota(jnp.int32, shape, 0) + lax.axis_index("alt") * depth - halo
    return (rows >= 0) & (rows < depth * lax.axis_size("alt"))


def sweep(weights, field, halo, target, target_halo, masked=True):
    applied, centre = apply_op(weights, field, halo)
    diagonal = trim(weights[0][6], weights[1], halo - 1)
    updated = centre + OMEGA * (trim(target, target_halo, halo - 1) - applied) / diagonal
    if not masked:
        return updated
    return jnp.where(inside(updated.shape, halo - 1), updated, 0.0)


def pad_rows(values):
    zero = jnp.zeros_like(values[:1])
    return jnp.concatenate([zero, values, zero], axis=0)


def split_sweep(weights, field, target, target_halo):
    parts, have = weights
    depth = field.shape[0] - 2
    cuts = [0, 1, depth - 1, depth] if depth >= 3 else [0, depth]
    rows = []
    for low, high in zip(cuts[:-1], cuts[1:]):
        w_alt_lo, w_alt_hi, w_inc_lo, w_inc_hi, w_raan_lo, w_raan_hi, diagonal = (
            trim(part, have, 0)[low:high] for part in parts
        )
        centre = field[low + 1:high + 1]
        v_down, v_up = field[low:high], field[low + 2:high + 2]
        zero_inc = jnp.zeros_like(centre[:, :1])
        v_prev = jnp.concatenate([zero_inc, centre[:, :-1]], 1)
        v_next = jnp.concatenate([centre[:, 1:], zero_inc], 1)
        v_left, v_right = lane_shifts(centre)
        beside = (
            w_alt_lo * v_down
            + w_alt_hi * v_up
            + w_inc_lo * v_prev
            + w_inc_hi * v_next
            + w_raan_lo * v_left
            + w_raan_hi * v_right
        )
        applied = diagonal * centre - beside
        aim = trim(target, target_halo, 0)[low:high]
        rows.append(centre + OMEGA * (aim - applied) / diagonal)
    return jnp.concatenate(rows, axis=0)


def first_sweep(weights, target, halo):
    diagonal = trim(weights[0][6], weights[1], halo)
    return OMEGA * target / diagonal


def shards(source, k_alt, k_inc, k_raan):
    length = source.shape[-1]
    halo_r = min(RAAN_HALO, length)
    wide = raan_extend(jnp.stack([source, k_alt, k_inc, k_raan], axis=1), halo_r)
    wide_source, wide_alt, wide_inc, wide_raan = (wide[:, i] for i in range(4))
    coef_two = [coarsen(part) for part in (wide_alt, wide_inc, wide_raan)]
    coef_three = [coarsen(part) for part in coef_two]

    first = alt_extend(wide[:, 0:2], 2)
    rest = alt_extend(wide[:, 2:4], 1)
    source_x = first[:, 0]
    weights_one = make_weights(first[:, 1], rest[:, 0], rest[:, 1], 1.0, 1)

    density = sweep(weights_one, source_x, 2, source_x, 2)
    density = split_sweep(weights_one, density, source_x, 2)
    applied, density = apply_op(weights_one, alt_extend(density, 1), 1)
    rhs_two = coarsen(wide_source - applied)

    level_two = alt_extend(jnp.stack([rhs_two] + coef_two, 1), SWEEPS + 2)
    weights_two = make_weights(
        level_two[:, 1],
        trim(level_two[:, 2], SWEEPS + 2, SWEEPS + 1),
        trim(level_two[:, 3], SWEEPS + 2, SWEEPS + 1),
        0.25,
        SWEEPS + 1,
    )
    rhs_two_x = trim(level_two[:, 0], SWEEPS + 2, SWEEPS + 1)
    correction = first_sweep(weights_two, rhs_two_x, SWEEPS + 1)
    correction = sweep(weights_two, correction, SWEEPS + 1, rhs_two_x, SWEEPS + 1)
    applied, _ = apply_op(weights_two, trim(correction, SWEEPS, 1), 1)
    rhs_three = coarsen(trim(rhs_two_x, SWEEPS + 1, 0) - applied)

    height = rhs_three.shape[0]
    column = spread_gather(jnp.stack([rhs_three] + coef_three, 1))
    weights_three = make_weights(pad_rows(column[:, 1]), column[:, 2], column[:, 3], 0.0625, 0)
    rhs_three_x = column[:, 0]
    coarse_part = first_sweep(weights_three, rhs_three_x, 0)
    for _ in range(COARSE_SWEEPS - 1):
        coarse_part = sweep(weights_three, pad_rows(coarse_part), 1, rhs_three_x, 0, masked=False)
    reach = SWEEPS // 2
    coarse_part = jnp.pad(coarse_part, ((reach, reach), (0, 0), (0, 0)))
    coarse_part = lax.dynamic_slice_in_dim(coarse_part, lax.axis_index("alt") * height, height + 2 * reach, 0)

    correction = correction + refine(coarse_part)
    for halo in range(SWEEPS, 0, -1):
        correction = sweep(weights_two, correction, halo, rhs_two_x, SWEEPS + 1)

    density = alt_extend(density + refine(correction), 2)
    density = sweep(weights_one, density, 2, source_x, 2)
    density = split_sweep(weights_one, density, source_x, 2)
    applied, centre = apply_op(weights_one, alt_extend(density, 1), 1)
    scaled_residual = (wide_source - applied) / trim(weights_one[0][6], weights_one[1], 0)
    keep = slice(halo_r, halo_r + length)
    return (centre[..., keep], scaled_residual[..., keep])


def solution(mesh):
    spec = P("alt", None, "raan")
    return jax.shard_map(
        shards, mesh=mesh, in_specs=(spec,) * 4, out_specs=(spec, spec), check_vma=False
    )
```

```python
import jax
import jax.numpy as jnp
from jax import lax
from jax.sharding import PartitionSpec as P

SWEEPS = 2
COARSE_SWEEPS = 4
OMEGA = 0.75
RAAN_HALO = 32
HIGH = lax.Precision.HIGHEST


def pairing(fine):
    rows = lax.broadcasted_iota(jnp.int32, (fine, fine // 2), 0) // 2
    cols = lax.broadcasted_iota(jnp.int32, (fine, fine // 2), 1)
    return (rows == cols).astype(jnp.float32)


def coarsen(values):
    depth, width, length = values.shape
    summed = values.reshape(depth // 2, 2, width, length).sum(axis=1)
    summed = jnp.matmul(summed, pairing(length), precision=HIGH)
    summed = jnp.matmul(pairing(width).T[None], summed, precision=HIGH)
    return summed * 0.125


def refine(values):
    depth, width, length = values.shape
    grown = jnp.matmul(values, pairing(2 * length).T, precision=HIGH)
    grown = jnp.matmul(pairing(2 * width)[None], grown, precision=HIGH)
    grown = jnp.broadcast_to(grown[:, None], (depth, 2, 2 * width, 2 * length))
    return grown.reshape(2 * depth, 2 * width, 2 * length)


def raan_extend(values, halo):
    count, length = lax.axis_size("raan"), values.shape[-1]
    up = [(i, (i + 1) % count) for i in range(count)]
    down = [(j, i) for i, j in up]
    edge = values[..., :halo].shape
    dense = edge[:-2] + (edge[-2] * halo // 128, 128) if edge[-2] * halo % 128 == 0 else edge
    before = lax.ppermute(values[..., length - halo:].reshape(dense), "raan", up).reshape(edge)
    after = lax.ppermute(values[..., :halo].reshape(dense), "raan", down).reshape(edge)
    return jnp.concatenate([before, values, after], axis=-1)


def alt_extend(values, halo):
    count, depth = lax.axis_size("alt"), values.shape[0]
    below, above = [], []
    for distance in range(1, -(-halo // depth) + 1):
        low = max(0, distance * depth - halo)
        high = min(depth, halo - (distance - 1) * depth)
        up = [(i, i + distance) for i in range(count) if i + distance < count]
        down = [(i, i - distance) for i in range(count) if i - distance >= 0]
        below.insert(0, lax.ppermute(values[low:], "alt", up))
        above.append(lax.ppermute(values[:high], "alt", down))
    return jnp.concatenate(below + [values] + above, axis=0)


def spread_gather(values):
    count = lax.axis_size("alt")
    copies = jnp.broadcast_to(values[None], (count,) + values.shape)
    every = lax.all_to_all(copies, "alt", 0, 0)
    return every.reshape((count * values.shape[0],) + values.shape[1:])


def trim(values, have, want):
    cut = have - want
    return values[cut:values.shape[0] - cut] if cut else values


def lane_shifts(values):
    zero = jnp.zeros_like(values[..., :1])
    left = jnp.concatenate([zero, values[..., :-1]], axis=-1)
    right = jnp.concatenate([values[..., 1:], zero], axis=-1)
    return left, right


def make_weights(coef_alt, coef_inc, coef_raan, factor, halo):
    centre = coef_alt[1:-1]
    w_alt_lo = factor * 0.5 * (centre + coef_alt[:-2])
    w_alt_hi = factor * 0.5 * (centre + coef_alt[2:])
    inner_faces = factor * 0.5 * (coef_inc[:, :-1] + coef_inc[:, 1:])
    zero_inc = jnp.zeros_like(coef_inc[:, :1])
    w_inc_lo = jnp.concatenate([zero_inc, inner_faces], 1)
    w_inc_hi = jnp.concatenate([inner_faces, zero_inc], 1)
    raan_left, raan_right = lane_shifts(coef_raan)
    w_raan_lo = factor * 0.5 * (coef_raan + raan_left)
    w_raan_hi = factor * 0.5 * (coef_raan + raan_right)
    diagonal = 1.0 + (w_alt_lo + w_alt_hi + w_inc_lo + w_inc_hi + w_raan_lo + w_raan_hi)
    return (w_alt_lo, w_alt_hi, w_inc_lo, w_inc_hi, w_raan_lo, w_raan_hi, diagonal), halo


def apply_op(weights, field, halo):
    parts, have = weights
    w_alt_lo, w_alt_hi, w_inc_lo, w_inc_hi, w_raan_lo, w_raan_hi, diagonal = (
        trim(part, have, halo - 1) for part in parts
    )
    centre = field[1:-1]
    v_down, v_up = field[:-2], field[2:]
    zero_inc = jnp.zeros_like(centre[:, :1])
    v_prev = jnp.concatenate([zero_inc, centre[:, :-1]], 1)
    v_next = jnp.concatenate([centre[:, 1:], zero_inc], 1)
    v_left, v_right = lane_shifts(centre)
    beside = (
        w_alt_lo * v_down
        + w_alt_hi * v_up
        + w_inc_lo * v_prev
        + w_inc_hi * v_next
        + w_raan_lo * v_left
        + w_raan_hi * v_right
    )
    return diagonal * centre - beside, centre


def inside(shape, halo):
    depth = shape[0] - 2 * halo
    rows = lax.broadcasted_iota(jnp.int32, shape, 0) + lax.axis_index("alt") * depth - halo
    return (rows >= 0) & (rows < depth * lax.axis_size("alt"))


def sweep(weights, field, halo, target, target_halo, masked=True):
    applied, centre = apply_op(weights, field, halo)
    diagonal = trim(weights[0][6], weights[1], halo - 1)
    updated = centre + OMEGA * (trim(target, target_halo, halo - 1) - applied) / diagonal
    if not masked:
        return updated
    return jnp.where(inside(updated.shape, halo - 1), updated, 0.0)


def pad_rows(values):
    zero = jnp.zeros_like(values[:1])
    return jnp.concatenate([zero, values, zero], axis=0)


def split_sweep(weights, field, target, target_halo):
    parts, have = weights
    depth = field.shape[0] - 2
    cuts = [0, 1, depth - 1, depth] if depth >= 3 else [0, depth]
    rows = []
    for low, high in zip(cuts[:-1], cuts[1:]):
        w_alt_lo, w_alt_hi, w_inc_lo, w_inc_hi, w_raan_lo, w_raan_hi, diagonal = (
            trim(part, have, 0)[low:high] for part in parts
        )
        centre = field[low + 1:high + 1]
        v_down, v_up = field[low:high], field[low + 2:high + 2]
        zero_inc = jnp.zeros_like(centre[:, :1])
        v_prev = jnp.concatenate([zero_inc, centre[:, :-1]], 1)
        v_next = jnp.concatenate([centre[:, 1:], zero_inc], 1)
        v_left, v_right = lane_shifts(centre)
        beside = (
            w_alt_lo * v_down
            + w_alt_hi * v_up
            + w_inc_lo * v_prev
            + w_inc_hi * v_next
            + w_raan_lo * v_left
            + w_raan_hi * v_right
        )
        applied = diagonal * centre - beside
        aim = trim(target, target_halo, 0)[low:high]
        rows.append(centre + OMEGA * (aim - applied) / diagonal)
    return jnp.concatenate(rows, axis=0)


def first_sweep(weights, target, halo):
    diagonal = trim(weights[0][6], weights[1], halo)
    return OMEGA * target / diagonal


def shards(source, k_alt, k_inc, k_raan):
    length = source.shape[-1]
    halo_r = min(RAAN_HALO, length)
    raw = jnp.stack([source, k_alt, k_inc, k_raan], axis=1)
    count = lax.axis_size("alt")
    below = lax.ppermute(raw[-1:, 0:2], "alt", [(i, i + 1) for i in range(count - 1)])
    above = lax.ppermute(raw[:1, 0:2], "alt", [(i + 1, i) for i in range(count - 1)])
    wide = raan_extend(raw, halo_r)
    edges = raan_extend(jnp.concatenate([below, above], axis=0), halo_r)
    wide_source, wide_alt, wide_inc, wide_raan = (wide[:, i] for i in range(4))
    coef_two = [coarsen(part) for part in (wide_alt, wide_inc, wide_raan)]
    coef_three = [coarsen(part) for part in coef_two]

    first = jnp.concatenate([edges[:1], wide[:, 0:2], edges[1:]], axis=0)
    source_x = first[:, 0]
    weights_one = make_weights(first[:, 1], wide_inc, wide_raan, 1.0, 0)

    density = split_sweep(weights_one, source_x, source_x, 1)
    density = split_sweep(weights_one, alt_extend(density, 1), source_x, 1)
    applied, density = apply_op(weights_one, alt_extend(density, 1), 1)
    rhs_two = coarsen(wide_source - applied)

    level_two = alt_extend(jnp.stack([rhs_two] + coef_two, 1), SWEEPS + 2)
    weights_two = make_weights(
        level_two[:, 1],
        trim(level_two[:, 2], SWEEPS + 2, SWEEPS + 1),
        trim(level_two[:, 3], SWEEPS + 2, SWEEPS + 1),
        0.25,
        SWEEPS + 1,
    )
    rhs_two_x = trim(level_two[:, 0], SWEEPS + 2, SWEEPS + 1)
    correction = first_sweep(weights_two, rhs_two_x, SWEEPS + 1)
    correction = sweep(weights_two, correction, SWEEPS + 1, rhs_two_x, SWEEPS + 1)
    applied, _ = apply_op(weights_two, trim(correction, SWEEPS, 1), 1)
    rhs_three = coarsen(trim(rhs_two_x, SWEEPS + 1, 0) - applied)

    height = rhs_three.shape[0]
    column = spread_gather(jnp.stack([rhs_three] + coef_three, 1))
    weights_three = make_weights(pad_rows(column[:, 1]), column[:, 2], column[:, 3], 0.0625, 0)
    rhs_three_x = column[:, 0]
    coarse_part = first_sweep(weights_three, rhs_three_x, 0)
    for _ in range(COARSE_SWEEPS - 1):
        coarse_part = sweep(weights_three, pad_rows(coarse_part), 1, rhs_three_x, 0, masked=False)
    reach = SWEEPS // 2
    coarse_part = jnp.pad(coarse_part, ((reach, reach), (0, 0), (0, 0)))
    coarse_part = lax.dynamic_slice_in_dim(coarse_part, lax.axis_index("alt") * height, height + 2 * reach, 0)

    correction = correction + refine(coarse_part)
    for halo in range(SWEEPS, 0, -1):
        correction = sweep(weights_two, correction, halo, rhs_two_x, SWEEPS + 1)

    density = density + refine(correction)
    for _ in range(SWEEPS):
        density = split_sweep(weights_one, alt_extend(density, 1), source_x, 1)
    applied, centre = apply_op(weights_one, alt_extend(density, 1), 1)
    scaled_residual = (wide_source - applied) / weights_one[0][6]
    keep = slice(halo_r, halo_r + length)
    return (centre[..., keep], scaled_residual[..., keep])


def solution(mesh):
    spec = P("alt", None, "raan")
    return jax.shard_map(
        shards, mesh=mesh, in_specs=(spec,) * 4, out_specs=(spec, spec), check_vma=False
    )
```

```python
import jax
import jax.numpy as jnp
from jax import lax
from jax.sharding import PartitionSpec as P

SWEEPS = 2
COARSE_SWEEPS = 4
OMEGA = 0.75
RAAN_HALO = 32
HIGH = lax.Precision.HIGHEST


def pairing(fine):
    rows = lax.broadcasted_iota(jnp.int32, (fine, fine // 2), 0) // 2
    cols = lax.broadcasted_iota(jnp.int32, (fine, fine // 2), 1)
    return (rows == cols).astype(jnp.float32)


def coarsen(values):
    depth, width, length = values.shape
    summed = values.reshape(depth // 2, 2, width, length).sum(axis=1)
    summed = jnp.matmul(summed, pairing(length), precision=HIGH)
    summed = jnp.matmul(pairing(width).T[None], summed, precision=HIGH)
    return summed * 0.125


def refine(values):
    depth, width, length = values.shape
    grown = jnp.matmul(values, pairing(2 * length).T, precision=HIGH)
    grown = jnp.matmul(pairing(2 * width)[None], grown, precision=HIGH)
    grown = jnp.broadcast_to(grown[:, None], (depth, 2, 2 * width, 2 * length))
    return grown.reshape(2 * depth, 2 * width, 2 * length)


def raan_extend(values, halo):
    count, length = lax.axis_size("raan"), values.shape[-1]
    up = [(i, (i + 1) % count) for i in range(count)]
    down = [(j, i) for i, j in up]
    edge = values[..., :halo].shape
    dense = edge[:-2] + (edge[-2] * halo // 128, 128) if edge[-2] * halo % 128 == 0 else edge
    before = lax.ppermute(values[..., length - halo:].reshape(dense), "raan", up).reshape(edge)
    after = lax.ppermute(values[..., :halo].reshape(dense), "raan", down).reshape(edge)
    return jnp.concatenate([before, values, after], axis=-1)


def alt_extend(values, halo):
    count, depth = lax.axis_size("alt"), values.shape[0]
    below, above = [], []
    for distance in range(1, -(-halo // depth) + 1):
        low = max(0, distance * depth - halo)
        high = min(depth, halo - (distance - 1) * depth)
        up = [(i, i + distance) for i in range(count) if i + distance < count]
        down = [(i, i - distance) for i in range(count) if i - distance >= 0]
        below.insert(0, lax.ppermute(values[low:], "alt", up))
        above.append(lax.ppermute(values[:high], "alt", down))
    return jnp.concatenate(below + [values] + above, axis=0)


def spread_gather(values):
    count = lax.axis_size("alt")
    copies = jnp.broadcast_to(values[None], (count,) + values.shape)
    every = lax.all_to_all(copies, "alt", 0, 0)
    return every.reshape((count * values.shape[0],) + values.shape[1:])


def trim(values, have, want):
    cut = have - want
    return values[cut:values.shape[0] - cut] if cut else values


def lane_shifts(values):
    zero = jnp.zeros_like(values[..., :1])
    left = jnp.concatenate([zero, values[..., :-1]], axis=-1)
    right = jnp.concatenate([values[..., 1:], zero], axis=-1)
    return left, right


def make_weights(coef_alt, coef_inc, coef_raan, factor, halo):
    centre = coef_alt[1:-1]
    w_alt_lo = factor * 0.5 * (centre + coef_alt[:-2])
    w_alt_hi = factor * 0.5 * (centre + coef_alt[2:])
    inner_faces = factor * 0.5 * (coef_inc[:, :-1] + coef_inc[:, 1:])
    zero_inc = jnp.zeros_like(coef_inc[:, :1])
    w_inc_lo = jnp.concatenate([zero_inc, inner_faces], 1)
    w_inc_hi = jnp.concatenate([inner_faces, zero_inc], 1)
    raan_left, raan_right = lane_shifts(coef_raan)
    w_raan_lo = factor * 0.5 * (coef_raan + raan_left)
    w_raan_hi = factor * 0.5 * (coef_raan + raan_right)
    diagonal = 1.0 + (w_alt_lo + w_alt_hi + w_inc_lo + w_inc_hi + w_raan_lo + w_raan_hi)
    return (w_alt_lo, w_alt_hi, w_inc_lo, w_inc_hi, w_raan_lo, w_raan_hi, diagonal), halo


def apply_op(weights, field, halo):
    parts, have = weights
    w_alt_lo, w_alt_hi, w_inc_lo, w_inc_hi, w_raan_lo, w_raan_hi, diagonal = (
        trim(part, have, halo - 1) for part in parts
    )
    centre = field[1:-1]
    v_down, v_up = field[:-2], field[2:]
    zero_inc = jnp.zeros_like(centre[:, :1])
    v_prev = jnp.concatenate([zero_inc, centre[:, :-1]], 1)
    v_next = jnp.concatenate([centre[:, 1:], zero_inc], 1)
    v_left, v_right = lane_shifts(centre)
    beside = (
        w_alt_lo * v_down
        + w_alt_hi * v_up
        + w_inc_lo * v_prev
        + w_inc_hi * v_next
        + w_raan_lo * v_left
        + w_raan_hi * v_right
    )
    return diagonal * centre - beside, centre


def inside(shape, halo):
    depth = shape[0] - 2 * halo
    rows = lax.broadcasted_iota(jnp.int32, shape, 0) + lax.axis_index("alt") * depth - halo
    return (rows >= 0) & (rows < depth * lax.axis_size("alt"))


def sweep(weights, field, halo, target, target_halo, masked=True):
    applied, centre = apply_op(weights, field, halo)
    diagonal = trim(weights[0][6], weights[1], halo - 1)
    updated = centre + OMEGA * (trim(target, target_halo, halo - 1) - applied) / diagonal
    if not masked:
        return updated
    return jnp.where(inside(updated.shape, halo - 1), updated, 0.0)


def pad_rows(values):
    zero = jnp.zeros_like(values[:1])
    return jnp.concatenate([zero, values, zero], axis=0)


def split_sweep(weights, field, target, target_halo):
    parts, have = weights
    depth = field.shape[0] - 2
    cuts = [0, 1, depth - 1, depth] if depth >= 3 else [0, depth]
    rows = []
    for low, high in zip(cuts[:-1], cuts[1:]):
        w_alt_lo, w_alt_hi, w_inc_lo, w_inc_hi, w_raan_lo, w_raan_hi, diagonal = (
            trim(part, have, 0)[low:high] for part in parts
        )
        centre = field[low + 1:high + 1]
        v_down, v_up = field[low:high], field[low + 2:high + 2]
        zero_inc = jnp.zeros_like(centre[:, :1])
        v_prev = jnp.concatenate([zero_inc, centre[:, :-1]], 1)
        v_next = jnp.concatenate([centre[:, 1:], zero_inc], 1)
        v_left, v_right = lane_shifts(centre)
        beside = (
            w_alt_lo * v_down
            + w_alt_hi * v_up
            + w_inc_lo * v_prev
            + w_inc_hi * v_next
            + w_raan_lo * v_left
            + w_raan_hi * v_right
        )
        applied = diagonal * centre - beside
        aim = trim(target, target_halo, 0)[low:high]
        rows.append(centre + OMEGA * (aim - applied) / diagonal)
    return jnp.concatenate(rows, axis=0)


def first_sweep(weights, target, halo):
    diagonal = trim(weights[0][6], weights[1], halo)
    return OMEGA * target / diagonal


def shards(source, k_alt, k_inc, k_raan):
    length = source.shape[-1]
    halo_r = min(RAAN_HALO, length)
    wide = raan_extend(jnp.stack([source, k_alt, k_inc, k_raan], axis=1), halo_r)
    wide_source, wide_alt, wide_inc, wide_raan = (wide[:, i] for i in range(4))
    coef_two = [coarsen(part) for part in (wide_alt, wide_inc, wide_raan)]
    coef_three = [coarsen(part) for part in coef_two]

    first = alt_extend(wide[:, 0:2], 1)
    source_x = first[:, 0]
    weights_one = make_weights(first[:, 1], wide_inc, wide_raan, 1.0, 0)

    density = split_sweep(weights_one, source_x, source_x, 1)
    density = split_sweep(weights_one, alt_extend(density, 1), source_x, 1)
    density_x = alt_extend(density, 1)
    applied, density = apply_op(weights_one, density_x, 1)
    rhs_two = coarsen(wide_source - applied)

    wide_two = SWEEPS + 3
    level_two = alt_extend(jnp.stack([rhs_two] + coef_two, 1), wide_two)
    weights_two = make_weights(
        level_two[:, 1],
        trim(level_two[:, 2], wide_two, wide_two - 1),
        trim(level_two[:, 3], wide_two, wide_two - 1),
        0.25,
        wide_two - 1,
    )
    rhs_two_x = trim(level_two[:, 0], wide_two, wide_two - 1)
    correction = first_sweep(weights_two, rhs_two_x, wide_two - 1)
    correction = sweep(weights_two, correction, wide_two - 1, rhs_two_x, wide_two - 1)
    applied, _ = apply_op(weights_two, trim(correction, wide_two - 2, 1), 1)
    rhs_three = coarsen(trim(rhs_two_x, wide_two - 1, 0) - applied)

    height = rhs_three.shape[0]
    column = spread_gather(jnp.stack([rhs_three] + coef_three, 1))
    weights_three = make_weights(pad_rows(column[:, 1]), column[:, 2], column[:, 3], 0.0625, 0)
    rhs_three_x = column[:, 0]
    coarse_part = first_sweep(weights_three, rhs_three_x, 0)
    for _ in range(COARSE_SWEEPS - 1):
        coarse_part = sweep(weights_three, pad_rows(coarse_part), 1, rhs_three_x, 0, masked=False)
    reach = SWEEPS
    coarse_part = jnp.pad(coarse_part, ((reach, reach), (0, 0), (0, 0)))
    coarse_part = lax.dynamic_slice_in_dim(coarse_part, lax.axis_index("alt") * height, height + 2 * reach, 0)

    correction = correction + trim(refine(coarse_part), 2 * reach, wide_two - 2)
    for halo in range(wide_two - 2, 1, -1):
        correction = sweep(weights_two, correction, halo, rhs_two_x, wide_two - 1)

    density = density_x + trim(refine(correction), 2, 1)
    density = split_sweep(weights_one, density, source_x, 1)
    density = split_sweep(weights_one, alt_extend(density, 1), source_x, 1)
    applied, centre = apply_op(weights_one, alt_extend(density, 1), 1)
    scaled_residual = (wide_source - applied) / weights_one[0][6]
    keep = slice(halo_r, halo_r + length)
    return (centre[..., keep], scaled_residual[..., keep])


def solution(mesh):
    spec = P("alt", None, "raan")
    return jax.shard_map(
        shards, mesh=mesh, in_specs=(spec,) * 4, out_specs=(spec, spec), check_vma=False
    )
```

```python
import jax
import jax.numpy as jnp
from jax import lax
from jax.sharding import PartitionSpec as P

SWEEPS = 2
COARSE_SWEEPS = 4
OMEGA = 0.75
RAAN_HALO = 32
HIGH = lax.Precision.HIGHEST


def pairing(fine):
    rows = lax.broadcasted_iota(jnp.int32, (fine, fine // 2), 0) // 2
    cols = lax.broadcasted_iota(jnp.int32, (fine, fine // 2), 1)
    return (rows == cols).astype(jnp.float32)


def coarsen(values):
    depth, width, length = values.shape
    summed = values.reshape(depth // 2, 2, width, length).sum(axis=1)
    summed = jnp.matmul(summed, pairing(length), precision=HIGH)
    summed = jnp.matmul(pairing(width).T[None], summed, precision=HIGH)
    return summed * 0.125


def refine(values):
    depth, width, length = values.shape
    grown = jnp.matmul(values, pairing(2 * length).T, precision=HIGH)
    grown = jnp.matmul(pairing(2 * width)[None], grown, precision=HIGH)
    grown = jnp.broadcast_to(grown[:, None], (depth, 2, 2 * width, 2 * length))
    return grown.reshape(2 * depth, 2 * width, 2 * length)


def raan_extend(values, halo):
    count, length = lax.axis_size("raan"), values.shape[-1]
    up = [(i, (i + 1) % count) for i in range(count)]
    down = [(j, i) for i, j in up]
    edge = values[..., :halo].shape
    dense = edge[:-2] + (edge[-2] * halo // 128, 128) if edge[-2] * halo % 128 == 0 else edge
    before = lax.ppermute(values[..., length - halo:].reshape(dense), "raan", up).reshape(edge)
    after = lax.ppermute(values[..., :halo].reshape(dense), "raan", down).reshape(edge)
    return jnp.concatenate([before, values, after], axis=-1)


def alt_extend(values, halo):
    count, depth = lax.axis_size("alt"), values.shape[0]
    below, above = [], []
    for distance in range(1, -(-halo // depth) + 1):
        low = max(0, distance * depth - halo)
        high = min(depth, halo - (distance - 1) * depth)
        up = [(i, i + distance) for i in range(count) if i + distance < count]
        down = [(i, i - distance) for i in range(count) if i - distance >= 0]
        below.insert(0, lax.ppermute(values[low:], "alt", up))
        above.append(lax.ppermute(values[:high], "alt", down))
    return jnp.concatenate(below + [values] + above, axis=0)


def alt_row(values, offset):
    count, depth = lax.axis_size("alt"), values.shape[0]
    distance = -(-offset // depth)
    up = [(i, i + distance) for i in range(count) if i + distance < count]
    down = [(i, i - distance) for i in range(count) if i - distance >= 0]
    index = distance * depth - offset
    below = lax.ppermute(values[index:index + 1], "alt", up)
    above = lax.ppermute(values[depth - 1 - index:depth - index], "alt", down)
    return below, above


def spread_gather(values):
    count = lax.axis_size("alt")
    copies = jnp.broadcast_to(values[None], (count,) + values.shape)
    every = lax.all_to_all(copies, "alt", 0, 0)
    return every.reshape((count * values.shape[0],) + values.shape[1:])


def trim(values, have, want):
    cut = have - want
    return values[cut:values.shape[0] - cut] if cut else values


def lane_shifts(values):
    zero = jnp.zeros_like(values[..., :1])
    left = jnp.concatenate([zero, values[..., :-1]], axis=-1)
    right = jnp.concatenate([values[..., 1:], zero], axis=-1)
    return left, right


def make_weights(coef_alt, coef_inc, coef_raan, factor, halo):
    centre = coef_alt[1:-1]
    w_alt_lo = factor * 0.5 * (centre + coef_alt[:-2])
    w_alt_hi = factor * 0.5 * (centre + coef_alt[2:])
    inner_faces = factor * 0.5 * (coef_inc[:, :-1] + coef_inc[:, 1:])
    zero_inc = jnp.zeros_like(coef_inc[:, :1])
    w_inc_lo = jnp.concatenate([zero_inc, inner_faces], 1)
    w_inc_hi = jnp.concatenate([inner_faces, zero_inc], 1)
    raan_left, raan_right = lane_shifts(coef_raan)
    w_raan_lo = factor * 0.5 * (coef_raan + raan_left)
    w_raan_hi = factor * 0.5 * (coef_raan + raan_right)
    diagonal = 1.0 + (w_alt_lo + w_alt_hi + w_inc_lo + w_inc_hi + w_raan_lo + w_raan_hi)
    return (w_alt_lo, w_alt_hi, w_inc_lo, w_inc_hi, w_raan_lo, w_raan_hi, diagonal), halo


def apply_op(weights, field, halo):
    parts, have = weights
    w_alt_lo, w_alt_hi, w_inc_lo, w_inc_hi, w_raan_lo, w_raan_hi, diagonal = (
        trim(part, have, halo - 1) for part in parts
    )
    centre = field[1:-1]
    v_down, v_up = field[:-2], field[2:]
    zero_inc = jnp.zeros_like(centre[:, :1])
    v_prev = jnp.concatenate([zero_inc, centre[:, :-1]], 1)
    v_next = jnp.concatenate([centre[:, 1:], zero_inc], 1)
    v_left, v_right = lane_shifts(centre)
    beside = (
        w_alt_lo * v_down
        + w_alt_hi * v_up
        + w_inc_lo * v_prev
        + w_inc_hi * v_next
        + w_raan_lo * v_left
        + w_raan_hi * v_right
    )
    return diagonal * centre - beside, centre


def inside(shape, halo):
    depth = shape[0] - 2 * halo
    rows = lax.broadcasted_iota(jnp.int32, shape, 0) + lax.axis_index("alt") * depth - halo
    return (rows >= 0) & (rows < depth * lax.axis_size("alt"))


def sweep(weights, field, halo, target, target_halo, masked=True):
    applied, centre = apply_op(weights, field, halo)
    diagonal = trim(weights[0][6], weights[1], halo - 1)
    updated = centre + OMEGA * (trim(target, target_halo, halo - 1) - applied) / diagonal
    if not masked:
        return updated
    return jnp.where(inside(updated.shape, halo - 1), updated, 0.0)


def pad_rows(values):
    zero = jnp.zeros_like(values[:1])
    return jnp.concatenate([zero, values, zero], axis=0)


def split_sweep(weights, field, target, target_halo):
    parts, have = weights
    depth = field.shape[0] - 2
    cuts = [0, 1, depth - 1, depth] if depth >= 3 else [0, depth]
    rows = []
    for low, high in zip(cuts[:-1], cuts[1:]):
        w_alt_lo, w_alt_hi, w_inc_lo, w_inc_hi, w_raan_lo, w_raan_hi, diagonal = (
            trim(part, have, 0)[low:high] for part in parts
        )
        centre = field[low + 1:high + 1]
        v_down, v_up = field[low:high], field[low + 2:high + 2]
        zero_inc = jnp.zeros_like(centre[:, :1])
        v_prev = jnp.concatenate([zero_inc, centre[:, :-1]], 1)
        v_next = jnp.concatenate([centre[:, 1:], zero_inc], 1)
        v_left, v_right = lane_shifts(centre)
        beside = (
            w_alt_lo * v_down
            + w_alt_hi * v_up
            + w_inc_lo * v_prev
            + w_inc_hi * v_next
            + w_raan_lo * v_left
            + w_raan_hi * v_right
        )
        applied = diagonal * centre - beside
        aim = trim(target, target_halo, 0)[low:high]
        rows.append(centre + OMEGA * (aim - applied) / diagonal)
    return jnp.concatenate(rows, axis=0)


def first_sweep(weights, target, halo):
    diagonal = trim(weights[0][6], weights[1], halo)
    return OMEGA * target / diagonal


def shards(source, k_alt, k_inc, k_raan):
    length = source.shape[-1]
    halo_r = min(RAAN_HALO, length)
    wide = raan_extend(jnp.stack([source, k_alt, k_inc, k_raan], axis=1), halo_r)
    wide_source, wide_alt, wide_inc, wide_raan = (wide[:, i] for i in range(4))
    coef_two = [coarsen(part) for part in (wide_alt, wide_inc, wide_raan)]
    coef_three = [coarsen(part) for part in coef_two]

    first = alt_extend(wide[:, 0:2], 1)
    source_x = first[:, 0]
    weights_one = make_weights(first[:, 1], wide_inc, wide_raan, 1.0, 0)

    density = split_sweep(weights_one, source_x, source_x, 1)
    density = split_sweep(weights_one, alt_extend(density, 1), source_x, 1)
    density_x = alt_extend(density, 1)
    applied, density = apply_op(weights_one, density_x, 1)
    rhs_two = coarsen(wide_source - applied)

    wide_two = SWEEPS + 3
    level_two = alt_extend(jnp.stack([rhs_two] + coef_two, 1), wide_two - 1)
    far_below, far_above = alt_row(coef_two[0], wide_two)
    weights_two = make_weights(
        jnp.concatenate([far_below, level_two[:, 1], far_above], axis=0),
        level_two[:, 2],
        level_two[:, 3],
        0.25,
        wide_two - 1,
    )
    rhs_two_x = level_two[:, 0]
    correction = first_sweep(weights_two, rhs_two_x, wide_two - 1)
    correction = sweep(weights_two, correction, wide_two - 1, rhs_two_x, wide_two - 1)
    applied, _ = apply_op(weights_two, trim(correction, wide_two - 2, 1), 1)
    rhs_three = coarsen(trim(rhs_two_x, wide_two - 1, 0) - applied)

    height = rhs_three.shape[0]
    column = spread_gather(jnp.stack([rhs_three] + coef_three, 1))
    weights_three = make_weights(pad_rows(column[:, 1]), column[:, 2], column[:, 3], 0.0625, 0)
    rhs_three_x = column[:, 0]
    coarse_part = first_sweep(weights_three, rhs_three_x, 0)
    for _ in range(COARSE_SWEEPS - 1):
        coarse_part = sweep(weights_three, pad_rows(coarse_part), 1, rhs_three_x, 0, masked=False)
    reach = SWEEPS
    coarse_part = jnp.pad(coarse_part, ((reach, reach), (0, 0), (0, 0)))
    coarse_part = lax.dynamic_slice_in_dim(coarse_part, lax.axis_index("alt") * height, height + 2 * reach, 0)

    correction = correction + trim(refine(coarse_part), 2 * reach, wide_two - 2)
    for halo in range(wide_two - 2, 1, -1):
        correction = sweep(weights_two, correction, halo, rhs_two_x, wide_two - 1)

    density = density_x + trim(refine(correction), 2, 1)
    density = split_sweep(weights_one, density, source_x, 1)
    density = split_sweep(weights_one, alt_extend(density, 1), source_x, 1)
    applied, centre = apply_op(weights_one, alt_extend(density, 1), 1)
    scaled_residual = (wide_source - applied) / weights_one[0][6]
    keep = slice(halo_r, halo_r + length)
    return (centre[..., keep], scaled_residual[..., keep])


def solution(mesh):
    spec = P("alt", None, "raan")
    return jax.shard_map(
        shards, mesh=mesh, in_specs=(spec,) * 4, out_specs=(spec, spec), check_vma=False
    )
```

```python
import jax
import jax.numpy as jnp
from jax import lax
from jax.sharding import PartitionSpec as P

SWEEPS = 2
COARSE_SWEEPS = 4
OMEGA = 0.75
RAAN_HALO = 32
HIGH = lax.Precision.HIGHEST


def pairing(fine):
    rows = lax.broadcasted_iota(jnp.int32, (fine, fine // 2), 0) // 2
    cols = lax.broadcasted_iota(jnp.int32, (fine, fine // 2), 1)
    return (rows == cols).astype(jnp.float32)


def coarsen(values):
    depth, width, length = values.shape
    summed = values.reshape(depth // 2, 2, width, length).sum(axis=1)
    summed = jnp.matmul(summed, pairing(length), precision=HIGH)
    summed = jnp.matmul(pairing(width).T[None], summed, precision=HIGH)
    return summed * 0.125


def refine(values):
    depth, width, length = values.shape
    grown = jnp.matmul(values, pairing(2 * length).T, precision=HIGH)
    grown = jnp.matmul(pairing(2 * width)[None], grown, precision=HIGH)
    grown = jnp.broadcast_to(grown[:, None], (depth, 2, 2 * width, 2 * length))
    return grown.reshape(2 * depth, 2 * width, 2 * length)


def raan_extend(values, halo):
    count, length = lax.axis_size("raan"), values.shape[-1]
    up = [(i, (i + 1) % count) for i in range(count)]
    down = [(j, i) for i, j in up]
    edge = values[..., :halo].shape
    dense = edge[:-2] + (edge[-2] * halo // 128, 128) if edge[-2] * halo % 128 == 0 else edge
    before = lax.ppermute(values[..., length - halo:].reshape(dense), "raan", up).reshape(edge)
    after = lax.ppermute(values[..., :halo].reshape(dense), "raan", down).reshape(edge)
    return jnp.concatenate([before, values, after], axis=-1)


def alt_extend(values, halo):
    count, depth = lax.axis_size("alt"), values.shape[0]
    below, above = [], []
    for distance in range(1, -(-halo // depth) + 1):
        low = max(0, distance * depth - halo)
        high = min(depth, halo - (distance - 1) * depth)
        up = [(i, i + distance) for i in range(count) if i + distance < count]
        down = [(i, i - distance) for i in range(count) if i - distance >= 0]
        below.insert(0, lax.ppermute(values[low:], "alt", up))
        above.append(lax.ppermute(values[:high], "alt", down))
    return jnp.concatenate(below + [values] + above, axis=0)


def alt_row(values, offset):
    count, depth = lax.axis_size("alt"), values.shape[0]
    distance = -(-offset // depth)
    up = [(i, i + distance) for i in range(count) if i + distance < count]
    down = [(i, i - distance) for i in range(count) if i - distance >= 0]
    index = distance * depth - offset
    below = lax.ppermute(values[index:index + 1], "alt", up)
    above = lax.ppermute(values[depth - 1 - index:depth - index], "alt", down)
    return below, above


def spread_gather(values):
    count = lax.axis_size("alt")
    copies = jnp.broadcast_to(values[None], (count,) + values.shape)
    every = lax.all_to_all(copies, "alt", 0, 0)
    return every.reshape((count * values.shape[0],) + values.shape[1:])


def trim(values, have, want):
    cut = have - want
    return values[cut:values.shape[0] - cut] if cut else values


def lane_shifts(values):
    zero = jnp.zeros_like(values[..., :1])
    left = jnp.concatenate([zero, values[..., :-1]], axis=-1)
    right = jnp.concatenate([values[..., 1:], zero], axis=-1)
    return left, right


def make_weights(coef_alt, coef_inc, coef_raan, factor, halo):
    centre = coef_alt[1:-1]
    w_alt_lo = factor * 0.5 * (centre + coef_alt[:-2])
    w_alt_hi = factor * 0.5 * (centre + coef_alt[2:])
    inner_faces = factor * 0.5 * (coef_inc[:, :-1] + coef_inc[:, 1:])
    zero_inc = jnp.zeros_like(coef_inc[:, :1])
    w_inc_lo = jnp.concatenate([zero_inc, inner_faces], 1)
    w_inc_hi = jnp.concatenate([inner_faces, zero_inc], 1)
    raan_left, raan_right = lane_shifts(coef_raan)
    w_raan_lo = factor * 0.5 * (coef_raan + raan_left)
    w_raan_hi = factor * 0.5 * (coef_raan + raan_right)
    diagonal = 1.0 + (w_alt_lo + w_alt_hi + w_inc_lo + w_inc_hi + w_raan_lo + w_raan_hi)
    return (w_alt_lo, w_alt_hi, w_inc_lo, w_inc_hi, w_raan_lo, w_raan_hi, diagonal), halo


def apply_op(weights, field, halo):
    parts, have = weights
    w_alt_lo, w_alt_hi, w_inc_lo, w_inc_hi, w_raan_lo, w_raan_hi, diagonal = (
        trim(part, have, halo - 1) for part in parts
    )
    centre = field[1:-1]
    v_down, v_up = field[:-2], field[2:]
    zero_inc = jnp.zeros_like(centre[:, :1])
    v_prev = jnp.concatenate([zero_inc, centre[:, :-1]], 1)
    v_next = jnp.concatenate([centre[:, 1:], zero_inc], 1)
    v_left, v_right = lane_shifts(centre)
    beside = (
        w_alt_lo * v_down
        + w_alt_hi * v_up
        + w_inc_lo * v_prev
        + w_inc_hi * v_next
        + w_raan_lo * v_left
        + w_raan_hi * v_right
    )
    return diagonal * centre - beside, centre


def inside(shape, halo):
    depth = shape[0] - 2 * halo
    rows = lax.broadcasted_iota(jnp.int32, shape, 0) + lax.axis_index("alt") * depth - halo
    return (rows >= 0) & (rows < depth * lax.axis_size("alt"))


def sweep(weights, field, halo, target, target_halo, masked=True):
    applied, centre = apply_op(weights, field, halo)
    diagonal = trim(weights[0][6], weights[1], halo - 1)
    updated = centre + OMEGA * (trim(target, target_halo, halo - 1) - applied) / diagonal
    if not masked:
        return updated
    return jnp.where(inside(updated.shape, halo - 1), updated, 0.0)


def pad_rows(values):
    zero = jnp.zeros_like(values[:1])
    return jnp.concatenate([zero, values, zero], axis=0)


def split_sweep(weights, field, target, target_halo):
    parts, have = weights
    depth = field.shape[0] - 2
    cuts = [0, 1, depth - 1, depth] if depth >= 3 else [0, depth]
    rows = []
    for low, high in zip(cuts[:-1], cuts[1:]):
        w_alt_lo, w_alt_hi, w_inc_lo, w_inc_hi, w_raan_lo, w_raan_hi, diagonal = (
            trim(part, have, 0)[low:high] for part in parts
        )
        centre = field[low + 1:high + 1]
        v_down, v_up = field[low:high], field[low + 2:high + 2]
        zero_inc = jnp.zeros_like(centre[:, :1])
        v_prev = jnp.concatenate([zero_inc, centre[:, :-1]], 1)
        v_next = jnp.concatenate([centre[:, 1:], zero_inc], 1)
        v_left, v_right = lane_shifts(centre)
        beside = (
            w_alt_lo * v_down
            + w_alt_hi * v_up
            + w_inc_lo * v_prev
            + w_inc_hi * v_next
            + w_raan_lo * v_left
            + w_raan_hi * v_right
        )
        applied = diagonal * centre - beside
        aim = trim(target, target_halo, 0)[low:high]
        rows.append(centre + OMEGA * (aim - applied) / diagonal)
    return jnp.concatenate(rows, axis=0)


def first_sweep(weights, target, halo):
    diagonal = trim(weights[0][6], weights[1], halo)
    return OMEGA * target / diagonal


def shards(source, k_alt, k_inc, k_raan):
    length = source.shape[-1]
    halo_r = min(RAAN_HALO, length)
    wide = raan_extend(jnp.stack([source, k_alt, k_inc, k_raan], axis=1), halo_r)
    wide_source, wide_alt, wide_inc, wide_raan = (wide[:, i] for i in range(4))
    coef_two = [coarsen(part) for part in (wide_alt, wide_inc, wide_raan)]
    coef_three = [coarsen(part) for part in coef_two]

    first = alt_extend(wide[:, 0:2], 1)
    source_x = first[:, 0]
    weights_one = make_weights(first[:, 1], wide_inc, wide_raan, 1.0, 0)

    density = split_sweep(weights_one, source_x, source_x, 1)
    density = split_sweep(weights_one, alt_extend(density, 1), source_x, 1)
    density_x = alt_extend(density, 1)
    applied, density = apply_op(weights_one, density_x, 1)
    rhs_two = coarsen(wide_source - applied)

    wide_two = SWEEPS + 3
    lanes = rhs_two.shape[-1]
    level_two = alt_extend(jnp.concatenate([rhs_two] + coef_two, axis=-1), wide_two - 1)
    level_two = [level_two[..., i * lanes:(i + 1) * lanes] for i in range(4)]
    far_below, far_above = alt_row(coef_two[0], wide_two)
    weights_two = make_weights(
        jnp.concatenate([far_below, level_two[1], far_above], axis=0),
        level_two[2],
        level_two[3],
        0.25,
        wide_two - 1,
    )
    rhs_two_x = level_two[0]
    correction = first_sweep(weights_two, rhs_two_x, wide_two - 1)
    correction = sweep(weights_two, correction, wide_two - 1, rhs_two_x, wide_two - 1)
    applied, _ = apply_op(weights_two, trim(correction, wide_two - 2, 1), 1)
    rhs_three = coarsen(trim(rhs_two_x, wide_two - 1, 0) - applied)

    height = rhs_three.shape[0]
    column = spread_gather(jnp.stack([rhs_three] + coef_three, 1))
    weights_three = make_weights(pad_rows(column[:, 1]), column[:, 2], column[:, 3], 0.0625, 0)
    rhs_three_x = column[:, 0]
    coarse_part = first_sweep(weights_three, rhs_three_x, 0)
    for _ in range(COARSE_SWEEPS - 1):
        coarse_part = sweep(weights_three, pad_rows(coarse_part), 1, rhs_three_x, 0, masked=False)
    reach = SWEEPS
    coarse_part = jnp.pad(coarse_part, ((reach, reach), (0, 0), (0, 0)))
    coarse_part = lax.dynamic_slice_in_dim(coarse_part, lax.axis_index("alt") * height, height + 2 * reach, 0)

    correction = correction + trim(refine(coarse_part), 2 * reach, wide_two - 2)
    for halo in range(wide_two - 2, 1, -1):
        correction = sweep(weights_two, correction, halo, rhs_two_x, wide_two - 1)

    density = density_x + trim(refine(correction), 2, 1)
    density = split_sweep(weights_one, density, source_x, 1)
    density = split_sweep(weights_one, alt_extend(density, 1), source_x, 1)
    applied, centre = apply_op(weights_one, alt_extend(density, 1), 1)
    scaled_residual = (wide_source - applied) / weights_one[0][6]
    keep = slice(halo_r, halo_r + length)
    return (centre[..., keep], scaled_residual[..., keep])


def solution(mesh):
    spec = P("alt", None, "raan")
    return jax.shard_map(
        shards, mesh=mesh, in_specs=(spec,) * 4, out_specs=(spec, spec), check_vma=False
    )
```

```python
import jax
import jax.numpy as jnp
from jax import lax
from jax.sharding import PartitionSpec as P

SWEEPS = 2
COARSE_SWEEPS = 4
OMEGA = 0.75
RAAN_HALO = 32
HIGH = lax.Precision.HIGHEST


def pairing(fine):
    rows = lax.broadcasted_iota(jnp.int32, (fine, fine // 2), 0) // 2
    cols = lax.broadcasted_iota(jnp.int32, (fine, fine // 2), 1)
    return (rows == cols).astype(jnp.float32)


def coarsen(values):
    depth, width, length = values.shape
    summed = values.reshape(depth // 2, 2, width, length).sum(axis=1)
    summed = jnp.matmul(summed, pairing(length), precision=HIGH)
    summed = jnp.matmul(pairing(width).T[None], summed, precision=HIGH)
    return summed * 0.125


def refine(values):
    depth, width, length = values.shape
    grown = jnp.matmul(values, pairing(2 * length).T, precision=HIGH)
    grown = jnp.matmul(pairing(2 * width)[None], grown, precision=HIGH)
    grown = jnp.broadcast_to(grown[:, None], (depth, 2, 2 * width, 2 * length))
    return grown.reshape(2 * depth, 2 * width, 2 * length)


def raan_extend(values, halo):
    count, length = lax.axis_size("raan"), values.shape[-1]
    up = [(i, (i + 1) % count) for i in range(count)]
    down = [(j, i) for i, j in up]
    edge = values[..., :halo].shape
    dense = edge[:-2] + (edge[-2] * halo // 128, 128) if edge[-2] * halo % 128 == 0 else edge
    before = lax.ppermute(values[..., length - halo:].reshape(dense), "raan", up).reshape(edge)
    after = lax.ppermute(values[..., :halo].reshape(dense), "raan", down).reshape(edge)
    return jnp.concatenate([before, values, after], axis=-1)


def alt_extend(values, halo):
    count, depth = lax.axis_size("alt"), values.shape[0]
    below, above = [], []
    for distance in range(1, -(-halo // depth) + 1):
        low = max(0, distance * depth - halo)
        high = min(depth, halo - (distance - 1) * depth)
        up = [(i, i + distance) for i in range(count) if i + distance < count]
        down = [(i, i - distance) for i in range(count) if i - distance >= 0]
        below.insert(0, lax.ppermute(values[low:], "alt", up))
        above.append(lax.ppermute(values[:high], "alt", down))
    return jnp.concatenate(below + [values] + above, axis=0)


def alt_row(values, offset):
    count, depth = lax.axis_size("alt"), values.shape[0]
    distance = -(-offset // depth)
    up = [(i, i + distance) for i in range(count) if i + distance < count]
    down = [(i, i - distance) for i in range(count) if i - distance >= 0]
    index = distance * depth - offset
    below = lax.ppermute(values[index:index + 1], "alt", up)
    above = lax.ppermute(values[depth - 1 - index:depth - index], "alt", down)
    return below, above


def spread_gather(values):
    count = lax.axis_size("alt")
    copies = jnp.broadcast_to(values[None], (count,) + values.shape)
    every = lax.all_to_all(copies, "alt", 0, 0)
    return every.reshape((count * values.shape[0],) + values.shape[1:])


def trim(values, have, want):
    cut = have - want
    return values[cut:values.shape[0] - cut] if cut else values


def lane_shifts(values):
    zero = jnp.zeros_like(values[..., :1])
    left = jnp.concatenate([zero, values[..., :-1]], axis=-1)
    right = jnp.concatenate([values[..., 1:], zero], axis=-1)
    return left, right


def make_weights(coef_alt, coef_inc, coef_raan, factor, halo):
    centre = coef_alt[1:-1]
    w_alt_lo = factor * 0.5 * (centre + coef_alt[:-2])
    w_alt_hi = factor * 0.5 * (centre + coef_alt[2:])
    inner_faces = factor * 0.5 * (coef_inc[:, :-1] + coef_inc[:, 1:])
    zero_inc = jnp.zeros_like(coef_inc[:, :1])
    w_inc_lo = jnp.concatenate([zero_inc, inner_faces], 1)
    w_inc_hi = jnp.concatenate([inner_faces, zero_inc], 1)
    raan_left, raan_right = lane_shifts(coef_raan)
    w_raan_lo = factor * 0.5 * (coef_raan + raan_left)
    w_raan_hi = factor * 0.5 * (coef_raan + raan_right)
    diagonal = 1.0 + (w_alt_lo + w_alt_hi + w_inc_lo + w_inc_hi + w_raan_lo + w_raan_hi)
    return (w_alt_lo, w_alt_hi, w_inc_lo, w_inc_hi, w_raan_lo, w_raan_hi, diagonal), halo


def apply_op(weights, field, halo):
    parts, have = weights
    w_alt_lo, w_alt_hi, w_inc_lo, w_inc_hi, w_raan_lo, w_raan_hi, diagonal = (
        trim(part, have, halo - 1) for part in parts
    )
    centre = field[1:-1]
    v_down, v_up = field[:-2], field[2:]
    zero_inc = jnp.zeros_like(centre[:, :1])
    v_prev = jnp.concatenate([zero_inc, centre[:, :-1]], 1)
    v_next = jnp.concatenate([centre[:, 1:], zero_inc], 1)
    v_left, v_right = lane_shifts(centre)
    beside = (
        w_alt_lo * v_down
        + w_alt_hi * v_up
        + w_inc_lo * v_prev
        + w_inc_hi * v_next
        + w_raan_lo * v_left
        + w_raan_hi * v_right
    )
    return diagonal * centre - beside, centre


def inside(shape, halo):
    depth = shape[0] - 2 * halo
    rows = lax.broadcasted_iota(jnp.int32, shape, 0) + lax.axis_index("alt") * depth - halo
    return (rows >= 0) & (rows < depth * lax.axis_size("alt"))


def sweep(weights, field, halo, target, target_halo, masked=True):
    applied, centre = apply_op(weights, field, halo)
    diagonal = trim(weights[0][6], weights[1], halo - 1)
    updated = centre + OMEGA * (trim(target, target_halo, halo - 1) - applied) / diagonal
    if not masked:
        return updated
    return jnp.where(inside(updated.shape, halo - 1), updated, 0.0)


def pad_rows(values):
    zero = jnp.zeros_like(values[:1])
    return jnp.concatenate([zero, values, zero], axis=0)


def split_sweep(weights, field, target, target_halo):
    parts, have = weights
    depth = field.shape[0] - 2
    cuts = [0, 1, depth - 1, depth] if depth >= 3 else [0, depth]
    rows = []
    for low, high in zip(cuts[:-1], cuts[1:]):
        w_alt_lo, w_alt_hi, w_inc_lo, w_inc_hi, w_raan_lo, w_raan_hi, diagonal = (
            trim(part, have, 0)[low:high] for part in parts
        )
        centre = field[low + 1:high + 1]
        v_down, v_up = field[low:high], field[low + 2:high + 2]
        zero_inc = jnp.zeros_like(centre[:, :1])
        v_prev = jnp.concatenate([zero_inc, centre[:, :-1]], 1)
        v_next = jnp.concatenate([centre[:, 1:], zero_inc], 1)
        v_left, v_right = lane_shifts(centre)
        beside = (
            w_alt_lo * v_down
            + w_alt_hi * v_up
            + w_inc_lo * v_prev
            + w_inc_hi * v_next
            + w_raan_lo * v_left
            + w_raan_hi * v_right
        )
        applied = diagonal * centre - beside
        aim = trim(target, target_halo, 0)[low:high]
        rows.append(centre + OMEGA * (aim - applied) / diagonal)
    return jnp.concatenate(rows, axis=0)


def first_sweep(weights, target, halo):
    diagonal = trim(weights[0][6], weights[1], halo)
    return OMEGA * target / diagonal


def shards(source, k_alt, k_inc, k_raan):
    length = source.shape[-1]
    halo_r = min(RAAN_HALO, length)
    wide = raan_extend(jnp.stack([source, k_alt, k_inc, k_raan], axis=1), halo_r)
    wide_source, wide_alt, wide_inc, wide_raan = (wide[:, i] for i in range(4))
    coef_two = [coarsen(part) for part in (wide_alt, wide_inc, wide_raan)]
    coef_three = [coarsen(part) for part in coef_two]

    first = alt_extend(wide[:, 0:2], 1)
    source_x = first[:, 0]
    weights_one = make_weights(first[:, 1], wide_inc, wide_raan, 1.0, 0)

    density = split_sweep(weights_one, source_x, source_x, 1)
    density = split_sweep(weights_one, alt_extend(density, 1), source_x, 1)
    density_x = alt_extend(density, 1)
    applied, density = apply_op(weights_one, density_x, 1)
    rhs_two = coarsen(wide_source - applied)

    wide_two = SWEEPS + 3
    lanes = rhs_two.shape[-1]
    level_two = alt_extend(jnp.concatenate([rhs_two] + coef_two, axis=-1), wide_two - 1)
    level_two = [level_two[..., i * lanes:(i + 1) * lanes] for i in range(4)]
    far_below, far_above = alt_row(coef_two[0], wide_two)
    weights_two = make_weights(
        jnp.concatenate([far_below, level_two[1], far_above], axis=0),
        level_two[2],
        level_two[3],
        0.25,
        wide_two - 1,
    )
    rhs_two_x = level_two[0]
    correction = first_sweep(weights_two, rhs_two_x, wide_two - 1)
    correction = sweep(weights_two, correction, wide_two - 1, rhs_two_x, wide_two - 1)
    applied, _ = apply_op(weights_two, trim(correction, wide_two - 2, 1), 1)
    rhs_three = coarsen(trim(rhs_two_x, wide_two - 1, 0) - applied)

    height = rhs_three.shape[0]
    lanes = rhs_three.shape[-1]
    column = spread_gather(jnp.concatenate([rhs_three] + coef_three, axis=-1))
    column = [column[..., i * lanes:(i + 1) * lanes] for i in range(4)]
    weights_three = make_weights(pad_rows(column[1]), column[2], column[3], 0.0625, 0)
    rhs_three_x = column[0]
    coarse_part = first_sweep(weights_three, rhs_three_x, 0)
    for _ in range(COARSE_SWEEPS - 1):
        coarse_part = sweep(weights_three, pad_rows(coarse_part), 1, rhs_three_x, 0, masked=False)
    reach = SWEEPS
    coarse_part = jnp.pad(coarse_part, ((reach, reach), (0, 0), (0, 0)))
    coarse_part = lax.dynamic_slice_in_dim(coarse_part, lax.axis_index("alt") * height, height + 2 * reach, 0)

    correction = correction + trim(refine(coarse_part), 2 * reach, wide_two - 2)
    for halo in range(wide_two - 2, 1, -1):
        correction = sweep(weights_two, correction, halo, rhs_two_x, wide_two - 1)

    density = density_x + trim(refine(correction), 2, 1)
    density = split_sweep(weights_one, density, source_x, 1)
    density = split_sweep(weights_one, alt_extend(density, 1), source_x, 1)
    applied, centre = apply_op(weights_one, alt_extend(density, 1), 1)
    scaled_residual = (wide_source - applied) / weights_one[0][6]
    keep = slice(halo_r, halo_r + length)
    return (centre[..., keep], scaled_residual[..., keep])


def solution(mesh):
    spec = P("alt", None, "raan")
    return jax.shard_map(
        shards, mesh=mesh, in_specs=(spec,) * 4, out_specs=(spec, spec), check_vma=False
    )
```

```python
import jax
import jax.numpy as jnp
from jax import lax
from jax.sharding import PartitionSpec as P

SWEEPS = 2
COARSE_SWEEPS = 4
OMEGA = 0.75
RAAN_HALO = 32
HIGH = lax.Precision.HIGHEST


def pairing(fine):
    rows = lax.broadcasted_iota(jnp.int32, (fine, fine // 2), 0) // 2
    cols = lax.broadcasted_iota(jnp.int32, (fine, fine // 2), 1)
    return (rows == cols).astype(jnp.float32)


def coarsen(values):
    depth, width, length = values.shape
    summed = values.reshape(depth // 2, 2, width, length).sum(axis=1)
    summed = jnp.matmul(summed, pairing(length), precision=HIGH)
    summed = jnp.matmul(pairing(width).T[None], summed, precision=HIGH)
    return summed * 0.125


def refine(values):
    depth, width, length = values.shape
    grown = jnp.matmul(values, pairing(2 * length).T, precision=HIGH)
    grown = jnp.matmul(pairing(2 * width)[None], grown, precision=HIGH)
    grown = jnp.broadcast_to(grown[:, None], (depth, 2, 2 * width, 2 * length))
    return grown.reshape(2 * depth, 2 * width, 2 * length)


def raan_extend(values, halo):
    count, length = lax.axis_size("raan"), values.shape[-1]
    up = [(i, (i + 1) % count) for i in range(count)]
    down = [(j, i) for i, j in up]
    edge = values[..., :halo].shape
    dense = edge[:-2] + (edge[-2] * halo // 128, 128) if edge[-2] * halo % 128 == 0 else edge
    before = lax.ppermute(values[..., length - halo:].reshape(dense), "raan", up).reshape(edge)
    after = lax.ppermute(values[..., :halo].reshape(dense), "raan", down).reshape(edge)
    return jnp.concatenate([before, values, after], axis=-1)


def alt_extend(values, halo):
    count, depth = lax.axis_size("alt"), values.shape[0]
    below, above = [], []
    for distance in range(1, -(-halo // depth) + 1):
        low = max(0, distance * depth - halo)
        high = min(depth, halo - (distance - 1) * depth)
        up = [(i, i + distance) for i in range(count) if i + distance < count]
        down = [(i, i - distance) for i in range(count) if i - distance >= 0]
        below.insert(0, lax.ppermute(values[low:], "alt", up))
        above.append(lax.ppermute(values[:high], "alt", down))
    return jnp.concatenate(below + [values] + above, axis=0)


def alt_row(values, offset):
    count, depth = lax.axis_size("alt"), values.shape[0]
    distance = -(-offset // depth)
    up = [(i, i + distance) for i in range(count) if i + distance < count]
    down = [(i, i - distance) for i in range(count) if i - distance >= 0]
    index = distance * depth - offset
    below = lax.ppermute(values[index:index + 1], "alt", up)
    above = lax.ppermute(values[depth - 1 - index:depth - index], "alt", down)
    return below, above


def spread_gather(values):
    count = lax.axis_size("alt")
    copies = jnp.broadcast_to(values[None], (count,) + values.shape)
    every = lax.all_to_all(copies, "alt", 0, 0)
    return every.reshape((count * values.shape[0],) + values.shape[1:])


def trim(values, have, want):
    cut = have - want
    return values[cut:values.shape[0] - cut] if cut else values


def lane_shifts(values):
    zero = jnp.zeros_like(values[..., :1])
    left = jnp.concatenate([zero, values[..., :-1]], axis=-1)
    right = jnp.concatenate([values[..., 1:], zero], axis=-1)
    return left, right


def make_weights(coef_alt, coef_inc, coef_raan, factor, halo):
    centre = coef_alt[1:-1]
    w_alt_lo = factor * 0.5 * (centre + coef_alt[:-2])
    w_alt_hi = factor * 0.5 * (centre + coef_alt[2:])
    inner_faces = factor * 0.5 * (coef_inc[:, :-1] + coef_inc[:, 1:])
    zero_inc = jnp.zeros_like(coef_inc[:, :1])
    w_inc_lo = jnp.concatenate([zero_inc, inner_faces], 1)
    w_inc_hi = jnp.concatenate([inner_faces, zero_inc], 1)
    raan_left, raan_right = lane_shifts(coef_raan)
    w_raan_lo = factor * 0.5 * (coef_raan + raan_left)
    w_raan_hi = factor * 0.5 * (coef_raan + raan_right)
    diagonal = 1.0 + (w_alt_lo + w_alt_hi + w_inc_lo + w_inc_hi + w_raan_lo + w_raan_hi)
    return (w_alt_lo, w_alt_hi, w_inc_lo, w_inc_hi, w_raan_lo, w_raan_hi, diagonal), halo


def apply_op(weights, field, halo):
    parts, have = weights
    w_alt_lo, w_alt_hi, w_inc_lo, w_inc_hi, w_raan_lo, w_raan_hi, diagonal = (
        trim(part, have, halo - 1) for part in parts
    )
    centre = field[1:-1]
    v_down, v_up = field[:-2], field[2:]
    zero_inc = jnp.zeros_like(centre[:, :1])
    v_prev = jnp.concatenate([zero_inc, centre[:, :-1]], 1)
    v_next = jnp.concatenate([centre[:, 1:], zero_inc], 1)
    v_left, v_right = lane_shifts(centre)
    beside = (
        w_alt_lo * v_down
        + w_alt_hi * v_up
        + w_inc_lo * v_prev
        + w_inc_hi * v_next
        + w_raan_lo * v_left
        + w_raan_hi * v_right
    )
    return diagonal * centre - beside, centre


def inside(shape, halo):
    depth = shape[0] - 2 * halo
    rows = lax.broadcasted_iota(jnp.int32, shape, 0) + lax.axis_index("alt") * depth - halo
    return (rows >= 0) & (rows < depth * lax.axis_size("alt"))


def sweep(weights, field, halo, target, target_halo, masked=True):
    applied, centre = apply_op(weights, field, halo)
    diagonal = trim(weights[0][6], weights[1], halo - 1)
    updated = centre + OMEGA * (trim(target, target_halo, halo - 1) - applied) / diagonal
    if not masked:
        return updated
    return jnp.where(inside(updated.shape, halo - 1), updated, 0.0)


def pad_rows(values):
    zero = jnp.zeros_like(values[:1])
    return jnp.concatenate([zero, values, zero], axis=0)


def split_sweep(weights, field, target, target_halo):
    parts, have = weights
    depth = field.shape[0] - 2
    cuts = [0, 1, depth - 1, depth] if depth >= 3 else [0, depth]
    rows = []
    for low, high in zip(cuts[:-1], cuts[1:]):
        w_alt_lo, w_alt_hi, w_inc_lo, w_inc_hi, w_raan_lo, w_raan_hi, diagonal = (
            trim(part, have, 0)[low:high] for part in parts
        )
        centre = field[low + 1:high + 1]
        v_down, v_up = field[low:high], field[low + 2:high + 2]
        zero_inc = jnp.zeros_like(centre[:, :1])
        v_prev = jnp.concatenate([zero_inc, centre[:, :-1]], 1)
        v_next = jnp.concatenate([centre[:, 1:], zero_inc], 1)
        v_left, v_right = lane_shifts(centre)
        beside = (
            w_alt_lo * v_down
            + w_alt_hi * v_up
            + w_inc_lo * v_prev
            + w_inc_hi * v_next
            + w_raan_lo * v_left
            + w_raan_hi * v_right
        )
        applied = diagonal * centre - beside
        aim = trim(target, target_halo, 0)[low:high]
        rows.append(centre + OMEGA * (aim - applied) / diagonal)
    return jnp.concatenate(rows, axis=0)


def first_sweep(weights, target, halo):
    diagonal = trim(weights[0][6], weights[1], halo)
    return OMEGA * target / diagonal


def shards(source, k_alt, k_inc, k_raan):
    length = source.shape[-1]
    halo_r = min(RAAN_HALO, length)
    wide = raan_extend(jnp.stack([source, k_alt, k_inc, k_raan], axis=1), halo_r)
    wide_source, wide_alt, wide_inc, wide_raan = (wide[:, i] for i in range(4))
    coef_two = [coarsen(part) for part in (wide_alt, wide_inc, wide_raan)]
    coef_three = [coarsen(part) for part in coef_two]

    first = alt_extend(jnp.concatenate([wide[:, 0], wide[:, 1]], axis=-1), 1)
    lanes = wide.shape[-1]
    source_x = first[..., :lanes]
    weights_one = make_weights(first[..., lanes:], wide_inc, wide_raan, 1.0, 0)

    density = split_sweep(weights_one, source_x, source_x, 1)
    density = split_sweep(weights_one, alt_extend(density, 1), source_x, 1)
    density_x = alt_extend(density, 1)
    applied, density = apply_op(weights_one, density_x, 1)
    rhs_two = coarsen(wide_source - applied)

    wide_two = SWEEPS + 3
    lanes = rhs_two.shape[-1]
    level_two = alt_extend(jnp.concatenate([rhs_two] + coef_two, axis=-1), wide_two - 1)
    level_two = [level_two[..., i * lanes:(i + 1) * lanes] for i in range(4)]
    far_below, far_above = alt_row(coef_two[0], wide_two)
    weights_two = make_weights(
        jnp.concatenate([far_below, level_two[1], far_above], axis=0),
        level_two[2],
        level_two[3],
        0.25,
        wide_two - 1,
    )
    rhs_two_x = level_two[0]
    correction = first_sweep(weights_two, rhs_two_x, wide_two - 1)
    correction = sweep(weights_two, correction, wide_two - 1, rhs_two_x, wide_two - 1)
    applied, _ = apply_op(weights_two, trim(correction, wide_two - 2, 1), 1)
    rhs_three = coarsen(trim(rhs_two_x, wide_two - 1, 0) - applied)

    height = rhs_three.shape[0]
    column = spread_gather(jnp.stack([rhs_three] + coef_three, 1))
    weights_three = make_weights(pad_rows(column[:, 1]), column[:, 2], column[:, 3], 0.0625, 0)
    rhs_three_x = column[:, 0]
    coarse_part = first_sweep(weights_three, rhs_three_x, 0)
    for _ in range(COARSE_SWEEPS - 1):
        coarse_part = sweep(weights_three, pad_rows(coarse_part), 1, rhs_three_x, 0, masked=False)
    reach = SWEEPS
    coarse_part = jnp.pad(coarse_part, ((reach, reach), (0, 0), (0, 0)))
    coarse_part = lax.dynamic_slice_in_dim(coarse_part, lax.axis_index("alt") * height, height + 2 * reach, 0)

    correction = correction + trim(refine(coarse_part), 2 * reach, wide_two - 2)
    for halo in range(wide_two - 2, 1, -1):
        correction = sweep(weights_two, correction, halo, rhs_two_x, wide_two - 1)

    density = density_x + trim(refine(correction), 2, 1)
    density = split_sweep(weights_one, density, source_x, 1)
    density = split_sweep(weights_one, alt_extend(density, 1), source_x, 1)
    applied, centre = apply_op(weights_one, alt_extend(density, 1), 1)
    scaled_residual = (wide_source - applied) / weights_one[0][6]
    keep = slice(halo_r, halo_r + length)
    return (centre[..., keep], scaled_residual[..., keep])


def solution(mesh):
    spec = P("alt", None, "raan")
    return jax.shard_map(
        shards, mesh=mesh, in_specs=(spec,) * 4, out_specs=(spec, spec), check_vma=False
    )
```

```python
import jax
import jax.numpy as jnp
from jax import lax
from jax.sharding import PartitionSpec as P

SWEEPS = 2
COARSE_SWEEPS = 4
OMEGA = 0.75
RAAN_HALO = 32
HIGH = lax.Precision.HIGHEST


def pairing(fine):
    rows = lax.broadcasted_iota(jnp.int32, (fine, fine // 2), 0) // 2
    cols = lax.broadcasted_iota(jnp.int32, (fine, fine // 2), 1)
    return (rows == cols).astype(jnp.float32)


def coarsen(values):
    depth, width, length = values.shape
    summed = values.reshape(depth // 2, 2, width, length).sum(axis=1)
    summed = jnp.matmul(summed, pairing(length), precision=HIGH)
    summed = jnp.matmul(pairing(width).T[None], summed, precision=HIGH)
    return summed * 0.125


def refine(values):
    depth, width, length = values.shape
    grown = jnp.matmul(values, pairing(2 * length).T, precision=HIGH)
    grown = jnp.matmul(pairing(2 * width)[None], grown, precision=HIGH)
    grown = jnp.broadcast_to(grown[:, None], (depth, 2, 2 * width, 2 * length))
    return grown.reshape(2 * depth, 2 * width, 2 * length)


def raan_extend(values, halo):
    count, length = lax.axis_size("raan"), values.shape[-1]
    up = [(i, (i + 1) % count) for i in range(count)]
    down = [(j, i) for i, j in up]
    edge = values[..., :halo].shape
    dense = edge[:-2] + (edge[-2] * halo // 128, 128) if edge[-2] * halo % 128 == 0 else edge
    before = lax.ppermute(values[..., length - halo:].reshape(dense), "raan", up).reshape(edge)
    after = lax.ppermute(values[..., :halo].reshape(dense), "raan", down).reshape(edge)
    return jnp.concatenate([before, values, after], axis=-1)


def alt_extend(values, halo):
    count, depth = lax.axis_size("alt"), values.shape[0]
    below, above = [], []
    for distance in range(1, -(-halo // depth) + 1):
        low = max(0, distance * depth - halo)
        high = min(depth, halo - (distance - 1) * depth)
        up = [(i, i + distance) for i in range(count) if i + distance < count]
        down = [(i, i - distance) for i in range(count) if i - distance >= 0]
        below.insert(0, lax.ppermute(values[low:], "alt", up))
        above.append(lax.ppermute(values[:high], "alt", down))
    return jnp.concatenate(below + [values] + above, axis=0)


def alt_row(values, offset):
    count, depth = lax.axis_size("alt"), values.shape[0]
    distance = -(-offset // depth)
    up = [(i, i + distance) for i in range(count) if i + distance < count]
    down = [(i, i - distance) for i in range(count) if i - distance >= 0]
    index = distance * depth - offset
    below = lax.ppermute(values[index:index + 1], "alt", up)
    above = lax.ppermute(values[depth - 1 - index:depth - index], "alt", down)
    return below, above


def spread_gather(values):
    count = lax.axis_size("alt")
    copies = jnp.broadcast_to(values[None], (count,) + values.shape)
    every = lax.all_to_all(copies, "alt", 0, 0)
    return every.reshape((count * values.shape[0],) + values.shape[1:])


def trim(values, have, want):
    cut = have - want
    return values[cut:values.shape[0] - cut] if cut else values


def lane_shifts(values):
    zero = jnp.zeros_like(values[..., :1])
    left = jnp.concatenate([zero, values[..., :-1]], axis=-1)
    right = jnp.concatenate([values[..., 1:], zero], axis=-1)
    return left, right


def make_weights(coef_alt, coef_inc, coef_raan, factor, halo):
    centre = coef_alt[1:-1]
    w_alt_lo = factor * 0.5 * (centre + coef_alt[:-2])
    w_alt_hi = factor * 0.5 * (centre + coef_alt[2:])
    inner_faces = factor * 0.5 * (coef_inc[:, :-1] + coef_inc[:, 1:])
    zero_inc = jnp.zeros_like(coef_inc[:, :1])
    w_inc_lo = jnp.concatenate([zero_inc, inner_faces], 1)
    w_inc_hi = jnp.concatenate([inner_faces, zero_inc], 1)
    raan_left, raan_right = lane_shifts(coef_raan)
    w_raan_lo = factor * 0.5 * (coef_raan + raan_left)
    w_raan_hi = factor * 0.5 * (coef_raan + raan_right)
    diagonal = 1.0 + (w_alt_lo + w_alt_hi + w_inc_lo + w_inc_hi + w_raan_lo + w_raan_hi)
    return (w_alt_lo, w_alt_hi, w_inc_lo, w_inc_hi, w_raan_lo, w_raan_hi, diagonal), halo


def apply_op(weights, field, halo):
    parts, have = weights
    w_alt_lo, w_alt_hi, w_inc_lo, w_inc_hi, w_raan_lo, w_raan_hi, diagonal = (
        trim(part, have, halo - 1) for part in parts
    )
    centre = field[1:-1]
    v_down, v_up = field[:-2], field[2:]
    zero_inc = jnp.zeros_like(centre[:, :1])
    v_prev = jnp.concatenate([zero_inc, centre[:, :-1]], 1)
    v_next = jnp.concatenate([centre[:, 1:], zero_inc], 1)
    v_left, v_right = lane_shifts(centre)
    beside = (
        w_alt_lo * v_down
        + w_alt_hi * v_up
        + w_inc_lo * v_prev
        + w_inc_hi * v_next
        + w_raan_lo * v_left
        + w_raan_hi * v_right
    )
    return diagonal * centre - beside, centre


def inside(shape, halo):
    depth = shape[0] - 2 * halo
    rows = lax.broadcasted_iota(jnp.int32, shape, 0) + lax.axis_index("alt") * depth - halo
    return (rows >= 0) & (rows < depth * lax.axis_size("alt"))


def sweep(weights, field, halo, target, target_halo, masked=True):
    applied, centre = apply_op(weights, field, halo)
    diagonal = trim(weights[0][6], weights[1], halo - 1)
    updated = centre + OMEGA * (trim(target, target_halo, halo - 1) - applied) / diagonal
    if not masked:
        return updated
    return jnp.where(inside(updated.shape, halo - 1), updated, 0.0)


def pad_rows(values):
    zero = jnp.zeros_like(values[:1])
    return jnp.concatenate([zero, values, zero], axis=0)


def split_sweep(weights, field, target, target_halo):
    parts, have = weights
    depth = field.shape[0] - 2
    cuts = [0, 1, depth - 1, depth] if depth >= 3 else [0, depth]
    rows = []
    for low, high in zip(cuts[:-1], cuts[1:]):
        w_alt_lo, w_alt_hi, w_inc_lo, w_inc_hi, w_raan_lo, w_raan_hi, diagonal = (
            trim(part, have, 0)[low:high] for part in parts
        )
        centre = field[low + 1:high + 1]
        v_down, v_up = field[low:high], field[low + 2:high + 2]
        zero_inc = jnp.zeros_like(centre[:, :1])
        v_prev = jnp.concatenate([zero_inc, centre[:, :-1]], 1)
        v_next = jnp.concatenate([centre[:, 1:], zero_inc], 1)
        v_left, v_right = lane_shifts(centre)
        beside = (
            w_alt_lo * v_down
            + w_alt_hi * v_up
            + w_inc_lo * v_prev
            + w_inc_hi * v_next
            + w_raan_lo * v_left
            + w_raan_hi * v_right
        )
        applied = diagonal * centre - beside
        aim = trim(target, target_halo, 0)[low:high]
        rows.append(centre + OMEGA * (aim - applied) / diagonal)
    return jnp.concatenate(rows, axis=0)


def first_sweep(weights, target, halo):
    diagonal = trim(weights[0][6], weights[1], halo)
    return OMEGA * target / diagonal


def shards(source, k_alt, k_inc, k_raan):
    length = source.shape[-1]
    halo_r = min(RAAN_HALO, length)
    wide = raan_extend(jnp.stack([source, k_alt, k_inc, k_raan], axis=1), halo_r)
    wide_source, wide_alt, wide_inc, wide_raan = (wide[:, i] for i in range(4))
    coef_two = [coarsen(part) for part in (wide_alt, wide_inc, wide_raan)]
    coef_three = [coarsen(part) for part in coef_two]

    first = alt_extend(wide[:, 0:2], 1)
    source_x = first[:, 0]
    weights_one = make_weights(first[:, 1], wide_inc, wide_raan, 1.0, 0)

    density = sweep(weights_one, source_x, 1, source_x, 1, masked=False)
    density = sweep(weights_one, alt_extend(density, 1), 1, source_x, 1, masked=False)
    density_x = alt_extend(density, 1)
    applied, density = apply_op(weights_one, density_x, 1)
    rhs_two = coarsen(wide_source - applied)

    wide_two = SWEEPS + 3
    lanes = rhs_two.shape[-1]
    level_two = alt_extend(jnp.concatenate([rhs_two] + coef_two, axis=-1), wide_two - 1)
    level_two = [level_two[..., i * lanes:(i + 1) * lanes] for i in range(4)]
    far_below, far_above = alt_row(coef_two[0], wide_two)
    weights_two = make_weights(
        jnp.concatenate([far_below, level_two[1], far_above], axis=0),
        level_two[2],
        level_two[3],
        0.25,
        wide_two - 1,
    )
    rhs_two_x = level_two[0]
    correction = first_sweep(weights_two, rhs_two_x, wide_two - 1)
    correction = sweep(weights_two, correction, wide_two - 1, rhs_two_x, wide_two - 1)
    applied, _ = apply_op(weights_two, trim(correction, wide_two - 2, 1), 1)
    rhs_three = coarsen(trim(rhs_two_x, wide_two - 1, 0) - applied)

    height = rhs_three.shape[0]
    column = spread_gather(jnp.stack([rhs_three] + coef_three, 1))
    weights_three = make_weights(pad_rows(column[:, 1]), column[:, 2], column[:, 3], 0.0625, 0)
    rhs_three_x = column[:, 0]
    coarse_part = first_sweep(weights_three, rhs_three_x, 0)
    for _ in range(COARSE_SWEEPS - 1):
        coarse_part = sweep(weights_three, pad_rows(coarse_part), 1, rhs_three_x, 0, masked=False)
    reach = SWEEPS
    coarse_part = jnp.pad(coarse_part, ((reach, reach), (0, 0), (0, 0)))
    coarse_part = lax.dynamic_slice_in_dim(coarse_part, lax.axis_index("alt") * height, height + 2 * reach, 0)

    correction = correction + trim(refine(coarse_part), 2 * reach, wide_two - 2)
    for halo in range(wide_two - 2, 1, -1):
        correction = sweep(weights_two, correction, halo, rhs_two_x, wide_two - 1)

    density = density_x + trim(refine(correction), 2, 1)
    density = sweep(weights_one, density, 1, source_x, 1, masked=False)
    density = sweep(weights_one, alt_extend(density, 1), 1, source_x, 1, masked=False)
    applied, centre = apply_op(weights_one, alt_extend(density, 1), 1)
    scaled_residual = (wide_source - applied) / weights_one[0][6]
    keep = slice(halo_r, halo_r + length)
    return (centre[..., keep], scaled_residual[..., keep])


def solution(mesh):
    spec = P("alt", None, "raan")
    return jax.shard_map(
        shards, mesh=mesh, in_specs=(spec,) * 4, out_specs=(spec, spec), check_vma=False
    )
```

```python
import jax
import jax.numpy as jnp
from jax import lax
from jax.sharding import PartitionSpec as P

SWEEPS = 2
COARSE_SWEEPS = 4
OMEGA = 0.75
RAAN_HALO = 28
HIGH = lax.Precision.HIGHEST


def pairing(fine):
    rows = lax.broadcasted_iota(jnp.int32, (fine, fine // 2), 0) // 2
    cols = lax.broadcasted_iota(jnp.int32, (fine, fine // 2), 1)
    return (rows == cols).astype(jnp.float32)


def coarsen(values):
    depth, width, length = values.shape
    summed = values.reshape(depth // 2, 2, width, length).sum(axis=1)
    summed = jnp.matmul(summed, pairing(length), precision=HIGH)
    summed = jnp.matmul(pairing(width).T[None], summed, precision=HIGH)
    return summed * 0.125


def refine(values):
    depth, width, length = values.shape
    grown = jnp.matmul(values, pairing(2 * length).T, precision=HIGH)
    grown = jnp.matmul(pairing(2 * width)[None], grown, precision=HIGH)
    grown = jnp.broadcast_to(grown[:, None], (depth, 2, 2 * width, 2 * length))
    return grown.reshape(2 * depth, 2 * width, 2 * length)


def raan_extend(values, halo):
    count, length = lax.axis_size("raan"), values.shape[-1]
    up = [(i, (i + 1) % count) for i in range(count)]
    down = [(j, i) for i, j in up]
    edge = values[..., :halo].shape
    dense = edge[:-2] + (edge[-2] * halo // 128, 128) if edge[-2] * halo % 128 == 0 else edge
    before = lax.ppermute(values[..., length - halo:].reshape(dense), "raan", up).reshape(edge)
    after = lax.ppermute(values[..., :halo].reshape(dense), "raan", down).reshape(edge)
    return jnp.concatenate([before, values, after], axis=-1)


def alt_extend(values, halo):
    count, depth = lax.axis_size("alt"), values.shape[0]
    below, above = [], []
    for distance in range(1, -(-halo // depth) + 1):
        low = max(0, distance * depth - halo)
        high = min(depth, halo - (distance - 1) * depth)
        up = [(i, i + distance) for i in range(count) if i + distance < count]
        down = [(i, i - distance) for i in range(count) if i - distance >= 0]
        below.insert(0, lax.ppermute(values[low:], "alt", up))
        above.append(lax.ppermute(values[:high], "alt", down))
    return jnp.concatenate(below + [values] + above, axis=0)


def alt_row(values, offset):
    count, depth = lax.axis_size("alt"), values.shape[0]
    distance = -(-offset // depth)
    up = [(i, i + distance) for i in range(count) if i + distance < count]
    down = [(i, i - distance) for i in range(count) if i - distance >= 0]
    index = distance * depth - offset
    below = lax.ppermute(values[index:index + 1], "alt", up)
    above = lax.ppermute(values[depth - 1 - index:depth - index], "alt", down)
    return below, above


def spread_gather(values):
    count = lax.axis_size("alt")
    copies = jnp.broadcast_to(values[None], (count,) + values.shape)
    every = lax.all_to_all(copies, "alt", 0, 0)
    return every.reshape((count * values.shape[0],) + values.shape[1:])


def trim(values, have, want):
    cut = have - want
    return values[cut:values.shape[0] - cut] if cut else values


def lane_shifts(values):
    zero = jnp.zeros_like(values[..., :1])
    left = jnp.concatenate([zero, values[..., :-1]], axis=-1)
    right = jnp.concatenate([values[..., 1:], zero], axis=-1)
    return left, right


def make_weights(coef_alt, coef_inc, coef_raan, factor, halo):
    centre = coef_alt[1:-1]
    w_alt_lo = factor * 0.5 * (centre + coef_alt[:-2])
    w_alt_hi = factor * 0.5 * (centre + coef_alt[2:])
    inner_faces = factor * 0.5 * (coef_inc[:, :-1] + coef_inc[:, 1:])
    zero_inc = jnp.zeros_like(coef_inc[:, :1])
    w_inc_lo = jnp.concatenate([zero_inc, inner_faces], 1)
    w_inc_hi = jnp.concatenate([inner_faces, zero_inc], 1)
    raan_left, raan_right = lane_shifts(coef_raan)
    w_raan_lo = factor * 0.5 * (coef_raan + raan_left)
    w_raan_hi = factor * 0.5 * (coef_raan + raan_right)
    diagonal = 1.0 + (w_alt_lo + w_alt_hi + w_inc_lo + w_inc_hi + w_raan_lo + w_raan_hi)
    return (w_alt_lo, w_alt_hi, w_inc_lo, w_inc_hi, w_raan_lo, w_raan_hi, diagonal), halo


def apply_op(weights, field, halo):
    parts, have = weights
    w_alt_lo, w_alt_hi, w_inc_lo, w_inc_hi, w_raan_lo, w_raan_hi, diagonal = (
        trim(part, have, halo - 1) for part in parts
    )
    centre = field[1:-1]
    v_down, v_up = field[:-2], field[2:]
    zero_inc = jnp.zeros_like(centre[:, :1])
    v_prev = jnp.concatenate([zero_inc, centre[:, :-1]], 1)
    v_next = jnp.concatenate([centre[:, 1:], zero_inc], 1)
    v_left, v_right = lane_shifts(centre)
    beside = (
        w_alt_lo * v_down
        + w_alt_hi * v_up
        + w_inc_lo * v_prev
        + w_inc_hi * v_next
        + w_raan_lo * v_left
        + w_raan_hi * v_right
    )
    return diagonal * centre - beside, centre


def inside(shape, halo):
    depth = shape[0] - 2 * halo
    rows = lax.broadcasted_iota(jnp.int32, shape, 0) + lax.axis_index("alt") * depth - halo
    return (rows >= 0) & (rows < depth * lax.axis_size("alt"))


def sweep(weights, field, halo, target, target_halo, masked=True):
    applied, centre = apply_op(weights, field, halo)
    diagonal = trim(weights[0][6], weights[1], halo - 1)
    updated = centre + OMEGA * (trim(target, target_halo, halo - 1) - applied) / diagonal
    if not masked:
        return updated
    return jnp.where(inside(updated.shape, halo - 1), updated, 0.0)


def pad_rows(values):
    zero = jnp.zeros_like(values[:1])
    return jnp.concatenate([zero, values, zero], axis=0)


def split_sweep(weights, field, target, target_halo):
    parts, have = weights
    depth = field.shape[0] - 2
    cuts = [0, 1, depth - 1, depth] if depth >= 3 else [0, depth]
    rows = []
    for low, high in zip(cuts[:-1], cuts[1:]):
        w_alt_lo, w_alt_hi, w_inc_lo, w_inc_hi, w_raan_lo, w_raan_hi, diagonal = (
            trim(part, have, 0)[low:high] for part in parts
        )
        centre = field[low + 1:high + 1]
        v_down, v_up = field[low:high], field[low + 2:high + 2]
        zero_inc = jnp.zeros_like(centre[:, :1])
        v_prev = jnp.concatenate([zero_inc, centre[:, :-1]], 1)
        v_next = jnp.concatenate([centre[:, 1:], zero_inc], 1)
        v_left, v_right = lane_shifts(centre)
        beside = (
            w_alt_lo * v_down
            + w_alt_hi * v_up
            + w_inc_lo * v_prev
            + w_inc_hi * v_next
            + w_raan_lo * v_left
            + w_raan_hi * v_right
        )
        applied = diagonal * centre - beside
        aim = trim(target, target_halo, 0)[low:high]
        rows.append(centre + OMEGA * (aim - applied) / diagonal)
    return jnp.concatenate(rows, axis=0)


def first_sweep(weights, target, halo):
    diagonal = trim(weights[0][6], weights[1], halo)
    return OMEGA * target / diagonal


def shards(source, k_alt, k_inc, k_raan):
    length = source.shape[-1]
    halo_r = min(RAAN_HALO, length)
    wide = raan_extend(jnp.stack([source, k_alt, k_inc, k_raan], axis=1), halo_r)
    wide_source, wide_alt, wide_inc, wide_raan = (wide[:, i] for i in range(4))
    coef_two = [coarsen(part) for part in (wide_alt, wide_inc, wide_raan)]
    coef_three = [coarsen(part) for part in coef_two]

    first = alt_extend(wide[:, 0:2], 1)
    source_x = first[:, 0]
    weights_one = make_weights(first[:, 1], wide_inc, wide_raan, 1.0, 0)

    density = split_sweep(weights_one, source_x, source_x, 1)
    density = split_sweep(weights_one, alt_extend(density, 1), source_x, 1)
    density_x = alt_extend(density, 1)
    applied, density = apply_op(weights_one, density_x, 1)
    rhs_two = coarsen(wide_source - applied)

    wide_two = SWEEPS + 3
    lanes = rhs_two.shape[-1]
    level_two = alt_extend(jnp.concatenate([rhs_two] + coef_two, axis=-1), wide_two - 1)
    level_two = [level_two[..., i * lanes:(i + 1) * lanes] for i in range(4)]
    far_below, far_above = alt_row(coef_two[0], wide_two)
    weights_two = make_weights(
        jnp.concatenate([far_below, level_two[1], far_above], axis=0),
        level_two[2],
        level_two[3],
        0.25,
        wide_two - 1,
    )
    rhs_two_x = level_two[0]
    correction = first_sweep(weights_two, rhs_two_x, wide_two - 1)
    correction = sweep(weights_two, correction, wide_two - 1, rhs_two_x, wide_two - 1)
    applied, _ = apply_op(weights_two, trim(correction, wide_two - 2, 1), 1)
    rhs_three = coarsen(trim(rhs_two_x, wide_two - 1, 0) - applied)

    height = rhs_three.shape[0]
    column = spread_gather(jnp.stack([rhs_three] + coef_three, 1))
    weights_three = make_weights(pad_rows(column[:, 1]), column[:, 2], column[:, 3], 0.0625, 0)
    rhs_three_x = column[:, 0]
    coarse_part = first_sweep(weights_three, rhs_three_x, 0)
    for _ in range(COARSE_SWEEPS - 1):
        coarse_part = sweep(weights_three, pad_rows(coarse_part), 1, rhs_three_x, 0, masked=False)
    reach = SWEEPS
    coarse_part = jnp.pad(coarse_part, ((reach, reach), (0, 0), (0, 0)))
    coarse_part = lax.dynamic_slice_in_dim(coarse_part, lax.axis_index("alt") * height, height + 2 * reach, 0)

    correction = correction + trim(refine(coarse_part), 2 * reach, wide_two - 2)
    for halo in range(wide_two - 2, 1, -1):
        correction = sweep(weights_two, correction, halo, rhs_two_x, wide_two - 1)

    density = density_x + trim(refine(correction), 2, 1)
    density = split_sweep(weights_one, density, source_x, 1)
    density = split_sweep(weights_one, alt_extend(density, 1), source_x, 1)
    applied, centre = apply_op(weights_one, alt_extend(density, 1), 1)
    scaled_residual = (wide_source - applied) / weights_one[0][6]
    keep = slice(halo_r, halo_r + length)
    return (centre[..., keep], scaled_residual[..., keep])


def solution(mesh):
    spec = P("alt", None, "raan")
    return jax.shard_map(
        shards, mesh=mesh, in_specs=(spec,) * 4, out_specs=(spec, spec), check_vma=False
    )
```
